32 devices in a mesh: rows: 4 (over y, x), cols: 8 (over z, core).
Axes of the slice: x: 2, y: 2, z: 4, core: 2. Of those that a mesh axis runs over, the one named last changes fastest.
Arguments:
- frames: bfloat16 [2, 16, 8192], P(None, 'rows', 'cols'), may hold values from -6 to 6
- hidden_start: bfloat16 [16, 256, 128], P('rows', 'cols'), may hold values from -3 to 3
- cell_start: float32 [16, 256, 128], P('rows', 'cols'), may hold values from -6 to 6
- kernel: bfloat16 [1440, 512], replicated, may hold values from -0.15625 to 0.15625
- gate_bias: float32 [512], replicated, may hold values from -4 to 4
- cotangent: bfloat16 [2, 16, 256, 128], P(None, 'rows', 'cols'), may hold values from -6 to 6
Outputs:
- hidden_final: bfloat16 [16, 256, 128], P('rows', 'cols')
- grad_hidden_start: float32 [16, 256, 128], P('rows', 'cols')
- grad_cell_start: float32 [16, 256, 128], P('rows', 'cols')
- kernel_grad: float32 [1440, 512], replicated
- bias_grad: float32 [512], replicated
The draws below stay inside these ranges and needn't reach their ends.
All inputs are finite; a program needn't handle non-finite values.
Results may differ from the reference program's by a relative error of at most 0.015.
Values may be sent and summed in bfloat16 or wider, within the bound.
No kernel may reach another device: no remote copies, remote signals or barrier semaphores. Data moves between devices by JAX's collectives and lax.ppermute only.
A program may use at most 64 MiB of HBM per device.

```python
import jax
import jax.numpy as jnp
from jax import lax

HC = 128
CI = 32
KS = 3
STEPS = 2
NH = 16
NW = 256
GATES = 512
KIN = 1440


def shard_levels(key, shape, shards, low, high):
    gain = 1.0
    for position, shards_of in shards:
        draws = jax.random.uniform(jax.random.fold_in(jax.random.fold_in(key, 6), position), (shards_of,), jnp.float32, low / len(shards), high / len(shards))
        gain = gain * jnp.repeat(jnp.exp(draws), shape[position] // shards_of).reshape((-1,) + (1,) * (len(shape) - 1 - position))
    return gain


def gaussian(stream_key, shape, spread, limit, pieces=(), held_as=jnp.bfloat16):
    values = jax.random.normal(stream_key, shape, jnp.float32) * spread
    if len(pieces) > 0:
        values = shard_levels(stream_key, shape, pieces, -0.22, 0.18) * values
    return jnp.clip(values, min=-limit, max=limit).astype(held_as)


def setup_inputs(seed: int = 0) -> dict:
    splits = jax.random.split(jax.random.key(seed), 7)
    return {
        "frames": gaussian(splits[0], (STEPS, NH, NW * CI), 1.0, 6.0, ((1, 4), (2, 8))),
        "hidden_start": gaussian(splits[1], (NH, NW, HC), 0.5, 3.0, ((0, 4), (1, 8))),
        "cell_start": gaussian(splits[2], (NH, NW, HC), 1.0, 6.0, ((0, 4), (1, 8)), jnp.float32),
        "kernel": gaussian(splits[3], (KIN, GATES), KIN ** -0.5, 0.15625),
        "gate_bias": gaussian(splits[4], (GATES,), 1.0, 4.0, (), jnp.float32),
        "cotangent": gaussian(splits[5], (STEPS, NH, NW, HC), 1.0, 6.0, ((1, 4), (2, 8))),
    }


def convolve(field, weights):
    numbers = ('NHWC', 'HWIO', 'NHWC')
    result = lax.conv_general_dilated(field[None], weights, (1, 1), 'SAME', dimension_numbers=numbers, preferred_element_type=jnp.float32)
    return result[0]

def reference(frames, hidden_start, cell_start, kernel, gate_bias, cotangent):
    chans = CI + HC
    weights = kernel.reshape(KS, KS, chans, GATES)
    flipped = jnp.transpose(weights[::-1, ::-1], (0, 1, 3, 2))
    hidden = hidden_start
    cell = cell_start
    saved = []
    for moment in range(STEPS):
        inputs = frames[moment].reshape(NH, NW, CI)
        stacked = jnp.concatenate([inputs, hidden], axis=-1)
        gates = convolve(stacked, weights) + gate_bias
        gate_in = jax.nn.sigmoid(gates[..., :HC])
        gate_forget = jax.nn.sigmoid(gates[..., HC:2 * HC])
        gate_cand = jnp.tanh(gates[..., 2 * HC:3 * HC])
        gate_out = jax.nn.sigmoid(gates[..., 3 * HC:])
        cell_prev = cell
        cell = gate_forget * cell_prev + gate_in * gate_cand
        hidden = (gate_out * jnp.tanh(cell)).astype(jnp.bfloat16)
        saved.append((stacked, gate_in, gate_forget, gate_cand, gate_out, cell_prev, cell))
    hidden_final = hidden
    grad_hidden = cotangent[STEPS - 1].astype(jnp.float32)
    grad_cell = jnp.zeros((NH, NW, HC), jnp.float32)
    kernel_total = jnp.zeros((KS * KS, chans, GATES), jnp.float32)
    bias_total = jnp.zeros((GATES,), jnp.float32)
    for moment in range(STEPS - 1, -1, -1):
        stacked, gate_in, gate_forget, gate_cand, gate_out, cell_prev, cell_now = saved[moment]
        tanh_cell = jnp.tanh(cell_now)
        summed = grad_cell + grad_hidden * gate_out * (1.0 - tanh_cell * tanh_cell)
        pre_in = summed * gate_cand * gate_in * (1.0 - gate_in)
        pre_forget = summed * cell_prev * gate_forget * (1.0 - gate_forget)
        pre_cand = summed * gate_in * (1.0 - gate_cand * gate_cand)
        pre_out = grad_hidden * tanh_cell * gate_out * (1.0 - gate_out)
        grad_cell = summed * gate_forget
        grad_gates = jnp.concatenate([pre_in, pre_forget, pre_cand, pre_out], axis=-1).astype(jnp.bfloat16)
        padded = jnp.pad(stacked, ((1, 1), (1, 1), (0, 0)))
        flat_grads = grad_gates.reshape(NH * NW, GATES)
        parts = []
        for tap_row in range(KS):
            for tap_col in range(KS):
                window = padded[tap_row:tap_row + NH, tap_col:tap_col + NW].reshape(NH * NW, chans)
                parts.append(jnp.dot(window.T, flat_grads, preferred_element_type=jnp.float32))
        kernel_total = kernel_total + jnp.stack(parts)
        bias_total = bias_total + lax.optimization_barrier(jnp.sum(grad_gates.astype(jnp.float32), axis=(0, 1)))
        grad_stacked = convolve(grad_gates, flipped)
        grad_hidden = grad_stacked[..., CI:]
        if moment > 0:
            grad_hidden = grad_hidden + cotangent[moment - 1].astype(jnp.float32)
    norm_scale = 1.0 / jnp.sqrt(jnp.float32(STEPS * NH * NW))
    kernel_grad = kernel_total.reshape(KIN, GATES) * norm_scale
    bias_grad = bias_total * norm_scale
    return (hidden_final, grad_hidden, grad_cell, kernel_grad, bias_grad)
```

```python
import math

import jax
import jax.numpy as jnp
from jax import lax
from jax.sharding import PartitionSpec as P

HC = 128
CI = 32
KS = 3
STEPS = 2
GATES = 512
KIN = 1440
SUM_ROWS = 1536
SUM_WAYS = 3


def extended(cells, sides, width):
    for axis, dim in sides:
        count = lax.axis_size(axis)
        ends = count - 1
        head = lax.slice_in_dim(cells, 0, width, axis=dim)
        tail = lax.slice_in_dim(cells, cells.shape[dim] - width, cells.shape[dim], axis=dim)
        cells = jnp.concatenate(
            [
                lax.ppermute(tail, axis, [(i, (i + 1) % count) for i in range(ends)]),
                cells,
                lax.ppermute(head, axis, [((i + 1) % count, i) for i in range(ends)]),
            ],
            axis=dim,
        )
    return cells


def flip_pairs(axis, bit):
    count = lax.axis_size(axis)
    return [(i, i ^ (1 << bit)) for i in range(count)]


def summing_levels():
    levels = []
    for axis in ("cols", "rows"):
        count = lax.axis_size(axis)
        depth = count.bit_length() - 1
        assert (1 << depth) == count
        levels.extend((axis, bit) for bit in range(depth))
    cols_levels = [lv for lv in levels if lv[0] == "cols"]
    rows_levels = [lv for lv in levels if lv[0] == "rows"]
    return cols_levels[:1], cols_levels[1:2] + rows_levels + cols_levels[2:]


def halve(part, levels):
    halved = []
    for axis, bit in levels:
        rows = part.shape[0]
        if rows % 16 != 0:
            break
        half = rows // 2
        upper = (lax.axis_index(axis) >> bit) & 1
        keep = lax.dynamic_slice_in_dim(part, upper * half, half, 0)
        send = lax.dynamic_slice_in_dim(part, (1 - upper) * half, half, 0)
        part = keep + lax.ppermute(send, axis, flip_pairs(axis, bit))
        halved.append((axis, bit))
    for axis, bit in levels[len(halved):]:
        part = part + lax.ppermute(part, axis, flip_pairs(axis, bit))
    return part, halved


def double(piece, halved):
    for axis, bit in reversed(halved):
        upper = (lax.axis_index(axis) >> bit) & 1
        got = lax.ppermute(piece, axis, flip_pairs(axis, bit))
        low = jnp.where(upper == 0, piece, got)
        high = jnp.where(upper == 0, got, piece)
        piece = jnp.concatenate([low, high], axis=0)
    return piece


def sum_everywhere(total):
    first, rest = summing_levels()
    part, first_halved = halve(total, first)
    ways = min(SUM_WAYS, max(len(rest), 1))
    width = part.shape[0] // ways
    pieces = []
    for way in range(ways):
        order = rest[way:] + rest[:way]
        chunk, halved = halve(part[way * width : (way + 1) * width], order)
        pieces.append(double(chunk.astype(jnp.bfloat16), halved))
    return double(jnp.concatenate(pieces, axis=0), first_halved).astype(jnp.float32)

def tap_columns(padded, rows_dev, cols_dev, reverse):
    pieces = []
    for tap_row in range(KS):
        for tap_col in range(KS):
            if reverse:
                first_row = KS - 1 - tap_row
                first_col = KS - 1 - tap_col
            else:
                first_row = tap_row
                first_col = tap_col
            pieces.append(
                padded[first_row : first_row + rows_dev, first_col : first_col + cols_dev]
            )
    joined = jnp.concatenate(pieces, axis=-1)
    return joined.reshape(rows_dev * cols_dev, joined.shape[-1])


def shards(frames, hidden_start, cell_start, kernel, gate_bias, cotangent):
    rows_dev = hidden_start.shape[0]
    cols_dev = hidden_start.shape[1]
    chans = CI + HC
    taps = KS * KS
    cells = rows_dev * cols_dev
    hidden = hidden_start
    cell = cell_start
    saved = []
    for moment in range(STEPS):
        inputs = frames[moment].reshape(rows_dev, cols_dev, CI)
        stacked = jnp.concatenate([inputs, hidden], axis=-1)
        padded = extended(stacked, (("rows", 0), ("cols", 1)), 1)
        patches = tap_columns(padded, rows_dev, cols_dev, False)
        gates = jnp.dot(patches, kernel, preferred_element_type=jnp.float32) + gate_bias
        gates = gates.reshape(rows_dev, cols_dev, GATES)
        gate_in = jax.nn.sigmoid(gates[..., :HC])
        gate_forget = jax.nn.sigmoid(gates[..., HC : 2 * HC])
        gate_cand = jnp.tanh(gates[..., 2 * HC : 3 * HC])
        gate_out = jax.nn.sigmoid(gates[..., 3 * HC :])
        cell_prev = cell
        cell = gate_forget * cell_prev + gate_in * gate_cand
        hidden = (gate_out * jnp.tanh(cell)).astype(jnp.bfloat16)
        saved.append((patches, gate_in, gate_forget, gate_cand, gate_out, cell_prev, cell))
    blocks = kernel.reshape(taps, chans, GATES)
    adjoint_matrix = jnp.transpose(blocks, (0, 2, 1)).reshape(taps * GATES, chans)
    grad_hidden = cotangent[STEPS - 1].astype(jnp.float32)
    grad_cell = jnp.zeros((rows_dev, cols_dev, HC), jnp.float32)
    spare = SUM_ROWS - KIN - 1
    lifted = []
    grads_seen = []
    for moment in range(STEPS - 1, -1, -1):
        patches, gate_in, gate_forget, gate_cand, gate_out, cell_prev, cell_now = saved[moment]
        tanh_cell = jnp.tanh(cell_now)
        summed = grad_cell + grad_hidden * gate_out * (1.0 - tanh_cell * tanh_cell)
        pre_in = summed * gate_cand * gate_in * (1.0 - gate_in)
        pre_forget = summed * cell_prev * gate_forget * (1.0 - gate_forget)
        pre_cand = summed * gate_in * (1.0 - gate_cand * gate_cand)
        pre_out = grad_hidden * tanh_cell * gate_out * (1.0 - gate_out)
        grad_cell = summed * gate_forget
        grad_gates = jnp.concatenate([pre_in, pre_forget, pre_cand, pre_out], axis=-1).astype(
            jnp.bfloat16
        )
        flat_grads = grad_gates.reshape(cells, GATES)
        lifted.append(
            jnp.concatenate(
                [
                    patches,
                    jnp.ones((cells, 1), patches.dtype),
                    jnp.zeros((cells, spare), patches.dtype),
                ],
                axis=1,
            )
        )
        grads_seen.append(flat_grads)
        grad_padded = extended(grad_gates, (("rows", 0), ("cols", 1)), 1)
        reversed_cols = tap_columns(grad_padded, rows_dev, cols_dev, True)
        grad_stacked = jnp.dot(reversed_cols, adjoint_matrix, preferred_element_type=jnp.float32)
        grad_stacked = grad_stacked.reshape(rows_dev, cols_dev, chans)
        grad_hidden = grad_stacked[..., CI:]
        if moment > 0:
            grad_hidden = grad_hidden + cotangent[moment - 1].astype(jnp.float32)
    total_cells = STEPS * rows_dev * lax.axis_size("rows") * cols_dev * lax.axis_size("cols")
    norm_scale = 1.0 / math.sqrt(total_cells)
    joined = jnp.dot(
        jnp.concatenate(lifted, axis=0).T,
        jnp.concatenate(grads_seen, axis=0),
        preferred_element_type=jnp.float32,
    )
    summed_all = sum_everywhere(joined * norm_scale)
    return (hidden, grad_hidden, grad_cell, summed_all[:KIN], summed_all[KIN])


def solution(mesh):
    placed = (
        P(None, "rows", "cols"),
        P("rows", "cols", None),
        P("rows", "cols", None),
        P(),
        P(),
        P(None, "rows", "cols", None),
    )
    return jax.shard_map(
        shards,
        mesh=mesh,
        in_specs=placed,
        out_specs=(
            P("rows", "cols", None),
            P("rows", "cols", None),
            P("rows", "cols", None),
            P(),
            P(),
        ),
        check_vma=False,
    )
```

```python
import math

import jax
import jax.numpy as jnp
from jax import lax
from jax.sharding import PartitionSpec as P

HC = 128
CI = 32
KS = 3
STEPS = 2
GATES = 512
KIN = 1440
SUM_ROWS = 1536
SUM_WAYS = 3


def flip_pairs(axis, bit):
    count = lax.axis_size(axis)
    return [(i, i ^ (1 << bit)) for i in range(count)]


def summing_levels():
    levels = []
    for axis in ("cols", "rows"):
        count = lax.axis_size(axis)
        depth = count.bit_length() - 1
        assert (1 << depth) == count
        levels.extend((axis, bit) for bit in range(depth))
    cols_levels = [lv for lv in levels if lv[0] == "cols"]
    rows_levels = [lv for lv in levels if lv[0] == "rows"]
    return cols_levels[:1], cols_levels[1:2] + rows_levels + cols_levels[2:]


def halve(part, levels):
    halved = []
    for axis, bit in levels:
        rows = part.shape[0]
        if rows % 16 != 0:
            break
        half = rows // 2
        upper = (lax.axis_index(axis) >> bit) & 1
        keep = lax.dynamic_slice_in_dim(part, upper * half, half, 0)
        send = lax.dynamic_slice_in_dim(part, (1 - upper) * half, half, 0)
        part = keep + lax.ppermute(send, axis, flip_pairs(axis, bit))
        halved.append((axis, bit))
    for axis, bit in levels[len(halved):]:
        part = part + lax.ppermute(part, axis, flip_pairs(axis, bit))
    return part, halved


def double(piece, halved):
    for axis, bit in reversed(halved):
        upper = (lax.axis_index(axis) >> bit) & 1
        got = lax.ppermute(piece, axis, flip_pairs(axis, bit))
        low = jnp.where(upper == 0, piece, got)
        high = jnp.where(upper == 0, got, piece)
        piece = jnp.concatenate([low, high], axis=0)
    return piece


def sum_everywhere(total):
    first, rest = summing_levels()
    part, first_halved = halve(total, first)
    ways = min(SUM_WAYS, max(len(rest), 1))
    width = part.shape[0] // ways
    pieces = []
    for way in range(ways):
        order = rest[way:] + rest[:way]
        chunk, halved = halve(part[way * width : (way + 1) * width], order)
        pieces.append(double(chunk.astype(jnp.bfloat16), halved))
    return double(jnp.concatenate(pieces, axis=0), first_halved).astype(jnp.float32)

def tap_columns(padded, rows_dev, cols_dev, reverse):
    pieces = []
    for tap_row in range(KS):
        for tap_col in range(KS):
            if reverse:
                first_row = KS - 1 - tap_row
                first_col = KS - 1 - tap_col
            else:
                first_row = tap_row
                first_col = tap_col
            pieces.append(
                padded[first_row : first_row + rows_dev, first_col : first_col + cols_dev]
            )
    joined = jnp.concatenate(pieces, axis=-1)
    return joined.reshape(rows_dev * cols_dev, joined.shape[-1])


def widen(cells, axis, dim, width):
    count = lax.axis_size(axis)
    size = cells.shape[dim]
    before, after = [], []
    need, dist = width, 1
    while need > 0:
        take = min(need, size)
        if dist < count:
            tail = lax.slice_in_dim(cells, size - take, size, axis=dim)
            head = lax.slice_in_dim(cells, 0, take, axis=dim)
            before.insert(0, lax.ppermute(tail, axis, [(i, i + dist) for i in range(count - dist)]))
            after.append(lax.ppermute(head, axis, [(i + dist, i) for i in range(count - dist)]))
        else:
            blank = list(cells.shape)
            blank[dim] = take
            before.insert(0, jnp.zeros(blank, cells.dtype))
            after.append(jnp.zeros(blank, cells.dtype))
        need -= take
        dist += 1
    return jnp.concatenate(before + [cells] + after, axis=dim)


def surround(cells, width):
    return widen(widen(cells, "rows", 0, width), "cols", 1, width)


def inner(cells, outer, inner_width):
    cut = outer - inner_width
    return cells[cut : cells.shape[0] - cut, cut : cells.shape[1] - cut]


def inside(rows_dev, cols_dev, width):
    rows_all = rows_dev * lax.axis_size("rows")
    cols_all = cols_dev * lax.axis_size("cols")
    row_at = lax.axis_index("rows") * rows_dev - width + jnp.arange(rows_dev + 2 * width)
    col_at = lax.axis_index("cols") * cols_dev - width + jnp.arange(cols_dev + 2 * width)
    row_ok = (row_at >= 0) & (row_at < rows_all)
    col_ok = (col_at >= 0) & (col_at < cols_all)
    return (row_ok[:, None] & col_ok[None, :])[..., None]


def cell_step(patches, kernel, gate_bias, cell_prev, shape):
    gates = jnp.dot(patches, kernel, preferred_element_type=jnp.float32) + gate_bias
    gates = gates.reshape(shape + (GATES,))
    gate_in = jax.nn.sigmoid(gates[..., :HC])
    gate_forget = jax.nn.sigmoid(gates[..., HC : 2 * HC])
    gate_cand = jnp.tanh(gates[..., 2 * HC : 3 * HC])
    gate_out = jax.nn.sigmoid(gates[..., 3 * HC :])
    cell = gate_forget * cell_prev + gate_in * gate_cand
    hidden = (gate_out * jnp.tanh(cell)).astype(jnp.bfloat16)
    return (gate_in, gate_forget, gate_cand, gate_out), cell, hidden


def cell_grads(grad_cell, grad_hidden, gates, cell_prev, cell_now):
    gate_in, gate_forget, gate_cand, gate_out = gates
    tanh_cell = jnp.tanh(cell_now)
    summed = grad_hidden * gate_out * (1.0 - tanh_cell * tanh_cell)
    if grad_cell is not None:
        summed = grad_cell + summed
    pre_in = summed * gate_cand * gate_in * (1.0 - gate_in)
    pre_forget = summed * cell_prev * gate_forget * (1.0 - gate_forget)
    pre_cand = summed * gate_in * (1.0 - gate_cand * gate_cand)
    pre_out = grad_hidden * tanh_cell * gate_out * (1.0 - gate_out)
    grad_gates = jnp.concatenate([pre_in, pre_forget, pre_cand, pre_out], axis=-1).astype(
        jnp.bfloat16
    )
    return grad_gates, summed * gate_forget


def shards(frames, hidden_start, cell_start, kernel, gate_bias, cotangent):
    rows_dev = hidden_start.shape[0]
    cols_dev = hidden_start.shape[1]
    chans = CI + HC
    taps = KS * KS
    cells = rows_dev * cols_dev
    reach = 2 * STEPS
    pack = jnp.concatenate(
        [
            frames[0].reshape(rows_dev, cols_dev, CI),
            frames[1].reshape(rows_dev, cols_dev, CI),
            hidden_start,
            cotangent[0],
            cotangent[1],
        ],
        axis=-1,
    )
    pack = surround(pack, reach)
    cell_zero = surround(cell_start, reach - 1)
    inputs_one = pack[..., :CI]
    inputs_two = pack[..., CI : 2 * CI]
    hidden_zero = pack[..., 2 * CI : 2 * CI + HC]
    cot_zero = pack[..., 2 * CI + HC : 2 * CI + 2 * HC]
    cot_one = pack[..., 2 * CI + 2 * HC :]

    def dims(width):
        return (rows_dev + 2 * width, cols_dev + 2 * width)

    stacked_one = jnp.concatenate([inputs_one, hidden_zero], axis=-1)
    patches_one = tap_columns(stacked_one, *dims(reach - 1), False)
    gates_one, cell_one, hidden_one = cell_step(
        patches_one, kernel, gate_bias, cell_zero, dims(reach - 1)
    )
    hidden_one = jnp.where(inside(rows_dev, cols_dev, reach - 1), hidden_one, 0)

    stacked_two = jnp.concatenate([inner(inputs_two, reach, reach - 1), hidden_one], axis=-1)
    patches_two = tap_columns(stacked_two, *dims(reach - 2), False)
    cell_one_two = inner(cell_one, reach - 1, reach - 2)
    gates_two, cell_two, hidden_two = cell_step(
        patches_two, kernel, gate_bias, cell_one_two, dims(reach - 2)
    )
    hidden_final = inner(hidden_two, reach - 2, 0)

    blocks = kernel.reshape(taps, chans, GATES)
    adjoint_matrix = jnp.transpose(blocks[:, CI:, :], (0, 2, 1)).reshape(taps * GATES, HC)

    grad_gates_two, grad_cell = cell_grads(
        None, inner(cot_one, reach, reach - 2).astype(jnp.float32), gates_two, cell_one_two, cell_two
    )
    masked_two = jnp.where(inside(rows_dev, cols_dev, reach - 2), grad_gates_two, 0)
    reversed_two = tap_columns(masked_two, *dims(reach - 3), True)
    grad_hidden = jnp.dot(reversed_two, adjoint_matrix, preferred_element_type=jnp.float32)
    grad_hidden = grad_hidden.reshape(dims(reach - 3) + (HC,))
    grad_hidden = grad_hidden + inner(cot_zero, reach, reach - 3).astype(jnp.float32)

    def near(values, width):
        return inner(values, width, reach - 3)

    gates_near = tuple(near(g, reach - 1) for g in gates_one)
    grad_gates_one, grad_cell = cell_grads(
        near(grad_cell, reach - 2),
        grad_hidden,
        gates_near,
        near(cell_zero, reach - 1),
        near(cell_one, reach - 1),
    )
    grad_cell_start = inner(grad_cell, reach - 3, 0)
    masked_one = jnp.where(inside(rows_dev, cols_dev, reach - 3), grad_gates_one, 0)
    reversed_one = tap_columns(masked_one, rows_dev, cols_dev, True)
    grad_hidden_start = jnp.dot(reversed_one, adjoint_matrix, preferred_element_type=jnp.float32)
    grad_hidden_start = grad_hidden_start.reshape(rows_dev, cols_dev, HC)

    spare = SUM_ROWS - KIN - 1
    lifted = []
    for stacked, width in ((stacked_two, reach - 1), (stacked_one, reach)):
        patches = tap_columns(inner(stacked, width, 1), rows_dev, cols_dev, False)
        lifted.append(
            jnp.concatenate(
                [
                    patches,
                    jnp.ones((cells, 1), patches.dtype),
                    jnp.zeros((cells, spare), patches.dtype),
                ],
                axis=1,
            )
        )
    grads_seen = [
        inner(grad_gates_two, reach - 2, 0).reshape(cells, GATES),
        inner(grad_gates_one, reach - 3, 0).reshape(cells, GATES),
    ]
    total_cells = STEPS * rows_dev * lax.axis_size("rows") * cols_dev * lax.axis_size("cols")
    norm_scale = 1.0 / math.sqrt(total_cells)
    joined = jnp.dot(
        jnp.concatenate(lifted, axis=0).T,
        jnp.concatenate(grads_seen, axis=0),
        preferred_element_type=jnp.float32,
    )
    summed_all = sum_everywhere(joined * norm_scale)
    return (
        hidden_final,
        grad_hidden_start,
        grad_cell_start,
        summed_all[:KIN],
        summed_all[KIN],
    )


def solution(mesh):
    placed = (
        P(None, "rows", "cols"),
        P("rows", "cols", None),
        P("rows", "cols", None),
        P(),
        P(),
        P(None, "rows", "cols", None),
    )
    return jax.shard_map(
        shards,
        mesh=mesh,
        in_specs=placed,
        out_specs=(
            P("rows", "cols", None),
            P("rows", "cols", None),
            P("rows", "cols", None),
            P(),
            P(),
        ),
        check_vma=False,
    )
```

```python
import math

import jax
import jax.numpy as jnp
from jax import lax
from jax.sharding import PartitionSpec as P

HC = 128
CI = 32
KS = 3
STEPS = 2
GATES = 512
KIN = 1440
SUM_ROWS = 1536
SUM_WAYS = 3


def flip_pairs(axis, bit):
    count = lax.axis_size(axis)
    return [(i, i ^ (1 << bit)) for i in range(count)]


def summing_levels():
    levels = []
    for axis in ("cols", "rows"):
        count = lax.axis_size(axis)
        depth = count.bit_length() - 1
        assert (1 << depth) == count
        levels.extend((axis, bit) for bit in range(depth))
    cols_levels = [lv for lv in levels if lv[0] == "cols"]
    rows_levels = [lv for lv in levels if lv[0] == "rows"]
    return cols_levels[:1], cols_levels[1:2] + rows_levels + cols_levels[2:]


def halve(part, levels):
    halved = []
    for axis, bit in levels:
        rows = part.shape[0]
        if rows % 16 != 0:
            break
        half = rows // 2
        upper = (lax.axis_index(axis) >> bit) & 1
        keep = lax.dynamic_slice_in_dim(part, upper * half, half, 0)
        send = lax.dynamic_slice_in_dim(part, (1 - upper) * half, half, 0)
        part = keep + lax.ppermute(send, axis, flip_pairs(axis, bit))
        halved.append((axis, bit))
    for axis, bit in levels[len(halved):]:
        part = part + lax.ppermute(part, axis, flip_pairs(axis, bit))
    return part, halved


def double(piece, halved):
    for axis, bit in reversed(halved):
        upper = (lax.axis_index(axis) >> bit) & 1
        got = lax.ppermute(piece, axis, flip_pairs(axis, bit))
        low = jnp.where(upper == 0, piece, got)
        high = jnp.where(upper == 0, got, piece)
        piece = jnp.concatenate([low, high], axis=0)
    return piece


def sum_everywhere(total):
    first, rest = summing_levels()
    part, first_halved = halve(total, first)
    ways = min(SUM_WAYS, max(len(rest), 1))
    width = part.shape[0] // ways
    pieces = []
    for way in range(ways):
        order = rest[way:] + rest[:way]
        chunk, halved = halve(part[way * width : (way + 1) * width], order)
        pieces.append(double(chunk.astype(jnp.bfloat16), halved))
    return double(jnp.concatenate(pieces, axis=0), first_halved).astype(jnp.float32)

def tap_columns(padded, rows_dev, cols_dev, reverse):
    pieces = []
    for tap_row in range(KS):
        for tap_col in range(KS):
            if reverse:
                first_row = KS - 1 - tap_row
                first_col = KS - 1 - tap_col
            else:
                first_row = tap_row
                first_col = tap_col
            pieces.append(
                padded[first_row : first_row + rows_dev, first_col : first_col + cols_dev]
            )
    joined = jnp.concatenate(pieces, axis=-1)
    return joined.reshape(rows_dev * cols_dev, joined.shape[-1])


def widen(cells, axis, dim, width):
    count = lax.axis_size(axis)
    size = cells.shape[dim]
    before, after = [], []
    need, dist = width, 1
    while need > 0:
        take = min(need, size)
        if dist < count:
            tail = lax.slice_in_dim(cells, size - take, size, axis=dim)
            head = lax.slice_in_dim(cells, 0, take, axis=dim)
            before.insert(0, lax.ppermute(tail, axis, [(i, i + dist) for i in range(count - dist)]))
            after.append(lax.ppermute(head, axis, [(i + dist, i) for i in range(count - dist)]))
        else:
            blank = list(cells.shape)
            blank[dim] = take
            before.insert(0, jnp.zeros(blank, cells.dtype))
            after.append(jnp.zeros(blank, cells.dtype))
        need -= take
        dist += 1
    return jnp.concatenate(before + [cells] + after, axis=dim)


def surround(cells, width):
    return widen(widen(cells, "rows", 0, width), "cols", 1, width)


def inner(cells, outer, inner_width):
    cut = outer - inner_width
    return cells[cut : cells.shape[0] - cut, cut : cells.shape[1] - cut]


def inside(rows_dev, cols_dev, width):
    rows_all = rows_dev * lax.axis_size("rows")
    cols_all = cols_dev * lax.axis_size("cols")
    row_at = lax.axis_index("rows") * rows_dev - width + jnp.arange(rows_dev + 2 * width)
    col_at = lax.axis_index("cols") * cols_dev - width + jnp.arange(cols_dev + 2 * width)
    row_ok = (row_at >= 0) & (row_at < rows_all)
    col_ok = (col_at >= 0) & (col_at < cols_all)
    return (row_ok[:, None] & col_ok[None, :])[..., None]


def convolve(field, weights):
    numbers = ("NHWC", "HWIO", "NHWC")
    result = lax.conv_general_dilated(
        field[None], weights, (1, 1), "VALID", dimension_numbers=numbers,
        preferred_element_type=jnp.float32,
    )
    return result[0]


def cell_step(stacked, weights, gate_bias, cell_prev):
    gates = convolve(stacked, weights) + gate_bias
    gate_in = jax.nn.sigmoid(gates[..., :HC])
    gate_forget = jax.nn.sigmoid(gates[..., HC : 2 * HC])
    gate_cand = jnp.tanh(gates[..., 2 * HC : 3 * HC])
    gate_out = jax.nn.sigmoid(gates[..., 3 * HC :])
    cell = gate_forget * cell_prev + gate_in * gate_cand
    hidden = (gate_out * jnp.tanh(cell)).astype(jnp.bfloat16)
    return (gate_in, gate_forget, gate_cand, gate_out), cell, hidden


def cell_grads(grad_cell, grad_hidden, gates, cell_prev, cell_now):
    gate_in, gate_forget, gate_cand, gate_out = gates
    tanh_cell = jnp.tanh(cell_now)
    summed = grad_hidden * gate_out * (1.0 - tanh_cell * tanh_cell)
    if grad_cell is not None:
        summed = grad_cell + summed
    pre_in = summed * gate_cand * gate_in * (1.0 - gate_in)
    pre_forget = summed * cell_prev * gate_forget * (1.0 - gate_forget)
    pre_cand = summed * gate_in * (1.0 - gate_cand * gate_cand)
    pre_out = grad_hidden * tanh_cell * gate_out * (1.0 - gate_out)
    grad_gates = jnp.concatenate([pre_in, pre_forget, pre_cand, pre_out], axis=-1).astype(
        jnp.bfloat16
    )
    return grad_gates, summed * gate_forget


def shards(frames, hidden_start, cell_start, kernel, gate_bias, cotangent):
    rows_dev = hidden_start.shape[0]
    cols_dev = hidden_start.shape[1]
    chans = CI + HC
    cells = rows_dev * cols_dev
    reach = 2 * STEPS
    pack = jnp.concatenate(
        [
            frames[0].reshape(rows_dev, cols_dev, CI),
            frames[1].reshape(rows_dev, cols_dev, CI),
            hidden_start,
            cotangent[0],
            cotangent[1],
        ],
        axis=-1,
    )
    pack = surround(pack, reach)
    cell_zero = surround(cell_start, reach - 1)
    inputs_one = pack[..., :CI]
    inputs_two = pack[..., CI : 2 * CI]
    hidden_zero = pack[..., 2 * CI : 2 * CI + HC]
    cot_zero = pack[..., 2 * CI + HC : 2 * CI + 2 * HC]
    cot_one = pack[..., 2 * CI + 2 * HC :]

    weights = kernel.reshape(KS, KS, chans, GATES)
    flipped = jnp.transpose(weights[::-1, ::-1, CI:, :], (0, 1, 3, 2))
    stacked_one = jnp.concatenate([inputs_one, hidden_zero], axis=-1)
    gates_one, cell_one, hidden_one = cell_step(stacked_one, weights, gate_bias, cell_zero)
    hidden_one = jnp.where(inside(rows_dev, cols_dev, reach - 1), hidden_one, 0)

    stacked_two = jnp.concatenate([inner(inputs_two, reach, reach - 1), hidden_one], axis=-1)
    cell_one_two = inner(cell_one, reach - 1, reach - 2)
    gates_two, cell_two, hidden_two = cell_step(stacked_two, weights, gate_bias, cell_one_two)
    hidden_final = inner(hidden_two, reach - 2, 0)

    grad_gates_two, grad_cell = cell_grads(
        None, inner(cot_one, reach, reach - 2).astype(jnp.float32), gates_two, cell_one_two, cell_two
    )
    masked_two = jnp.where(inside(rows_dev, cols_dev, reach - 2), grad_gates_two, 0)
    grad_hidden = convolve(masked_two, flipped) + inner(cot_zero, reach, reach - 3).astype(jnp.float32)

    def near(values, width):
        return inner(values, width, reach - 3)

    gates_near = tuple(near(g, reach - 1) for g in gates_one)
    grad_gates_one, grad_cell = cell_grads(
        near(grad_cell, reach - 2),
        grad_hidden,
        gates_near,
        near(cell_zero, reach - 1),
        near(cell_one, reach - 1),
    )
    grad_cell_start = inner(grad_cell, reach - 3, 0)
    masked_one = jnp.where(inside(rows_dev, cols_dev, reach - 3), grad_gates_one, 0)
    grad_hidden_start = convolve(masked_one, flipped)

    spare = SUM_ROWS - KIN - 1
    lifted = []
    for stacked, width in ((stacked_two, reach - 1), (stacked_one, reach)):
        patches = tap_columns(inner(stacked, width, 1), rows_dev, cols_dev, False)
        lifted.append(
            jnp.concatenate(
                [
                    patches,
                    jnp.ones((cells, 1), patches.dtype),
                    jnp.zeros((cells, spare), patches.dtype),
                ],
                axis=1,
            )
        )
    grads_seen = [
        inner(grad_gates_two, reach - 2, 0).reshape(cells, GATES),
        inner(grad_gates_one, reach - 3, 0).reshape(cells, GATES),
    ]
    total_cells = STEPS * rows_dev * lax.axis_size("rows") * cols_dev * lax.axis_size("cols")
    norm_scale = 1.0 / math.sqrt(total_cells)
    joined = jnp.dot(
        jnp.concatenate(lifted, axis=0).T,
        jnp.concatenate(grads_seen, axis=0),
        preferred_element_type=jnp.float32,
    )
    summed_all = sum_everywhere(joined * norm_scale)
    return (
        hidden_final,
        grad_hidden_start,
        grad_cell_start,
        summed_all[:KIN],
        summed_all[KIN],
    )


def solution(mesh):
    placed = (
        P(None, "rows", "cols"),
        P("rows", "cols", None),
        P("rows", "cols", None),
        P(),
        P(),
        P(None, "rows", "cols", None),
    )
    return jax.shard_map(
        shards,
        mesh=mesh,
        in_specs=placed,
        out_specs=(
            P("rows", "cols", None),
            P("rows", "cols", None),
            P("rows", "cols", None),
            P(),
            P(),
        ),
        check_vma=False,
    )
```

```python
import math

import jax
import jax.numpy as jnp
from jax import lax
from jax.sharding import PartitionSpec as P

HC = 128
CI = 32
KS = 3
STEPS = 2
GATES = 512
KIN = 1440
SUM_ROWS = 1536


def flip_pairs(axis, bit):
    count = lax.axis_size(axis)
    return [(i, i ^ (1 << bit)) for i in range(count)]


def summing_levels():
    levels = []
    for axis in ("cols", "rows"):
        count = lax.axis_size(axis)
        depth = count.bit_length() - 1
        assert (1 << depth) == count
        levels.extend((axis, bit) for bit in range(depth))
    cols_levels = [lv for lv in levels if lv[0] == "cols"]
    rows_levels = [lv for lv in levels if lv[0] == "rows"]
    return cols_levels[:1], cols_levels[1:2] + rows_levels + cols_levels[2:]


def halve(part, levels):
    halved = []
    for axis, bit in levels:
        rows = part.shape[0]
        if rows % 16 != 0:
            break
        half = rows // 2
        upper = (lax.axis_index(axis) >> bit) & 1
        keep = lax.dynamic_slice_in_dim(part, upper * half, half, 0)
        send = lax.dynamic_slice_in_dim(part, (1 - upper) * half, half, 0)
        part = keep + lax.ppermute(send, axis, flip_pairs(axis, bit))
        halved.append((axis, bit))
    for axis, bit in levels[len(halved):]:
        part = part + lax.ppermute(part, axis, flip_pairs(axis, bit))
    return part, halved


def double(piece, halved):
    for axis, bit in reversed(halved):
        upper = (lax.axis_index(axis) >> bit) & 1
        got = lax.ppermute(piece, axis, flip_pairs(axis, bit))
        low = jnp.where(upper == 0, piece, got)
        high = jnp.where(upper == 0, got, piece)
        piece = jnp.concatenate([low, high], axis=0)
    return piece


def sum_everywhere(total):
    first, rest = summing_levels()
    part, first_halved = halve(total, first)
    if len(rest) >= 2:
        width = part.shape[0] // 2
        orders = (rest[:2], [rest[1], rest[0]])
        chunks, halves = [], []
        for way, order in enumerate(orders):
            chunk, halved = halve(part[way * width : (way + 1) * width], order)
            chunks.append(chunk)
            halves.append(halved)
        merged, merged_halved = halve(jnp.concatenate(chunks, axis=0), rest[2:])
        merged = double(merged.astype(jnp.bfloat16), merged_halved)
        size = merged.shape[0] // 2
        pieces = [
            double(merged[way * size : (way + 1) * size], halves[way]) for way in range(2)
        ]
        piece = jnp.concatenate(pieces, axis=0)
    else:
        chunk, halved = halve(part, rest)
        piece = double(chunk.astype(jnp.bfloat16), halved)
    return double(piece, first_halved).astype(jnp.float32)

def tap_columns(padded, rows_dev, cols_dev, reverse):
    pieces = []
    for tap_row in range(KS):
        for tap_col in range(KS):
            if reverse:
                first_row = KS - 1 - tap_row
                first_col = KS - 1 - tap_col
            else:
                first_row = tap_row
                first_col = tap_col
            pieces.append(
                padded[first_row : first_row + rows_dev, first_col : first_col + cols_dev]
            )
    joined = jnp.concatenate(pieces, axis=-1)
    return joined.reshape(rows_dev * cols_dev, joined.shape[-1])


def widen(cells, axis, dim, width):
    count = lax.axis_size(axis)
    size = cells.shape[dim]
    before, after = [], []
    need, dist = width, 1
    while need > 0:
        take = min(need, size)
        if dist < count:
            tail = lax.slice_in_dim(cells, size - take, size, axis=dim)
            head = lax.slice_in_dim(cells, 0, take, axis=dim)
            before.insert(0, lax.ppermute(tail, axis, [(i, i + dist) for i in range(count - dist)]))
            after.append(lax.ppermute(head, axis, [(i + dist, i) for i in range(count - dist)]))
        else:
            blank = list(cells.shape)
            blank[dim] = take
            before.insert(0, jnp.zeros(blank, cells.dtype))
            after.append(jnp.zeros(blank, cells.dtype))
        need -= take
        dist += 1
    return jnp.concatenate(before + [cells] + after, axis=dim)


def surround(cells, width):
    return widen(widen(cells, "rows", 0, width), "cols", 1, width)


def inner(cells, outer, inner_width):
    cut = outer - inner_width
    return cells[cut : cells.shape[0] - cut, cut : cells.shape[1] - cut]


def inside(rows_dev, cols_dev, width):
    rows_all = rows_dev * lax.axis_size("rows")
    cols_all = cols_dev * lax.axis_size("cols")
    row_at = lax.axis_index("rows") * rows_dev - width + jnp.arange(rows_dev + 2 * width)
    col_at = lax.axis_index("cols") * cols_dev - width + jnp.arange(cols_dev + 2 * width)
    row_ok = (row_at >= 0) & (row_at < rows_all)
    col_ok = (col_at >= 0) & (col_at < cols_all)
    return (row_ok[:, None] & col_ok[None, :])[..., None]


def convolve(field, weights):
    numbers = ("NHWC", "HWIO", "NHWC")
    result = lax.conv_general_dilated(
        field[None], weights, (1, 1), "VALID", dimension_numbers=numbers,
        preferred_element_type=jnp.float32,
    )
    return result[0]


def cell_step(stacked, weights, gate_bias, cell_prev):
    gates = convolve(stacked, weights) + gate_bias
    gate_in = jax.nn.sigmoid(gates[..., :HC])
    gate_forget = jax.nn.sigmoid(gates[..., HC : 2 * HC])
    gate_cand = jnp.tanh(gates[..., 2 * HC : 3 * HC])
    gate_out = jax.nn.sigmoid(gates[..., 3 * HC :])
    cell = gate_forget * cell_prev + gate_in * gate_cand
    hidden = (gate_out * jnp.tanh(cell)).astype(jnp.bfloat16)
    return (gate_in, gate_forget, gate_cand, gate_out), cell, hidden


def cell_grads(grad_cell, grad_hidden, gates, cell_prev, cell_now):
    gate_in, gate_forget, gate_cand, gate_out = gates
    tanh_cell = jnp.tanh(cell_now)
    summed = grad_hidden * gate_out * (1.0 - tanh_cell * tanh_cell)
    if grad_cell is not None:
        summed = grad_cell + summed
    pre_in = summed * gate_cand * gate_in * (1.0 - gate_in)
    pre_forget = summed * cell_prev * gate_forget * (1.0 - gate_forget)
    pre_cand = summed * gate_in * (1.0 - gate_cand * gate_cand)
    pre_out = grad_hidden * tanh_cell * gate_out * (1.0 - gate_out)
    grad_gates = jnp.concatenate([pre_in, pre_forget, pre_cand, pre_out], axis=-1).astype(
        jnp.bfloat16
    )
    return grad_gates, summed * gate_forget


def shards(frames, hidden_start, cell_start, kernel, gate_bias, cotangent):
    rows_dev = hidden_start.shape[0]
    cols_dev = hidden_start.shape[1]
    chans = CI + HC
    cells = rows_dev * cols_dev
    reach = 2 * STEPS
    pack = jnp.concatenate(
        [
            frames[0].reshape(rows_dev, cols_dev, CI),
            frames[1].reshape(rows_dev, cols_dev, CI),
            hidden_start,
            cotangent[0],
            cotangent[1],
        ],
        axis=-1,
    )
    pack = surround(pack, reach)
    cell_zero = surround(cell_start, reach - 1)
    inputs_one = pack[..., :CI]
    inputs_two = pack[..., CI : 2 * CI]
    hidden_zero = pack[..., 2 * CI : 2 * CI + HC]
    cot_zero = pack[..., 2 * CI + HC : 2 * CI + 2 * HC]
    cot_one = pack[..., 2 * CI + 2 * HC :]

    weights = kernel.reshape(KS, KS, chans, GATES)
    flipped = jnp.transpose(weights[::-1, ::-1, CI:, :], (0, 1, 3, 2))
    stacked_one = jnp.concatenate([inputs_one, hidden_zero], axis=-1)
    gates_one, cell_one, hidden_one = cell_step(stacked_one, weights, gate_bias, cell_zero)
    hidden_one = jnp.where(inside(rows_dev, cols_dev, reach - 1), hidden_one, 0)

    stacked_two = jnp.concatenate([inner(inputs_two, reach, reach - 1), hidden_one], axis=-1)
    cell_one_two = inner(cell_one, reach - 1, reach - 2)
    gates_two, cell_two, hidden_two = cell_step(stacked_two, weights, gate_bias, cell_one_two)
    hidden_final = inner(hidden_two, reach - 2, 0)

    grad_gates_two, grad_cell = cell_grads(
        None, inner(cot_one, reach, reach - 2).astype(jnp.float32), gates_two, cell_one_two, cell_two
    )
    masked_two = jnp.where(inside(rows_dev, cols_dev, reach - 2), grad_gates_two, 0)
    grad_hidden = convolve(masked_two, flipped) + inner(cot_zero, reach, reach - 3).astype(jnp.float32)

    def near(values, width):
        return inner(values, width, reach - 3)

    gates_near = tuple(near(g, reach - 1) for g in gates_one)
    grad_gates_one, grad_cell = cell_grads(
        near(grad_cell, reach - 2),
        grad_hidden,
        gates_near,
        near(cell_zero, reach - 1),
        near(cell_one, reach - 1),
    )
    grad_cell_start = inner(grad_cell, reach - 3, 0)
    masked_one = jnp.where(inside(rows_dev, cols_dev, reach - 3), grad_gates_one, 0)
    grad_hidden_start = convolve(masked_one, flipped)

    spare = SUM_ROWS - KIN - 1
    lifted = []
    for stacked, width in ((stacked_two, reach - 1), (stacked_one, reach)):
        patches = tap_columns(inner(stacked, width, 1), rows_dev, cols_dev, False)
        lifted.append(
            jnp.concatenate(
                [
                    patches,
                    jnp.ones((cells, 1), patches.dtype),
                    jnp.zeros((cells, spare), patches.dtype),
                ],
                axis=1,
            )
        )
    grads_seen = [
        inner(grad_gates_two, reach - 2, 0).reshape(cells, GATES),
        inner(grad_gates_one, reach - 3, 0).reshape(cells, GATES),
    ]
    total_cells = STEPS * rows_dev * lax.axis_size("rows") * cols_dev * lax.axis_size("cols")
    norm_scale = 1.0 / math.sqrt(total_cells)
    joined = jnp.dot(
        jnp.concatenate(lifted, axis=0).T,
        jnp.concatenate(grads_seen, axis=0),
        preferred_element_type=jnp.float32,
    )
    summed_all = sum_everywhere(joined * norm_scale)
    return (
        hidden_final,
        grad_hidden_start,
        grad_cell_start,
        summed_all[:KIN],
        summed_all[KIN],
    )


def solution(mesh):
    placed = (
        P(None, "rows", "cols"),
        P("rows", "cols", None),
        P("rows", "cols", None),
        P(),
        P(),
        P(None, "rows", "cols", None),
    )
    return jax.shard_map(
        shards,
        mesh=mesh,
        in_specs=placed,
        out_specs=(
            P("rows", "cols", None),
            P("rows", "cols", None),
            P("rows", "cols", None),
            P(),
            P(),
        ),
        check_vma=False,
    )
```

```python
import math

import jax
import jax.numpy as jnp
from jax import lax
from jax.sharding import PartitionSpec as P

HC = 128
CI = 32
KS = 3
STEPS = 2
GATES = 512
KIN = 1440
SUM_ROWS = 1536
SUM_WAYS = 3


def flip_pairs(axis, bit):
    count = lax.axis_size(axis)
    return [(i, i ^ (1 << bit)) for i in range(count)]


def summing_levels():
    levels = []
    for axis in ("cols", "rows"):
        count = lax.axis_size(axis)
        depth = count.bit_length() - 1
        assert (1 << depth) == count
        levels.extend((axis, bit) for bit in range(depth))
    cols_levels = [lv for lv in levels if lv[0] == "cols"]
    rows_levels = [lv for lv in levels if lv[0] == "rows"]
    return cols_levels[:1], cols_levels[1:2] + rows_levels + cols_levels[2:]


def halve(part, levels):
    halved = []
    for axis, bit in levels:
        rows = part.shape[0]
        if rows % 16 != 0:
            break
        half = rows // 2
        upper = (lax.axis_index(axis) >> bit) & 1
        keep = lax.dynamic_slice_in_dim(part, upper * half, half, 0)
        send = lax.dynamic_slice_in_dim(part, (1 - upper) * half, half, 0)
        part = keep + lax.ppermute(send, axis, flip_pairs(axis, bit))
        halved.append((axis, bit))
    for axis, bit in levels[len(halved):]:
        part = part + lax.ppermute(part, axis, flip_pairs(axis, bit))
    return part, halved


def double(piece, halved):
    for axis, bit in reversed(halved):
        upper = (lax.axis_index(axis) >> bit) & 1
        got = lax.ppermute(piece, axis, flip_pairs(axis, bit))
        low = jnp.where(upper == 0, piece, got)
        high = jnp.where(upper == 0, got, piece)
        piece = jnp.concatenate([low, high], axis=0)
    return piece


def sum_everywhere(total):
    first, rest = summing_levels()
    part, first_halved = halve(total, first)
    ways = min(SUM_WAYS, max(len(rest), 1))
    width = part.shape[0] // ways
    pieces = []
    for way in range(ways):
        order = rest[way:] + rest[:way]
        chunk, halved = halve(part[way * width : (way + 1) * width], order)
        pieces.append(double(chunk.astype(jnp.bfloat16), halved))
    piece = jnp.concatenate(pieces, axis=0)
    if len(first_halved) == 1:
        axis, bit = first_halved[0]
        upper = (lax.axis_index(axis) >> bit) & 1
        got = lax.ppermute(piece, axis, flip_pairs(axis, bit))
        low = jnp.where(upper == 0, piece, got)
        high = jnp.where(upper == 0, got, piece)
        split = KIN - low.shape[0]
        kernel_part = jnp.concatenate([low, high[:split]], axis=0).astype(jnp.float32)
        return kernel_part, high[split].astype(jnp.float32)
    summed = double(piece, first_halved).astype(jnp.float32)
    return summed[:KIN], summed[KIN]

def tap_columns(padded, rows_dev, cols_dev, reverse):
    pieces = []
    for tap_row in range(KS):
        for tap_col in range(KS):
            if reverse:
                first_row = KS - 1 - tap_row
                first_col = KS - 1 - tap_col
            else:
                first_row = tap_row
                first_col = tap_col
            pieces.append(
                padded[first_row : first_row + rows_dev, first_col : first_col + cols_dev]
            )
    joined = jnp.concatenate(pieces, axis=-1)
    return joined.reshape(rows_dev * cols_dev, joined.shape[-1])


def widen(cells, axis, dim, width):
    count = lax.axis_size(axis)
    size = cells.shape[dim]
    before, after = [], []
    need, dist = width, 1
    while need > 0:
        take = min(need, size)
        if dist < count:
            tail = lax.slice_in_dim(cells, size - take, size, axis=dim)
            head = lax.slice_in_dim(cells, 0, take, axis=dim)
            before.insert(0, lax.ppermute(tail, axis, [(i, i + dist) for i in range(count - dist)]))
            after.append(lax.ppermute(head, axis, [(i + dist, i) for i in range(count - dist)]))
        else:
            blank = list(cells.shape)
            blank[dim] = take
            before.insert(0, jnp.zeros(blank, cells.dtype))
            after.append(jnp.zeros(blank, cells.dtype))
        need -= take
        dist += 1
    return jnp.concatenate(before + [cells] + after, axis=dim)


def surround(cells, width):
    return widen(widen(cells, "rows", 0, width), "cols", 1, width)


def inner(cells, outer, inner_width):
    cut = outer - inner_width
    return cells[cut : cells.shape[0] - cut, cut : cells.shape[1] - cut]


def inside(rows_dev, cols_dev, width):
    rows_all = rows_dev * lax.axis_size("rows")
    cols_all = cols_dev * lax.axis_size("cols")
    row_at = lax.axis_index("rows") * rows_dev - width + jnp.arange(rows_dev + 2 * width)
    col_at = lax.axis_index("cols") * cols_dev - width + jnp.arange(cols_dev + 2 * width)
    row_ok = (row_at >= 0) & (row_at < rows_all)
    col_ok = (col_at >= 0) & (col_at < cols_all)
    return (row_ok[:, None] & col_ok[None, :])[..., None]


def convolve(field, weights):
    numbers = ("NHWC", "HWIO", "NHWC")
    result = lax.conv_general_dilated(
        field[None], weights, (1, 1), "VALID", dimension_numbers=numbers,
        preferred_element_type=jnp.float32,
    )
    return result[0]


def cell_step(stacked, weights, gate_bias, cell_prev):
    gates = convolve(stacked, weights) + gate_bias
    gate_in = jax.nn.sigmoid(gates[..., :HC])
    gate_forget = jax.nn.sigmoid(gates[..., HC : 2 * HC])
    gate_cand = jnp.tanh(gates[..., 2 * HC : 3 * HC])
    gate_out = jax.nn.sigmoid(gates[..., 3 * HC :])
    cell = gate_forget * cell_prev + gate_in * gate_cand
    hidden = (gate_out * jnp.tanh(cell)).astype(jnp.bfloat16)
    return (gate_in, gate_forget, gate_cand, gate_out), cell, hidden


def cell_grads(grad_cell, grad_hidden, gates, cell_prev, cell_now):
    gate_in, gate_forget, gate_cand, gate_out = gates
    tanh_cell = jnp.tanh(cell_now)
    summed = grad_hidden * gate_out * (1.0 - tanh_cell * tanh_cell)
    if grad_cell is not None:
        summed = grad_cell + summed
    pre_in = summed * gate_cand * gate_in * (1.0 - gate_in)
    pre_forget = summed * cell_prev * gate_forget * (1.0 - gate_forget)
    pre_cand = summed * gate_in * (1.0 - gate_cand * gate_cand)
    pre_out = grad_hidden * tanh_cell * gate_out * (1.0 - gate_out)
    grad_gates = jnp.concatenate([pre_in, pre_forget, pre_cand, pre_out], axis=-1).astype(
        jnp.bfloat16
    )
    return grad_gates, summed * gate_forget


def shards(frames, hidden_start, cell_start, kernel, gate_bias, cotangent):
    rows_dev = hidden_start.shape[0]
    cols_dev = hidden_start.shape[1]
    chans = CI + HC
    cells = rows_dev * cols_dev
    reach = 2 * STEPS
    pack = jnp.concatenate(
        [
            frames[0].reshape(rows_dev, cols_dev, CI),
            frames[1].reshape(rows_dev, cols_dev, CI),
            hidden_start,
            cotangent[0],
            cotangent[1],
        ],
        axis=-1,
    )
    pack = surround(pack, reach)
    cell_zero = surround(cell_start, reach - 1)
    inputs_one = pack[..., :CI]
    inputs_two = pack[..., CI : 2 * CI]
    hidden_zero = pack[..., 2 * CI : 2 * CI + HC]
    cot_zero = pack[..., 2 * CI + HC : 2 * CI + 2 * HC]
    cot_one = pack[..., 2 * CI + 2 * HC :]

    weights = kernel.reshape(KS, KS, chans, GATES)
    flipped = jnp.transpose(weights[::-1, ::-1, CI:, :], (0, 1, 3, 2))
    stacked_one = jnp.concatenate([inputs_one, hidden_zero], axis=-1)
    gates_one, cell_one, hidden_one = cell_step(stacked_one, weights, gate_bias, cell_zero)
    hidden_one = jnp.where(inside(rows_dev, cols_dev, reach - 1), hidden_one, 0)

    stacked_two = jnp.concatenate([inner(inputs_two, reach, reach - 1), hidden_one], axis=-1)
    cell_one_two = inner(cell_one, reach - 1, reach - 2)
    gates_two, cell_two, hidden_two = cell_step(stacked_two, weights, gate_bias, cell_one_two)
    hidden_final = inner(hidden_two, reach - 2, 0)

    grad_gates_two, grad_cell = cell_grads(
        None, inner(cot_one, reach, reach - 2).astype(jnp.float32), gates_two, cell_one_two, cell_two
    )
    masked_two = jnp.where(inside(rows_dev, cols_dev, reach - 2), grad_gates_two, 0)
    grad_hidden = convolve(masked_two, flipped) + inner(cot_zero, reach, reach - 3).astype(jnp.float32)

    def near(values, width):
        return inner(values, width, reach - 3)

    gates_near = tuple(near(g, reach - 1) for g in gates_one)
    grad_gates_one, grad_cell = cell_grads(
        near(grad_cell, reach - 2),
        grad_hidden,
        gates_near,
        near(cell_zero, reach - 1),
        near(cell_one, reach - 1),
    )
    grad_cell_start = inner(grad_cell, reach - 3, 0)
    masked_one = jnp.where(inside(rows_dev, cols_dev, reach - 3), grad_gates_one, 0)
    grad_hidden_start = convolve(masked_one, flipped)

    spare = SUM_ROWS - KIN - 1
    lifted = []
    for stacked, width in ((stacked_two, reach - 1), (stacked_one, reach)):
        patches = tap_columns(inner(stacked, width, 1), rows_dev, cols_dev, False)
        lifted.append(
            jnp.concatenate(
                [
                    patches,
                    jnp.ones((cells, 1), patches.dtype),
                    jnp.zeros((cells, spare), patches.dtype),
                ],
                axis=1,
            )
        )
    grads_seen = [
        inner(grad_gates_two, reach - 2, 0).reshape(cells, GATES),
        inner(grad_gates_one, reach - 3, 0).reshape(cells, GATES),
    ]
    total_cells = STEPS * rows_dev * lax.axis_size("rows") * cols_dev * lax.axis_size("cols")
    norm_scale = 1.0 / math.sqrt(total_cells)
    joined = jnp.dot(
        jnp.concatenate(lifted, axis=0).T,
        jnp.concatenate(grads_seen, axis=0),
        preferred_element_type=jnp.float32,
    )
    kernel_grad, bias_grad = sum_everywhere(joined * norm_scale)
    return (hidden_final, grad_hidden_start, grad_cell_start, kernel_grad, bias_grad)


def solution(mesh):
    placed = (
        P(None, "rows", "cols"),
        P("rows", "cols", None),
        P("rows", "cols", None),
        P(),
        P(),
        P(None, "rows", "cols", None),
    )
    return jax.shard_map(
        shards,
        mesh=mesh,
        in_specs=placed,
        out_specs=(
            P("rows", "cols", None),
            P("rows", "cols", None),
            P("rows", "cols", None),
            P(),
            P(),
        ),
        check_vma=False,
    )
```

```python
import math

import jax
import jax.numpy as jnp
from jax import lax
from jax.sharding import PartitionSpec as P

HC = 128
CI = 32
KS = 3
STEPS = 2
GATES = 512
KIN = 1440
SUM_ROWS = 1536
SUM_WAYS = 3


def flip_pairs(axis, bit):
    count = lax.axis_size(axis)
    return [(i, i ^ (1 << bit)) for i in range(count)]


def summing_levels():
    levels = []
    for axis in ("cols", "rows"):
        count = lax.axis_size(axis)
        depth = count.bit_length() - 1
        assert (1 << depth) == count
        levels.extend((axis, bit) for bit in range(depth))
    cols_levels = [lv for lv in levels if lv[0] == "cols"]
    rows_levels = [lv for lv in levels if lv[0] == "rows"]
    return cols_levels[:1], cols_levels[1:2] + rows_levels + cols_levels[2:]


def halve(part, levels):
    halved = []
    for axis, bit in levels:
        rows = part.shape[0]
        if rows % 16 != 0:
            break
        half = rows // 2
        upper = (lax.axis_index(axis) >> bit) & 1
        keep = lax.dynamic_slice_in_dim(part, upper * half, half, 0)
        send = lax.dynamic_slice_in_dim(part, (1 - upper) * half, half, 0)
        part = keep + lax.ppermute(send, axis, flip_pairs(axis, bit))
        halved.append((axis, bit))
    for axis, bit in levels[len(halved):]:
        part = part + lax.ppermute(part, axis, flip_pairs(axis, bit))
    return part, halved


def double(piece, halved):
    for axis, bit in reversed(halved):
        upper = (lax.axis_index(axis) >> bit) & 1
        got = lax.ppermute(piece, axis, flip_pairs(axis, bit))
        low = jnp.where(upper == 0, piece, got)
        high = jnp.where(upper == 0, got, piece)
        piece = jnp.concatenate([low, high], axis=0)
    return piece


def sum_everywhere(part, first_halved, rest):
    ways = min(SUM_WAYS, max(len(rest), 1))
    width = part.shape[0] // ways
    pieces = []
    for way in range(ways):
        order = rest[way:] + rest[:way]
        chunk, halved = halve(part[way * width : (way + 1) * width], order)
        pieces.append(double(chunk.astype(jnp.bfloat16), halved))
    piece = jnp.concatenate(pieces, axis=0)
    if len(first_halved) == 1:
        axis, bit = first_halved[0]
        upper = (lax.axis_index(axis) >> bit) & 1
        got = lax.ppermute(piece, axis, flip_pairs(axis, bit))
        low = jnp.where(upper == 0, piece, got)
        high = jnp.where(upper == 0, got, piece)
        split = KIN - low.shape[0]
        kernel_part = jnp.concatenate([low, high[:split]], axis=0).astype(jnp.float32)
        return kernel_part, high[split].astype(jnp.float32)
    summed = double(piece, first_halved).astype(jnp.float32)
    return summed[:KIN], summed[KIN]

def tap_columns(padded, rows_dev, cols_dev, reverse):
    pieces = []
    for tap_row in range(KS):
        for tap_col in range(KS):
            if reverse:
                first_row = KS - 1 - tap_row
                first_col = KS - 1 - tap_col
            else:
                first_row = tap_row
                first_col = tap_col
            pieces.append(
                padded[first_row : first_row + rows_dev, first_col : first_col + cols_dev]
            )
    joined = jnp.concatenate(pieces, axis=-1)
    return joined.reshape(rows_dev * cols_dev, joined.shape[-1])


def widen(cells, axis, dim, width):
    count = lax.axis_size(axis)
    size = cells.shape[dim]
    before, after = [], []
    need, dist = width, 1
    while need > 0:
        take = min(need, size)
        if dist < count:
            tail = lax.slice_in_dim(cells, size - take, size, axis=dim)
            head = lax.slice_in_dim(cells, 0, take, axis=dim)
            before.insert(0, lax.ppermute(tail, axis, [(i, i + dist) for i in range(count - dist)]))
            after.append(lax.ppermute(head, axis, [(i + dist, i) for i in range(count - dist)]))
        else:
            blank = list(cells.shape)
            blank[dim] = take
            before.insert(0, jnp.zeros(blank, cells.dtype))
            after.append(jnp.zeros(blank, cells.dtype))
        need -= take
        dist += 1
    return jnp.concatenate(before + [cells] + after, axis=dim)


def surround(cells, width):
    return widen(widen(cells, "rows", 0, width), "cols", 1, width)


def inner(cells, outer, inner_width):
    cut = outer - inner_width
    return cells[cut : cells.shape[0] - cut, cut : cells.shape[1] - cut]


def inside(rows_dev, cols_dev, width):
    rows_all = rows_dev * lax.axis_size("rows")
    cols_all = cols_dev * lax.axis_size("cols")
    row_at = lax.axis_index("rows") * rows_dev - width + jnp.arange(rows_dev + 2 * width)
    col_at = lax.axis_index("cols") * cols_dev - width + jnp.arange(cols_dev + 2 * width)
    row_ok = (row_at >= 0) & (row_at < rows_all)
    col_ok = (col_at >= 0) & (col_at < cols_all)
    return (row_ok[:, None] & col_ok[None, :])[..., None]


def convolve(field, weights):
    numbers = ("NHWC", "HWIO", "NHWC")
    result = lax.conv_general_dilated(
        field[None], weights, (1, 1), "VALID", dimension_numbers=numbers,
        preferred_element_type=jnp.float32,
    )
    return result[0]


def cell_step(stacked, weights, gate_bias, cell_prev):
    gates = convolve(stacked, weights) + gate_bias
    gate_in = jax.nn.sigmoid(gates[..., :HC])
    gate_forget = jax.nn.sigmoid(gates[..., HC : 2 * HC])
    gate_cand = jnp.tanh(gates[..., 2 * HC : 3 * HC])
    gate_out = jax.nn.sigmoid(gates[..., 3 * HC :])
    cell = gate_forget * cell_prev + gate_in * gate_cand
    hidden = (gate_out * jnp.tanh(cell)).astype(jnp.bfloat16)
    return (gate_in, gate_forget, gate_cand, gate_out), cell, hidden


def cell_grads(grad_cell, grad_hidden, gates, cell_prev, cell_now):
    gate_in, gate_forget, gate_cand, gate_out = gates
    tanh_cell = jnp.tanh(cell_now)
    summed = grad_hidden * gate_out * (1.0 - tanh_cell * tanh_cell)
    if grad_cell is not None:
        summed = grad_cell + summed
    pre_in = summed * gate_cand * gate_in * (1.0 - gate_in)
    pre_forget = summed * cell_prev * gate_forget * (1.0 - gate_forget)
    pre_cand = summed * gate_in * (1.0 - gate_cand * gate_cand)
    pre_out = grad_hidden * tanh_cell * gate_out * (1.0 - gate_out)
    grad_gates = jnp.concatenate([pre_in, pre_forget, pre_cand, pre_out], axis=-1).astype(
        jnp.bfloat16
    )
    return grad_gates, summed * gate_forget


def shards(frames, hidden_start, cell_start, kernel, gate_bias, cotangent):
    rows_dev = hidden_start.shape[0]
    cols_dev = hidden_start.shape[1]
    chans = CI + HC
    cells = rows_dev * cols_dev
    reach = 2 * STEPS
    pack = jnp.concatenate(
        [
            frames[0].reshape(rows_dev, cols_dev, CI),
            frames[1].reshape(rows_dev, cols_dev, CI),
            hidden_start,
            cotangent[0],
            cotangent[1],
        ],
        axis=-1,
    )
    pack = surround(pack, reach)
    cell_zero = surround(cell_start, reach - 1)
    inputs_one = pack[..., :CI]
    inputs_two = pack[..., CI : 2 * CI]
    hidden_zero = pack[..., 2 * CI : 2 * CI + HC]
    cot_zero = pack[..., 2 * CI + HC : 2 * CI + 2 * HC]
    cot_one = pack[..., 2 * CI + 2 * HC :]

    weights = kernel.reshape(KS, KS, chans, GATES)
    flipped = jnp.transpose(weights[::-1, ::-1, CI:, :], (0, 1, 3, 2))
    stacked_one = jnp.concatenate([inputs_one, hidden_zero], axis=-1)
    gates_one, cell_one, hidden_one = cell_step(stacked_one, weights, gate_bias, cell_zero)
    hidden_one = jnp.where(inside(rows_dev, cols_dev, reach - 1), hidden_one, 0)

    stacked_two = jnp.concatenate([inner(inputs_two, reach, reach - 1), hidden_one], axis=-1)
    cell_one_two = inner(cell_one, reach - 1, reach - 2)
    gates_two, cell_two, hidden_two = cell_step(stacked_two, weights, gate_bias, cell_one_two)
    hidden_final = inner(hidden_two, reach - 2, 0)

    grad_gates_two, grad_cell = cell_grads(
        None, inner(cot_one, reach, reach - 2).astype(jnp.float32), gates_two, cell_one_two, cell_two
    )
    masked_two = jnp.where(inside(rows_dev, cols_dev, reach - 2), grad_gates_two, 0)
    grad_hidden = convolve(masked_two, flipped) + inner(cot_zero, reach, reach - 3).astype(jnp.float32)

    def near(values, width):
        return inner(values, width, reach - 3)

    gates_near = tuple(near(g, reach - 1) for g in gates_one)
    grad_gates_one, grad_cell = cell_grads(
        near(grad_cell, reach - 2),
        grad_hidden,
        gates_near,
        near(cell_zero, reach - 1),
        near(cell_one, reach - 1),
    )
    grad_cell_start = inner(grad_cell, reach - 3, 0)
    masked_one = jnp.where(inside(rows_dev, cols_dev, reach - 3), grad_gates_one, 0)
    grad_hidden_start = convolve(masked_one, flipped)

    spare = SUM_ROWS - KIN - 1
    near = [inner(stacked_two, reach - 1, 1), inner(stacked_one, reach, 1)]
    grads_seen = [
        inner(grad_gates_two, reach - 2, 0).reshape(cells, GATES),
        inner(grad_gates_one, reach - 3, 0).reshape(cells, GATES),
    ]
    first, rest = summing_levels()
    axis, bit = first[0]
    pairs = flip_pairs(axis, bit)
    upper = (lax.axis_index(axis) >> bit) & 1
    near = near + [lax.ppermute(s, axis, pairs) for s in near]
    grads_seen = grads_seen + [lax.ppermute(g, axis, pairs) for g in grads_seen]
    lifted = []
    for stacked in near:
        patches = tap_columns(stacked, rows_dev, cols_dev, False)
        lifted.append(
            jnp.concatenate(
                [
                    patches,
                    jnp.ones((cells, 1), patches.dtype),
                    jnp.zeros((cells, spare), patches.dtype),
                ],
                axis=1,
            )
        )
    half = SUM_ROWS // 2
    lifted = lax.dynamic_slice_in_dim(jnp.concatenate(lifted, axis=0), upper * half, half, 1)
    total_cells = STEPS * rows_dev * lax.axis_size("rows") * cols_dev * lax.axis_size("cols")
    norm_scale = 1.0 / math.sqrt(total_cells)
    joined = jnp.dot(
        lifted.T, jnp.concatenate(grads_seen, axis=0), preferred_element_type=jnp.float32
    )
    kernel_grad, bias_grad = sum_everywhere(joined * norm_scale, first, rest)
    return (hidden_final, grad_hidden_start, grad_cell_start, kernel_grad, bias_grad)


def solution(mesh):
    placed = (
        P(None, "rows", "cols"),
        P("rows", "cols", None),
        P("rows", "cols", None),
        P(),
        P(),
        P(None, "rows", "cols", None),
    )
    return jax.shard_map(
        shards,
        mesh=mesh,
        in_specs=placed,
        out_specs=(
            P("rows", "cols", None),
            P("rows", "cols", None),
            P("rows", "cols", None),
            P(),
            P(),
        ),
        check_vma=False,
    )
```

```python
import math

import jax
import jax.numpy as jnp
from jax import lax
from jax.sharding import PartitionSpec as P

HC = 128
CI = 32
KS = 3
STEPS = 2
GATES = 512
KIN = 1440
SUM_ROWS = 1536
SUM_WAYS = 3
SUM_SHARED = 2


def flip_pairs(axis, bit):
    count = lax.axis_size(axis)
    return [(i, i ^ (1 << bit)) for i in range(count)]


def summing_levels():
    levels = []
    for axis in ("cols", "rows"):
        count = lax.axis_size(axis)
        depth = count.bit_length() - 1
        assert (1 << depth) == count
        levels.extend((axis, bit) for bit in range(depth))
    cols_levels = [lv for lv in levels if lv[0] == "cols"]
    rows_levels = [lv for lv in levels if lv[0] == "rows"]
    return cols_levels[:1], cols_levels[1:2] + rows_levels + cols_levels[2:]


def halve(part, levels, limit=None):
    halved = []
    for axis, bit in levels:
        rows = part.shape[0]
        if rows % 16 != 0 or len(halved) == limit:
            break
        half = rows // 2
        upper = (lax.axis_index(axis) >> bit) & 1
        keep = lax.dynamic_slice_in_dim(part, upper * half, half, 0)
        send = lax.dynamic_slice_in_dim(part, (1 - upper) * half, half, 0)
        part = keep + lax.ppermute(send, axis, flip_pairs(axis, bit))
        halved.append((axis, bit))
    for axis, bit in levels[len(halved):]:
        part = part + lax.ppermute(part, axis, flip_pairs(axis, bit))
    return part, halved


def double(piece, halved):
    for axis, bit in reversed(halved):
        upper = (lax.axis_index(axis) >> bit) & 1
        got = lax.ppermute(piece, axis, flip_pairs(axis, bit))
        low = jnp.where(upper == 0, piece, got)
        high = jnp.where(upper == 0, got, piece)
        piece = jnp.concatenate([low, high], axis=0)
    return piece


def sum_everywhere(part, first_halved, rest):
    ways = min(SUM_WAYS, max(len(rest), 1))
    width = part.shape[0] // ways
    pieces = []
    for way in range(ways):
        order = rest[way:] + rest[:way]
        chunk, halved = halve(
            part[way * width : (way + 1) * width], order, max(len(order) - SUM_SHARED, 0)
        )
        pieces.append(double(chunk.astype(jnp.bfloat16), halved))
    piece = jnp.concatenate(pieces, axis=0)
    if len(first_halved) == 1:
        axis, bit = first_halved[0]
        upper = (lax.axis_index(axis) >> bit) & 1
        got = lax.ppermute(piece, axis, flip_pairs(axis, bit))
        low = jnp.where(upper == 0, piece, got)
        high = jnp.where(upper == 0, got, piece)
        split = KIN - low.shape[0]
        kernel_part = jnp.concatenate([low, high[:split]], axis=0).astype(jnp.float32)
        return kernel_part, high[split].astype(jnp.float32)
    summed = double(piece, first_halved).astype(jnp.float32)
    return summed[:KIN], summed[KIN]

def tap_columns(padded, rows_dev, cols_dev, reverse):
    pieces = []
    for tap_row in range(KS):
        for tap_col in range(KS):
            if reverse:
                first_row = KS - 1 - tap_row
                first_col = KS - 1 - tap_col
            else:
                first_row = tap_row
                first_col = tap_col
            pieces.append(
                padded[first_row : first_row + rows_dev, first_col : first_col + cols_dev]
            )
    joined = jnp.concatenate(pieces, axis=-1)
    return joined.reshape(rows_dev * cols_dev, joined.shape[-1])


def widen(cells, axis, dim, width):
    count = lax.axis_size(axis)
    size = cells.shape[dim]
    before, after = [], []
    need, dist = width, 1
    while need > 0:
        take = min(need, size)
        if dist < count:
            tail = lax.slice_in_dim(cells, size - take, size, axis=dim)
            head = lax.slice_in_dim(cells, 0, take, axis=dim)
            before.insert(0, lax.ppermute(tail, axis, [(i, i + dist) for i in range(count - dist)]))
            after.append(lax.ppermute(head, axis, [(i + dist, i) for i in range(count - dist)]))
        else:
            blank = list(cells.shape)
            blank[dim] = take
            before.insert(0, jnp.zeros(blank, cells.dtype))
            after.append(jnp.zeros(blank, cells.dtype))
        need -= take
        dist += 1
    return jnp.concatenate(before + [cells] + after, axis=dim)


def surround(cells, width):
    return widen(widen(cells, "rows", 0, width), "cols", 1, width)


def inner(cells, outer, inner_width):
    cut = outer - inner_width
    return cells[cut : cells.shape[0] - cut, cut : cells.shape[1] - cut]


def inside(rows_dev, cols_dev, width):
    rows_all = rows_dev * lax.axis_size("rows")
    cols_all = cols_dev * lax.axis_size("cols")
    row_at = lax.axis_index("rows") * rows_dev - width + jnp.arange(rows_dev + 2 * width)
    col_at = lax.axis_index("cols") * cols_dev - width + jnp.arange(cols_dev + 2 * width)
    row_ok = (row_at >= 0) & (row_at < rows_all)
    col_ok = (col_at >= 0) & (col_at < cols_all)
    return (row_ok[:, None] & col_ok[None, :])[..., None]


def convolve(field, weights):
    numbers = ("NHWC", "HWIO", "NHWC")
    result = lax.conv_general_dilated(
        field[None], weights, (1, 1), "VALID", dimension_numbers=numbers,
        preferred_element_type=jnp.float32,
    )
    return result[0]


def cell_step(stacked, weights, gate_bias, cell_prev):
    gates = convolve(stacked, weights) + gate_bias
    gate_in = jax.nn.sigmoid(gates[..., :HC])
    gate_forget = jax.nn.sigmoid(gates[..., HC : 2 * HC])
    gate_cand = jnp.tanh(gates[..., 2 * HC : 3 * HC])
    gate_out = jax.nn.sigmoid(gates[..., 3 * HC :])
    cell = gate_forget * cell_prev + gate_in * gate_cand
    hidden = (gate_out * jnp.tanh(cell)).astype(jnp.bfloat16)
    return (gate_in, gate_forget, gate_cand, gate_out), cell, hidden


def cell_grads(grad_cell, grad_hidden, gates, cell_prev, cell_now):
    gate_in, gate_forget, gate_cand, gate_out = gates
    tanh_cell = jnp.tanh(cell_now)
    summed = grad_hidden * gate_out * (1.0 - tanh_cell * tanh_cell)
    if grad_cell is not None:
        summed = grad_cell + summed
    pre_in = summed * gate_cand * gate_in * (1.0 - gate_in)
    pre_forget = summed * cell_prev * gate_forget * (1.0 - gate_forget)
    pre_cand = summed * gate_in * (1.0 - gate_cand * gate_cand)
    pre_out = grad_hidden * tanh_cell * gate_out * (1.0 - gate_out)
    grad_gates = jnp.concatenate([pre_in, pre_forget, pre_cand, pre_out], axis=-1).astype(
        jnp.bfloat16
    )
    return grad_gates, summed * gate_forget


def shards(frames, hidden_start, cell_start, kernel, gate_bias, cotangent):
    rows_dev = hidden_start.shape[0]
    cols_dev = hidden_start.shape[1]
    chans = CI + HC
    cells = rows_dev * cols_dev
    reach = 2 * STEPS
    pack = jnp.concatenate(
        [
            frames[0].reshape(rows_dev, cols_dev, CI),
            frames[1].reshape(rows_dev, cols_dev, CI),
            hidden_start,
            cotangent[0],
            cotangent[1],
        ],
        axis=-1,
    )
    pack = surround(pack, reach)
    cell_zero = surround(cell_start, reach - 1)
    inputs_one = pack[..., :CI]
    inputs_two = pack[..., CI : 2 * CI]
    hidden_zero = pack[..., 2 * CI : 2 * CI + HC]
    cot_zero = pack[..., 2 * CI + HC : 2 * CI + 2 * HC]
    cot_one = pack[..., 2 * CI + 2 * HC :]

    weights = kernel.reshape(KS, KS, chans, GATES)
    flipped = jnp.transpose(weights[::-1, ::-1, CI:, :], (0, 1, 3, 2))
    stacked_one = jnp.concatenate([inputs_one, hidden_zero], axis=-1)
    gates_one, cell_one, hidden_one = cell_step(stacked_one, weights, gate_bias, cell_zero)
    hidden_one = jnp.where(inside(rows_dev, cols_dev, reach - 1), hidden_one, 0)

    stacked_two = jnp.concatenate([inner(inputs_two, reach, reach - 1), hidden_one], axis=-1)
    cell_one_two = inner(cell_one, reach - 1, reach - 2)
    gates_two, cell_two, hidden_two = cell_step(stacked_two, weights, gate_bias, cell_one_two)
    hidden_final = inner(hidden_two, reach - 2, 0)

    grad_gates_two, grad_cell = cell_grads(
        None, inner(cot_one, reach, reach - 2).astype(jnp.float32), gates_two, cell_one_two, cell_two
    )
    masked_two = jnp.where(inside(rows_dev, cols_dev, reach - 2), grad_gates_two, 0)
    grad_hidden = convolve(masked_two, flipped) + inner(cot_zero, reach, reach - 3).astype(jnp.float32)

    def near(values, width):
        return inner(values, width, reach - 3)

    gates_near = tuple(near(g, reach - 1) for g in gates_one)
    grad_gates_one, grad_cell = cell_grads(
        near(grad_cell, reach - 2),
        grad_hidden,
        gates_near,
        near(cell_zero, reach - 1),
        near(cell_one, reach - 1),
    )
    grad_cell_start = inner(grad_cell, reach - 3, 0)
    masked_one = jnp.where(inside(rows_dev, cols_dev, reach - 3), grad_gates_one, 0)
    grad_hidden_start = convolve(masked_one, flipped)

    spare = SUM_ROWS - KIN - 1
    near = [inner(stacked_two, reach - 1, 1), inner(stacked_one, reach, 1)]
    grads_seen = [
        inner(grad_gates_two, reach - 2, 0).reshape(cells, GATES),
        inner(grad_gates_one, reach - 3, 0).reshape(cells, GATES),
    ]
    first, rest = summing_levels()
    axis, bit = first[0]
    pairs = flip_pairs(axis, bit)
    upper = (lax.axis_index(axis) >> bit) & 1
    near = near + [lax.ppermute(s, axis, pairs) for s in near]
    grads_seen = grads_seen + [lax.ppermute(g, axis, pairs) for g in grads_seen]
    lifted = []
    for stacked in near:
        patches = tap_columns(stacked, rows_dev, cols_dev, False)
        lifted.append(
            jnp.concatenate(
                [
                    patches,
                    jnp.ones((cells, 1), patches.dtype),
                    jnp.zeros((cells, spare), patches.dtype),
                ],
                axis=1,
            )
        )
    half = SUM_ROWS // 2
    lifted = lax.dynamic_slice_in_dim(jnp.concatenate(lifted, axis=0), upper * half, half, 1)
    total_cells = STEPS * rows_dev * lax.axis_size("rows") * cols_dev * lax.axis_size("cols")
    norm_scale = 1.0 / math.sqrt(total_cells)
    joined = jnp.dot(
        lifted.T, jnp.concatenate(grads_seen, axis=0), preferred_element_type=jnp.float32
    )
    kernel_grad, bias_grad = sum_everywhere(joined * norm_scale, first, rest)
    return (hidden_final, grad_hidden_start, grad_cell_start, kernel_grad, bias_grad)


def solution(mesh):
    placed = (
        P(None, "rows", "cols"),
        P("rows", "cols", None),
        P("rows", "cols", None),
        P(),
        P(),
        P(None, "rows", "cols", None),
    )
    return jax.shard_map(
        shards,
        mesh=mesh,
        in_specs=placed,
        out_specs=(
            P("rows", "cols", None),
            P("rows", "cols", None),
            P("rows", "cols", None),
            P(),
            P(),
        ),
        check_vma=False,
    )
```

```python
import math

import jax
import jax.numpy as jnp
from jax import lax
from jax.sharding import PartitionSpec as P

HC = 128
CI = 32
KS = 3
STEPS = 2
GATES = 512
KIN = 1440
SUM_ROWS = 1536
SUM_WAYS = 3
SUM_SHARED = 2


def flip_pairs(axis, bit):
    count = lax.axis_size(axis)
    return [(i, i ^ (1 << bit)) for i in range(count)]


def summing_levels():
    levels = []
    for axis in ("cols", "rows"):
        count = lax.axis_size(axis)
        depth = count.bit_length() - 1
        assert (1 << depth) == count
        levels.extend((axis, bit) for bit in range(depth))
    cols_levels = [lv for lv in levels if lv[0] == "cols"]
    rows_levels = [lv for lv in levels if lv[0] == "rows"]
    return cols_levels[:1], cols_levels[1:2] + rows_levels + cols_levels[2:]


def halve(part, levels, limit=None):
    halved = []
    for axis, bit in levels:
        rows = part.shape[0]
        if rows % 16 != 0 or len(halved) == limit:
            break
        half = rows // 2
        upper = (lax.axis_index(axis) >> bit) & 1
        keep = lax.dynamic_slice_in_dim(part, upper * half, half, 0)
        send = lax.dynamic_slice_in_dim(part, (1 - upper) * half, half, 0)
        part = keep + lax.ppermute(send, axis, flip_pairs(axis, bit))
        halved.append((axis, bit))
    for axis, bit in levels[len(halved):]:
        part = part + lax.ppermute(part, axis, flip_pairs(axis, bit))
    return part, halved


def double(piece, halved):
    for axis, bit in reversed(halved):
        upper = (lax.axis_index(axis) >> bit) & 1
        got = lax.ppermute(piece, axis, flip_pairs(axis, bit))
        low = jnp.where(upper == 0, piece, got)
        high = jnp.where(upper == 0, got, piece)
        piece = jnp.concatenate([low, high], axis=0)
    return piece


def sum_everywhere(part, first_halved, rest):
    ways = min(SUM_WAYS, max(len(rest), 1))
    width = part.shape[0] // ways
    pieces = []
    for way in range(ways):
        order = rest[way:] + rest[:way]
        chunk, halved = halve(
            part[way * width : (way + 1) * width], order, max(len(order) - SUM_SHARED, 0)
        )
        pieces.append(double(chunk.astype(jnp.bfloat16), halved))
    piece = jnp.concatenate(pieces, axis=0)
    if len(first_halved) == 1:
        axis, bit = first_halved[0]
        upper = (lax.axis_index(axis) >> bit) & 1
        got = lax.ppermute(piece, axis, flip_pairs(axis, bit))
        low = jnp.where(upper == 0, piece, got)
        high = jnp.where(upper == 0, got, piece)
        split = KIN - low.shape[0]
        kernel_part = jnp.concatenate([low, high[:split]], axis=0).astype(jnp.float32)
        return kernel_part, high[split].astype(jnp.float32)
    summed = double(piece, first_halved).astype(jnp.float32)
    return summed[:KIN], summed[KIN]

def tap_columns(padded, rows_dev, cols_dev, reverse):
    pieces = []
    for tap_row in range(KS):
        for tap_col in range(KS):
            if reverse:
                first_row = KS - 1 - tap_row
                first_col = KS - 1 - tap_col
            else:
                first_row = tap_row
                first_col = tap_col
            pieces.append(
                padded[first_row : first_row + rows_dev, first_col : first_col + cols_dev]
            )
    joined = jnp.concatenate(pieces, axis=-1)
    return joined.reshape(rows_dev * cols_dev, joined.shape[-1])


def widen(cells, axis, dim, width):
    count = lax.axis_size(axis)
    size = cells.shape[dim]
    before, after = [], []
    need, dist = width, 1
    while need > 0:
        take = min(need, size)
        if dist < count:
            tail = lax.slice_in_dim(cells, size - take, size, axis=dim)
            head = lax.slice_in_dim(cells, 0, take, axis=dim)
            before.insert(0, lax.ppermute(tail, axis, [(i, i + dist) for i in range(count - dist)]))
            after.append(lax.ppermute(head, axis, [(i + dist, i) for i in range(count - dist)]))
        else:
            blank = list(cells.shape)
            blank[dim] = take
            before.insert(0, jnp.zeros(blank, cells.dtype))
            after.append(jnp.zeros(blank, cells.dtype))
        need -= take
        dist += 1
    return jnp.concatenate(before + [cells] + after, axis=dim)


def split_exact(values):
    high = lax.reduce_precision(values, exponent_bits=8, mantissa_bits=7)
    rest = values - high
    middle = lax.reduce_precision(rest, exponent_bits=8, mantissa_bits=7)
    low = rest - middle
    parts = [high, middle, low]
    return jnp.concatenate([p.astype(jnp.bfloat16) for p in parts], axis=-1)


def join_exact(parts):
    width = parts.shape[-1] // 3
    pieces = [parts[..., k * width : (k + 1) * width].astype(jnp.float32) for k in range(3)]
    return (pieces[0] + pieces[1]) + pieces[2]


def surround(cells, width):
    return widen(widen(cells, "rows", 0, width), "cols", 1, width)


def inner(cells, outer, inner_width):
    cut = outer - inner_width
    return cells[cut : cells.shape[0] - cut, cut : cells.shape[1] - cut]


def inside(rows_dev, cols_dev, width):
    rows_all = rows_dev * lax.axis_size("rows")
    cols_all = cols_dev * lax.axis_size("cols")
    row_at = lax.axis_index("rows") * rows_dev - width + jnp.arange(rows_dev + 2 * width)
    col_at = lax.axis_index("cols") * cols_dev - width + jnp.arange(cols_dev + 2 * width)
    row_ok = (row_at >= 0) & (row_at < rows_all)
    col_ok = (col_at >= 0) & (col_at < cols_all)
    return (row_ok[:, None] & col_ok[None, :])[..., None]


def convolve(field, weights):
    numbers = ("NHWC", "HWIO", "NHWC")
    result = lax.conv_general_dilated(
        field[None], weights, (1, 1), "VALID", dimension_numbers=numbers,
        preferred_element_type=jnp.float32,
    )
    return result[0]


def cell_step(stacked, weights, gate_bias, cell_prev):
    gates = convolve(stacked, weights) + gate_bias
    gate_in = jax.nn.sigmoid(gates[..., :HC])
    gate_forget = jax.nn.sigmoid(gates[..., HC : 2 * HC])
    gate_cand = jnp.tanh(gates[..., 2 * HC : 3 * HC])
    gate_out = jax.nn.sigmoid(gates[..., 3 * HC :])
    cell = gate_forget * cell_prev + gate_in * gate_cand
    hidden = (gate_out * jnp.tanh(cell)).astype(jnp.bfloat16)
    return (gate_in, gate_forget, gate_cand, gate_out), cell, hidden


def cell_grads(grad_cell, grad_hidden, gates, cell_prev, cell_now):
    gate_in, gate_forget, gate_cand, gate_out = gates
    tanh_cell = jnp.tanh(cell_now)
    summed = grad_hidden * gate_out * (1.0 - tanh_cell * tanh_cell)
    if grad_cell is not None:
        summed = grad_cell + summed
    pre_in = summed * gate_cand * gate_in * (1.0 - gate_in)
    pre_forget = summed * cell_prev * gate_forget * (1.0 - gate_forget)
    pre_cand = summed * gate_in * (1.0 - gate_cand * gate_cand)
    pre_out = grad_hidden * tanh_cell * gate_out * (1.0 - gate_out)
    grad_gates = jnp.concatenate([pre_in, pre_forget, pre_cand, pre_out], axis=-1).astype(
        jnp.bfloat16
    )
    return grad_gates, summed * gate_forget


def shards(frames, hidden_start, cell_start, kernel, gate_bias, cotangent):
    rows_dev = hidden_start.shape[0]
    cols_dev = hidden_start.shape[1]
    chans = CI + HC
    cells = rows_dev * cols_dev
    reach = 2 * STEPS
    pack = jnp.concatenate(
        [
            frames[0].reshape(rows_dev, cols_dev, CI),
            frames[1].reshape(rows_dev, cols_dev, CI),
            hidden_start,
            cotangent[0],
            cotangent[1],
            split_exact(cell_start),
        ],
        axis=-1,
    )
    pack = surround(pack, reach)
    cell_zero = inner(join_exact(pack[..., 2 * CI + 3 * HC :]), reach, reach - 1)
    pack = pack[..., : 2 * CI + 3 * HC]
    inputs_one = pack[..., :CI]
    inputs_two = pack[..., CI : 2 * CI]
    hidden_zero = pack[..., 2 * CI : 2 * CI + HC]
    cot_zero = pack[..., 2 * CI + HC : 2 * CI + 2 * HC]
    cot_one = pack[..., 2 * CI + 2 * HC :]

    weights = kernel.reshape(KS, KS, chans, GATES)
    flipped = jnp.transpose(weights[::-1, ::-1, CI:, :], (0, 1, 3, 2))
    stacked_one = jnp.concatenate([inputs_one, hidden_zero], axis=-1)
    gates_one, cell_one, hidden_one = cell_step(stacked_one, weights, gate_bias, cell_zero)
    hidden_one = jnp.where(inside(rows_dev, cols_dev, reach - 1), hidden_one, 0)

    stacked_two = jnp.concatenate([inner(inputs_two, reach, reach - 1), hidden_one], axis=-1)
    cell_one_two = inner(cell_one, reach - 1, reach - 2)
    gates_two, cell_two, hidden_two = cell_step(stacked_two, weights, gate_bias, cell_one_two)
    hidden_final = inner(hidden_two, reach - 2, 0)

    grad_gates_two, grad_cell = cell_grads(
        None, inner(cot_one, reach, reach - 2).astype(jnp.float32), gates_two, cell_one_two, cell_two
    )
    masked_two = jnp.where(inside(rows_dev, cols_dev, reach - 2), grad_gates_two, 0)
    grad_hidden = convolve(masked_two, flipped) + inner(cot_zero, reach, reach - 3).astype(jnp.float32)

    def near(values, width):
        return inner(values, width, reach - 3)

    gates_near = tuple(near(g, reach - 1) for g in gates_one)
    grad_gates_one, grad_cell = cell_grads(
        near(grad_cell, reach - 2),
        grad_hidden,
        gates_near,
        near(cell_zero, reach - 1),
        near(cell_one, reach - 1),
    )
    grad_cell_start = inner(grad_cell, reach - 3, 0)
    masked_one = jnp.where(inside(rows_dev, cols_dev, reach - 3), grad_gates_one, 0)
    grad_hidden_start = convolve(masked_one, flipped)

    spare = SUM_ROWS - KIN - 1
    near = [inner(stacked_two, reach - 1, 1), inner(stacked_one, reach, 1)]
    grads_seen = [
        inner(grad_gates_two, reach - 2, 0).reshape(cells, GATES),
        inner(grad_gates_one, reach - 3, 0).reshape(cells, GATES),
    ]
    first, rest = summing_levels()
    axis, bit = first[0]
    pairs = flip_pairs(axis, bit)
    upper = (lax.axis_index(axis) >> bit) & 1
    near = near + [lax.ppermute(s, axis, pairs) for s in near]
    grads_seen = grads_seen + [lax.ppermute(g, axis, pairs) for g in grads_seen]
    lifted = []
    for stacked in near:
        patches = tap_columns(stacked, rows_dev, cols_dev, False)
        lifted.append(
            jnp.concatenate(
                [
                    patches,
                    jnp.ones((cells, 1), patches.dtype),
                    jnp.zeros((cells, spare), patches.dtype),
                ],
                axis=1,
            )
        )
    half = SUM_ROWS // 2
    lifted = lax.dynamic_slice_in_dim(jnp.concatenate(lifted, axis=0), upper * half, half, 1)
    total_cells = STEPS * rows_dev * lax.axis_size("rows") * cols_dev * lax.axis_size("cols")
    norm_scale = 1.0 / math.sqrt(total_cells)
    joined = jnp.dot(
        lifted.T, jnp.concatenate(grads_seen, axis=0), preferred_element_type=jnp.float32
    )
    kernel_grad, bias_grad = sum_everywhere(joined * norm_scale, first, rest)
    return (hidden_final, grad_hidden_start, grad_cell_start, kernel_grad, bias_grad)


def solution(mesh):
    placed = (
        P(None, "rows", "cols"),
        P("rows", "cols", None),
        P("rows", "cols", None),
        P(),
        P(),
        P(None, "rows", "cols", None),
    )
    return jax.shard_map(
        shards,
        mesh=mesh,
        in_specs=placed,
        out_specs=(
            P("rows", "cols", None),
            P("rows", "cols", None),
            P("rows", "cols", None),
            P(),
            P(),
        ),
        check_vma=False,
    )
```

```python
import math

import jax
import jax.numpy as jnp
from jax import lax
from jax.sharding import PartitionSpec as P

HC = 128
CI = 32
KS = 3
STEPS = 2
GATES = 512
KIN = 1440
SUM_ROWS = 1536
SUM_WAYS = 3
SUM_SHARED = 2


def flip_pairs(axis, bit):
    count = lax.axis_size(axis)
    return [(i, i ^ (1 << bit)) for i in range(count)]


def summing_levels():
    levels = []
    for axis in ("cols", "rows"):
        count = lax.axis_size(axis)
        depth = count.bit_length() - 1
        assert (1 << depth) == count
        levels.extend((axis, bit) for bit in range(depth))
    cols_levels = [lv for lv in levels if lv[0] == "cols"]
    rows_levels = [lv for lv in levels if lv[0] == "rows"]
    return cols_levels[:1], cols_levels[1:2] + rows_levels + cols_levels[2:]


def halve(part, levels, limit=None):
    halved = []
    for axis, bit in levels:
        rows = part.shape[0]
        if rows % 16 != 0 or len(halved) == limit:
            break
        half = rows // 2
        upper = (lax.axis_index(axis) >> bit) & 1
        keep = lax.dynamic_slice_in_dim(part, upper * half, half, 0)
        send = lax.dynamic_slice_in_dim(part, (1 - upper) * half, half, 0)
        part = keep + lax.ppermute(send, axis, flip_pairs(axis, bit))
        halved.append((axis, bit))
    for axis, bit in levels[len(halved):]:
        part = part + lax.ppermute(part, axis, flip_pairs(axis, bit))
    return part, halved


def double(piece, halved):
    for axis, bit in reversed(halved):
        upper = (lax.axis_index(axis) >> bit) & 1
        got = lax.ppermute(piece, axis, flip_pairs(axis, bit))
        low = jnp.where(upper == 0, piece, got)
        high = jnp.where(upper == 0, got, piece)
        piece = jnp.concatenate([low, high], axis=0)
    return piece


def sum_everywhere(part, first_halved, rest):
    ways = min(SUM_WAYS, max(len(rest), 1))
    width = part.shape[0] // ways
    pieces = []
    for way in range(ways):
        order = rest[way:] + rest[:way]
        chunk, halved = halve(
            part[way * width : (way + 1) * width], order, max(len(order) - SUM_SHARED, 0)
        )
        pieces.append(double(chunk.astype(jnp.bfloat16), halved))
    piece = jnp.concatenate(pieces, axis=0)
    if len(first_halved) == 1:
        axis, bit = first_halved[0]
        upper = (lax.axis_index(axis) >> bit) & 1
        got = lax.ppermute(piece, axis, flip_pairs(axis, bit))
        low = jnp.where(upper == 0, piece, got)
        high = jnp.where(upper == 0, got, piece)
        split = KIN - low.shape[0]
        kernel_part = jnp.concatenate([low, high[:split]], axis=0).astype(jnp.float32)
        return kernel_part, high[split].astype(jnp.float32)
    summed = double(piece, first_halved).astype(jnp.float32)
    return summed[:KIN], summed[KIN]

def tap_columns(padded, rows_dev, cols_dev, reverse):
    pieces = []
    for tap_row in range(KS):
        for tap_col in range(KS):
            if reverse:
                first_row = KS - 1 - tap_row
                first_col = KS - 1 - tap_col
            else:
                first_row = tap_row
                first_col = tap_col
            pieces.append(
                padded[first_row : first_row + rows_dev, first_col : first_col + cols_dev]
            )
    joined = jnp.concatenate(pieces, axis=-1)
    return joined.reshape(rows_dev * cols_dev, joined.shape[-1])


def widen(cells, axis, dim, width):
    count = lax.axis_size(axis)
    size = cells.shape[dim]
    before, after = [], []
    need, dist = width, 1
    while need > 0:
        take = min(need, size)
        if dist < count:
            tail = lax.slice_in_dim(cells, size - take, size, axis=dim)
            head = lax.slice_in_dim(cells, 0, take, axis=dim)
            before.insert(0, lax.ppermute(tail, axis, [(i, i + dist) for i in range(count - dist)]))
            after.append(lax.ppermute(head, axis, [(i + dist, i) for i in range(count - dist)]))
        else:
            blank = list(cells.shape)
            blank[dim] = take
            before.insert(0, jnp.zeros(blank, cells.dtype))
            after.append(jnp.zeros(blank, cells.dtype))
        need -= take
        dist += 1
    return jnp.concatenate(before + [cells] + after, axis=dim)


def split_exact(values):
    high = lax.reduce_precision(values, exponent_bits=8, mantissa_bits=7)
    rest = values - high
    middle = lax.reduce_precision(rest, exponent_bits=8, mantissa_bits=7)
    low = rest - middle
    parts = [high, middle, low]
    return jnp.concatenate([p.astype(jnp.bfloat16) for p in parts], axis=-1)


def join_exact(parts):
    width = parts.shape[-1] // 3
    pieces = [parts[..., k * width : (k + 1) * width].astype(jnp.float32) for k in range(3)]
    return (pieces[0] + pieces[1]) + pieces[2]


def surround(cells, width):
    return widen(widen(cells, "rows", 0, width), "cols", 1, width)


def inner(cells, outer, inner_width):
    cut = outer - inner_width
    return cells[cut : cells.shape[0] - cut, cut : cells.shape[1] - cut]


def inside(rows_dev, cols_dev, width):
    rows_all = rows_dev * lax.axis_size("rows")
    cols_all = cols_dev * lax.axis_size("cols")
    row_at = lax.axis_index("rows") * rows_dev - width + jnp.arange(rows_dev + 2 * width)
    col_at = lax.axis_index("cols") * cols_dev - width + jnp.arange(cols_dev + 2 * width)
    row_ok = (row_at >= 0) & (row_at < rows_all)
    col_ok = (col_at >= 0) & (col_at < cols_all)
    return (row_ok[:, None] & col_ok[None, :])[..., None]


def convolve(field, weights):
    numbers = ("NHWC", "HWIO", "NHWC")
    result = lax.conv_general_dilated(
        field[None], weights, (1, 1), "VALID", dimension_numbers=numbers,
        preferred_element_type=jnp.float32,
    )
    return result[0]


def cell_step(stacked, weights, gate_bias, cell_prev):
    gates = convolve(stacked, weights) + gate_bias
    gate_in = jax.nn.sigmoid(gates[..., :HC])
    gate_forget = jax.nn.sigmoid(gates[..., HC : 2 * HC])
    gate_cand = jnp.tanh(gates[..., 2 * HC : 3 * HC])
    gate_out = jax.nn.sigmoid(gates[..., 3 * HC :])
    cell = gate_forget * cell_prev + gate_in * gate_cand
    hidden = (gate_out * jnp.tanh(cell)).astype(jnp.bfloat16)
    return (gate_in, gate_forget, gate_cand, gate_out), cell, hidden


def cell_grads(grad_cell, grad_hidden, gates, cell_prev, cell_now):
    gate_in, gate_forget, gate_cand, gate_out = gates
    tanh_cell = jnp.tanh(cell_now)
    summed = grad_hidden * gate_out * (1.0 - tanh_cell * tanh_cell)
    if grad_cell is not None:
        summed = grad_cell + summed
    pre_in = summed * gate_cand * gate_in * (1.0 - gate_in)
    pre_forget = summed * cell_prev * gate_forget * (1.0 - gate_forget)
    pre_cand = summed * gate_in * (1.0 - gate_cand * gate_cand)
    pre_out = grad_hidden * tanh_cell * gate_out * (1.0 - gate_out)
    grad_gates = jnp.concatenate([pre_in, pre_forget, pre_cand, pre_out], axis=-1).astype(
        jnp.bfloat16
    )
    return grad_gates, summed * gate_forget


def shards(frames, hidden_start, cell_start, kernel, gate_bias, cotangent):
    rows_dev = hidden_start.shape[0]
    cols_dev = hidden_start.shape[1]
    chans = CI + HC
    cells = rows_dev * cols_dev
    reach = 2 * STEPS
    pack = jnp.concatenate(
        [
            frames[0].reshape(rows_dev, cols_dev, CI),
            frames[1].reshape(rows_dev, cols_dev, CI),
            hidden_start,
            cotangent[0],
            cotangent[1],
            split_exact(cell_start),
        ],
        axis=-1,
    )
    pack = surround(pack, reach)
    cell_zero = inner(join_exact(pack[..., 2 * CI + 3 * HC :]), reach, reach - 1)
    pack = pack[..., : 2 * CI + 3 * HC]
    inputs_one = pack[..., :CI]
    inputs_two = pack[..., CI : 2 * CI]
    hidden_zero = pack[..., 2 * CI : 2 * CI + HC]
    cot_zero = pack[..., 2 * CI + HC : 2 * CI + 2 * HC]
    cot_one = pack[..., 2 * CI + 2 * HC :]

    weights = kernel.reshape(KS, KS, chans, GATES)
    flipped = jnp.transpose(weights[::-1, ::-1, CI:, :], (0, 1, 3, 2))
    stacked_one = jnp.concatenate([inputs_one, hidden_zero], axis=-1)
    gates_one, cell_one, hidden_one = cell_step(stacked_one, weights, gate_bias, cell_zero)
    hidden_one = jnp.where(inside(rows_dev, cols_dev, reach - 1), hidden_one, 0)

    stacked_two = jnp.concatenate([inner(inputs_two, reach, reach - 1), hidden_one], axis=-1)
    cell_one_two = inner(cell_one, reach - 1, reach - 2)
    gates_two, cell_two, hidden_two = cell_step(stacked_two, weights, gate_bias, cell_one_two)
    hidden_final = inner(hidden_two, reach - 2, 0)

    grad_gates_two, grad_cell = cell_grads(
        None, inner(cot_one, reach, reach - 2).astype(jnp.float32), gates_two, cell_one_two, cell_two
    )
    masked_two = jnp.where(inside(rows_dev, cols_dev, reach - 2), grad_gates_two, 0)
    grad_hidden = convolve(masked_two, flipped) + inner(cot_zero, reach, reach - 3).astype(jnp.float32)

    def near(values, width):
        return inner(values, width, reach - 3)

    gates_near = tuple(near(g, reach - 1) for g in gates_one)
    grad_gates_one, grad_cell = cell_grads(
        near(grad_cell, reach - 2),
        grad_hidden,
        gates_near,
        near(cell_zero, reach - 1),
        near(cell_one, reach - 1),
    )
    grad_cell_start = inner(grad_cell, reach - 3, 0)
    masked_one = jnp.where(inside(rows_dev, cols_dev, reach - 3), grad_gates_one, 0)
    grad_hidden_start = convolve(masked_one, flipped)

    spare = SUM_ROWS - KIN - 1
    near = [inner(stacked_two, reach - 1, 1), inner(stacked_one, reach, 1)]
    grads_seen = [
        inner(grad_gates_two, reach - 2, 0).reshape(cells, GATES),
        inner(grad_gates_one, reach - 3, 0).reshape(cells, GATES),
    ]
    first, rest = summing_levels()
    axis, bit = first[0]
    pairs = flip_pairs(axis, bit)
    upper = (lax.axis_index(axis) >> bit) & 1
    theirs = lax.ppermute(jnp.concatenate(near, axis=-1), axis, pairs)
    near = near + [theirs[..., :chans], theirs[..., chans:]]
    grads_seen = grads_seen + [lax.ppermute(jnp.concatenate(grads_seen, axis=0), axis, pairs)]
    lifted = []
    for stacked in near:
        patches = tap_columns(stacked, rows_dev, cols_dev, False)
        lifted.append(
            jnp.concatenate(
                [
                    patches,
                    jnp.ones((cells, 1), patches.dtype),
                    jnp.zeros((cells, spare), patches.dtype),
                ],
                axis=1,
            )
        )
    half = SUM_ROWS // 2
    lifted = lax.dynamic_slice_in_dim(jnp.concatenate(lifted, axis=0), upper * half, half, 1)
    total_cells = STEPS * rows_dev * lax.axis_size("rows") * cols_dev * lax.axis_size("cols")
    norm_scale = 1.0 / math.sqrt(total_cells)
    joined = jnp.dot(
        lifted.T, jnp.concatenate(grads_seen, axis=0), preferred_element_type=jnp.float32
    )
    kernel_grad, bias_grad = sum_everywhere(joined * norm_scale, first, rest)
    return (hidden_final, grad_hidden_start, grad_cell_start, kernel_grad, bias_grad)


def solution(mesh):
    placed = (
        P(None, "rows", "cols"),
        P("rows", "cols", None),
        P("rows", "cols", None),
        P(),
        P(),
        P(None, "rows", "cols", None),
    )
    return jax.shard_map(
        shards,
        mesh=mesh,
        in_specs=placed,
        out_specs=(
            P("rows", "cols", None),
            P("rows", "cols", None),
            P("rows", "cols", None),
            P(),
            P(),
        ),
        check_vma=False,
    )
```

```python
import math

import jax
import jax.numpy as jnp
from jax import lax
from jax.sharding import PartitionSpec as P

HC = 128
CI = 32
KS = 3
STEPS = 2
GATES = 512
KIN = 1440
SUM_ROWS = 1536
SUM_WAYS = 3
SUM_SHARED = 2


def flip_pairs(axis, bit):
    count = lax.axis_size(axis)
    return [(i, i ^ (1 << bit)) for i in range(count)]


def summing_levels():
    levels = []
    for axis in ("cols", "rows"):
        count = lax.axis_size(axis)
        depth = count.bit_length() - 1
        assert (1 << depth) == count
        levels.extend((axis, bit) for bit in range(depth))
    cols_levels = [lv for lv in levels if lv[0] == "cols"]
    rows_levels = [lv for lv in levels if lv[0] == "rows"]
    return cols_levels[:1], cols_levels[1:2] + rows_levels + cols_levels[2:]


def halve(part, levels, limit=None):
    halved = []
    for axis, bit in levels:
        rows = part.shape[0]
        if rows % 16 != 0 or len(halved) == limit:
            break
        half = rows // 2
        upper = (lax.axis_index(axis) >> bit) & 1
        keep = lax.dynamic_slice_in_dim(part, upper * half, half, 0)
        send = lax.dynamic_slice_in_dim(part, (1 - upper) * half, half, 0)
        part = keep + lax.ppermute(send, axis, flip_pairs(axis, bit))
        halved.append((axis, bit))
    for axis, bit in levels[len(halved):]:
        part = part + lax.ppermute(part, axis, flip_pairs(axis, bit))
    return part, halved


def double(piece, halved):
    for axis, bit in reversed(halved):
        upper = (lax.axis_index(axis) >> bit) & 1
        got = lax.ppermute(piece, axis, flip_pairs(axis, bit))
        low = jnp.where(upper == 0, piece, got)
        high = jnp.where(upper == 0, got, piece)
        piece = jnp.concatenate([low, high], axis=0)
    return piece


def sum_everywhere(part, first_halved, rest):
    ways = min(SUM_WAYS, max(len(rest), 1))
    width = part.shape[0] // ways
    pieces = []
    for way in range(ways):
        order = rest[way:] + rest[:way]
        chunk, halved = halve(
            part[way * width : (way + 1) * width], order, max(len(order) - SUM_SHARED, 0)
        )
        pieces.append(double(chunk.astype(jnp.bfloat16), halved))
    piece = jnp.concatenate(pieces, axis=0)
    if len(first_halved) == 1:
        axis, bit = first_halved[0]
        upper = (lax.axis_index(axis) >> bit) & 1
        got = lax.ppermute(piece, axis, flip_pairs(axis, bit))
        low = jnp.where(upper == 0, piece, got)
        high = jnp.where(upper == 0, got, piece)
        split = KIN - low.shape[0]
        kernel_part = jnp.concatenate([low, high[:split]], axis=0).astype(jnp.float32)
        return kernel_part, high[split].astype(jnp.float32)
    summed = double(piece, first_halved).astype(jnp.float32)
    return summed[:KIN], summed[KIN]

def tap_columns(padded, rows_dev, cols_dev, reverse):
    pieces = []
    for tap_row in range(KS):
        for tap_col in range(KS):
            if reverse:
                first_row = KS - 1 - tap_row
                first_col = KS - 1 - tap_col
            else:
                first_row = tap_row
                first_col = tap_col
            pieces.append(
                padded[first_row : first_row + rows_dev, first_col : first_col + cols_dev]
            )
    joined = jnp.concatenate(pieces, axis=-1)
    return joined.reshape(rows_dev * cols_dev, joined.shape[-1])


def widen(cells, axis, dim, width):
    count = lax.axis_size(axis)
    size = cells.shape[dim]
    before, after = [], []
    need, dist = width, 1
    while need > 0:
        take = min(need, size)
        if dist < count:
            tail = lax.slice_in_dim(cells, size - take, size, axis=dim)
            head = lax.slice_in_dim(cells, 0, take, axis=dim)
            before.insert(0, lax.ppermute(tail, axis, [(i, i + dist) for i in range(count - dist)]))
            after.append(lax.ppermute(head, axis, [(i + dist, i) for i in range(count - dist)]))
        else:
            blank = list(cells.shape)
            blank[dim] = take
            before.insert(0, jnp.zeros(blank, cells.dtype))
            after.append(jnp.zeros(blank, cells.dtype))
        need -= take
        dist += 1
    return jnp.concatenate(before + [cells] + after, axis=dim)


def split_exact(values):
    high = lax.reduce_precision(values, exponent_bits=8, mantissa_bits=7)
    rest = values - high
    middle = lax.reduce_precision(rest, exponent_bits=8, mantissa_bits=7)
    low = rest - middle
    parts = [high, middle, low]
    return jnp.concatenate([p.astype(jnp.bfloat16) for p in parts], axis=-1)


def join_exact(parts):
    width = parts.shape[-1] // 3
    pieces = [parts[..., k * width : (k + 1) * width].astype(jnp.float32) for k in range(3)]
    return (pieces[0] + pieces[1]) + pieces[2]


def surround(cells, width):
    return widen(widen(cells, "cols", 1, width), "rows", 0, width)


def inner(cells, outer, inner_width):
    cut = outer - inner_width
    return cells[cut : cells.shape[0] - cut, cut : cells.shape[1] - cut]


def inside(rows_dev, cols_dev, width):
    rows_all = rows_dev * lax.axis_size("rows")
    cols_all = cols_dev * lax.axis_size("cols")
    row_at = lax.axis_index("rows") * rows_dev - width + jnp.arange(rows_dev + 2 * width)
    col_at = lax.axis_index("cols") * cols_dev - width + jnp.arange(cols_dev + 2 * width)
    row_ok = (row_at >= 0) & (row_at < rows_all)
    col_ok = (col_at >= 0) & (col_at < cols_all)
    return (row_ok[:, None] & col_ok[None, :])[..., None]


def convolve(field, weights):
    numbers = ("NHWC", "HWIO", "NHWC")
    result = lax.conv_general_dilated(
        field[None], weights, (1, 1), "VALID", dimension_numbers=numbers,
        preferred_element_type=jnp.float32,
    )
    return result[0]


def cell_step(stacked, weights, gate_bias, cell_prev):
    gates = convolve(stacked, weights) + gate_bias
    gate_in = jax.nn.sigmoid(gates[..., :HC])
    gate_forget = jax.nn.sigmoid(gates[..., HC : 2 * HC])
    gate_cand = jnp.tanh(gates[..., 2 * HC : 3 * HC])
    gate_out = jax.nn.sigmoid(gates[..., 3 * HC :])
    cell = gate_forget * cell_prev + gate_in * gate_cand
    hidden = (gate_out * jnp.tanh(cell)).astype(jnp.bfloat16)
    return (gate_in, gate_forget, gate_cand, gate_out), cell, hidden


def cell_grads(grad_cell, grad_hidden, gates, cell_prev, cell_now):
    gate_in, gate_forget, gate_cand, gate_out = gates
    tanh_cell = jnp.tanh(cell_now)
    summed = grad_hidden * gate_out * (1.0 - tanh_cell * tanh_cell)
    if grad_cell is not None:
        summed = grad_cell + summed
    pre_in = summed * gate_cand * gate_in * (1.0 - gate_in)
    pre_forget = summed * cell_prev * gate_forget * (1.0 - gate_forget)
    pre_cand = summed * gate_in * (1.0 - gate_cand * gate_cand)
    pre_out = grad_hidden * tanh_cell * gate_out * (1.0 - gate_out)
    grad_gates = jnp.concatenate([pre_in, pre_forget, pre_cand, pre_out], axis=-1).astype(
        jnp.bfloat16
    )
    return grad_gates, summed * gate_forget


def shards(frames, hidden_start, cell_start, kernel, gate_bias, cotangent):
    rows_dev = hidden_start.shape[0]
    cols_dev = hidden_start.shape[1]
    chans = CI + HC
    cells = rows_dev * cols_dev
    reach = 2 * STEPS
    pack = jnp.concatenate(
        [
            frames[0].reshape(rows_dev, cols_dev, CI),
            frames[1].reshape(rows_dev, cols_dev, CI),
            hidden_start,
            cotangent[0],
            cotangent[1],
            split_exact(cell_start),
        ],
        axis=-1,
    )
    pack = surround(pack, reach)
    cell_zero = inner(join_exact(pack[..., 2 * CI + 3 * HC :]), reach, reach - 1)
    pack = pack[..., : 2 * CI + 3 * HC]
    inputs_one = pack[..., :CI]
    inputs_two = pack[..., CI : 2 * CI]
    hidden_zero = pack[..., 2 * CI : 2 * CI + HC]
    cot_zero = pack[..., 2 * CI + HC : 2 * CI + 2 * HC]
    cot_one = pack[..., 2 * CI + 2 * HC :]

    weights = kernel.reshape(KS, KS, chans, GATES)
    flipped = jnp.transpose(weights[::-1, ::-1, CI:, :], (0, 1, 3, 2))
    stacked_one = jnp.concatenate([inputs_one, hidden_zero], axis=-1)
    gates_one, cell_one, hidden_one = cell_step(stacked_one, weights, gate_bias, cell_zero)
    hidden_one = jnp.where(inside(rows_dev, cols_dev, reach - 1), hidden_one, 0)

    stacked_two = jnp.concatenate([inner(inputs_two, reach, reach - 1), hidden_one], axis=-1)
    cell_one_two = inner(cell_one, reach - 1, reach - 2)
    gates_two, cell_two, hidden_two = cell_step(stacked_two, weights, gate_bias, cell_one_two)
    hidden_final = inner(hidden_two, reach - 2, 0)

    grad_gates_two, grad_cell = cell_grads(
        None, inner(cot_one, reach, reach - 2).astype(jnp.float32), gates_two, cell_one_two, cell_two
    )
    masked_two = jnp.where(inside(rows_dev, cols_dev, reach - 2), grad_gates_two, 0)
    grad_hidden = convolve(masked_two, flipped) + inner(cot_zero, reach, reach - 3).astype(jnp.float32)

    def near(values, width):
        return inner(values, width, reach - 3)

    gates_near = tuple(near(g, reach - 1) for g in gates_one)
    grad_gates_one, grad_cell = cell_grads(
        near(grad_cell, reach - 2),
        grad_hidden,
        gates_near,
        near(cell_zero, reach - 1),
        near(cell_one, reach - 1),
    )
    grad_cell_start = inner(grad_cell, reach - 3, 0)
    masked_one = jnp.where(inside(rows_dev, cols_dev, reach - 3), grad_gates_one, 0)
    grad_hidden_start = convolve(masked_one, flipped)

    spare = SUM_ROWS - KIN - 1
    near = [inner(stacked_two, reach - 1, 1), inner(stacked_one, reach, 1)]
    grads_seen = [
        inner(grad_gates_two, reach - 2, 0).reshape(cells, GATES),
        inner(grad_gates_one, reach - 3, 0).reshape(cells, GATES),
    ]
    first, rest = summing_levels()
    axis, bit = first[0]
    pairs = flip_pairs(axis, bit)
    upper = (lax.axis_index(axis) >> bit) & 1
    near = near + [lax.ppermute(s, axis, pairs) for s in near]
    grads_seen = grads_seen + [lax.ppermute(g, axis, pairs) for g in grads_seen]
    lifted = []
    for stacked in near:
        patches = tap_columns(stacked, rows_dev, cols_dev, False)
        lifted.append(
            jnp.concatenate(
                [
                    patches,
                    jnp.ones((cells, 1), patches.dtype),
                    jnp.zeros((cells, spare), patches.dtype),
                ],
                axis=1,
            )
        )
    half = SUM_ROWS // 2
    lifted = lax.dynamic_slice_in_dim(jnp.concatenate(lifted, axis=0), upper * half, half, 1)
    total_cells = STEPS * rows_dev * lax.axis_size("rows") * cols_dev * lax.axis_size("cols")
    norm_scale = 1.0 / math.sqrt(total_cells)
    joined = jnp.dot(
        lifted.T, jnp.concatenate(grads_seen, axis=0), preferred_element_type=jnp.float32
    )
    kernel_grad, bias_grad = sum_everywhere(joined * norm_scale, first, rest)
    return (hidden_final, grad_hidden_start, grad_cell_start, kernel_grad, bias_grad)


def solution(mesh):
    placed = (
        P(None, "rows", "cols"),
        P("rows", "cols", None),
        P("rows", "cols", None),
        P(),
        P(),
        P(None, "rows", "cols", None),
    )
    return jax.shard_map(
        shards,
        mesh=mesh,
        in_specs=placed,
        out_specs=(
            P("rows", "cols", None),
            P("rows", "cols", None),
            P("rows", "cols", None),
            P(),
            P(),
        ),
        check_vma=False,
    )
```

```python
import math

import jax
import jax.numpy as jnp
from jax import lax
from jax.sharding import PartitionSpec as P

HC = 128
CI = 32
KS = 3
STEPS = 2
GATES = 512
KIN = 1440
SUM_ROWS = 1536
SUM_WAYS = 3
SUM_SHARED = 2


def flip_pairs(axis, bit):
    count = lax.axis_size(axis)
    return [(i, i ^ (1 << bit)) for i in range(count)]


def summing_levels():
    levels = []
    for axis in ("cols", "rows"):
        count = lax.axis_size(axis)
        depth = count.bit_length() - 1
        assert (1 << depth) == count
        levels.extend((axis, bit) for bit in range(depth))
    cols_levels = [lv for lv in levels if lv[0] == "cols"]
    rows_levels = [lv for lv in levels if lv[0] == "rows"]
    return cols_levels[:1], cols_levels[1:2] + rows_levels + cols_levels[2:]


def halve(part, levels, limit=None):
    halved = []
    for axis, bit in levels:
        rows = part.shape[0]
        if rows % 16 != 0 or len(halved) == limit:
            break
        half = rows // 2
        upper = (lax.axis_index(axis) >> bit) & 1
        keep = lax.dynamic_slice_in_dim(part, upper * half, half, 0)
        send = lax.dynamic_slice_in_dim(part, (1 - upper) * half, half, 0)
        part = keep + lax.ppermute(send, axis, flip_pairs(axis, bit))
        halved.append((axis, bit))
    for axis, bit in levels[len(halved):]:
        part = part + lax.ppermute(part, axis, flip_pairs(axis, bit))
    return part, halved


def double(piece, halved):
    for axis, bit in reversed(halved):
        upper = (lax.axis_index(axis) >> bit) & 1
        got = lax.ppermute(piece, axis, flip_pairs(axis, bit))
        low = jnp.where(upper == 0, piece, got)
        high = jnp.where(upper == 0, got, piece)
        piece = jnp.concatenate([low, high], axis=0)
    return piece


def sum_everywhere(parts, first_halved, rest):
    pieces = []
    for way, part in enumerate(parts):
        order = rest[way:] + rest[:way]
        chunk, halved = halve(part, order, max(len(order) - SUM_SHARED, 0))
        pieces.append(double(chunk.astype(jnp.bfloat16), halved))
    piece = jnp.concatenate(pieces, axis=0)
    if len(first_halved) == 1:
        axis, bit = first_halved[0]
        upper = (lax.axis_index(axis) >> bit) & 1
        got = lax.ppermute(piece, axis, flip_pairs(axis, bit))
        low = jnp.where(upper == 0, piece, got)
        high = jnp.where(upper == 0, got, piece)
        split = KIN - low.shape[0]
        kernel_part = jnp.concatenate([low, high[:split]], axis=0).astype(jnp.float32)
        return kernel_part, high[split].astype(jnp.float32)
    summed = double(piece, first_halved).astype(jnp.float32)
    return summed[:KIN], summed[KIN]

def tap_columns(padded, rows_dev, cols_dev, reverse):
    pieces = []
    for tap_row in range(KS):
        for tap_col in range(KS):
            if reverse:
                first_row = KS - 1 - tap_row
                first_col = KS - 1 - tap_col
            else:
                first_row = tap_row
                first_col = tap_col
            pieces.append(
                padded[first_row : first_row + rows_dev, first_col : first_col + cols_dev]
            )
    joined = jnp.concatenate(pieces, axis=-1)
    return joined.reshape(rows_dev * cols_dev, joined.shape[-1])


def widen(cells, axis, dim, width):
    count = lax.axis_size(axis)
    size = cells.shape[dim]
    before, after = [], []
    need, dist = width, 1
    while need > 0:
        take = min(need, size)
        if dist < count:
            tail = lax.slice_in_dim(cells, size - take, size, axis=dim)
            head = lax.slice_in_dim(cells, 0, take, axis=dim)
            before.insert(0, lax.ppermute(tail, axis, [(i, i + dist) for i in range(count - dist)]))
            after.append(lax.ppermute(head, axis, [(i + dist, i) for i in range(count - dist)]))
        else:
            blank = list(cells.shape)
            blank[dim] = take
            before.insert(0, jnp.zeros(blank, cells.dtype))
            after.append(jnp.zeros(blank, cells.dtype))
        need -= take
        dist += 1
    return jnp.concatenate(before + [cells] + after, axis=dim)


def split_exact(values):
    high = lax.reduce_precision(values, exponent_bits=8, mantissa_bits=7)
    rest = values - high
    middle = lax.reduce_precision(rest, exponent_bits=8, mantissa_bits=7)
    low = rest - middle
    parts = [high, middle, low]
    return jnp.concatenate([p.astype(jnp.bfloat16) for p in parts], axis=-1)


def join_exact(parts):
    width = parts.shape[-1] // 3
    pieces = [parts[..., k * width : (k + 1) * width].astype(jnp.float32) for k in range(3)]
    return (pieces[0] + pieces[1]) + pieces[2]


def surround(cells, width):
    return widen(widen(cells, "rows", 0, width), "cols", 1, width)


def inner(cells, outer, inner_width):
    cut = outer - inner_width
    return cells[cut : cells.shape[0] - cut, cut : cells.shape[1] - cut]


def inside(rows_dev, cols_dev, width):
    rows_all = rows_dev * lax.axis_size("rows")
    cols_all = cols_dev * lax.axis_size("cols")
    row_at = lax.axis_index("rows") * rows_dev - width + jnp.arange(rows_dev + 2 * width)
    col_at = lax.axis_index("cols") * cols_dev - width + jnp.arange(cols_dev + 2 * width)
    row_ok = (row_at >= 0) & (row_at < rows_all)
    col_ok = (col_at >= 0) & (col_at < cols_all)
    return (row_ok[:, None] & col_ok[None, :])[..., None]


def convolve(field, weights):
    numbers = ("NHWC", "HWIO", "NHWC")
    result = lax.conv_general_dilated(
        field[None], weights, (1, 1), "VALID", dimension_numbers=numbers,
        preferred_element_type=jnp.float32,
    )
    return result[0]


def cell_step(stacked, weights, gate_bias, cell_prev):
    gates = convolve(stacked, weights) + gate_bias
    gate_in = jax.nn.sigmoid(gates[..., :HC])
    gate_forget = jax.nn.sigmoid(gates[..., HC : 2 * HC])
    gate_cand = jnp.tanh(gates[..., 2 * HC : 3 * HC])
    gate_out = jax.nn.sigmoid(gates[..., 3 * HC :])
    cell = gate_forget * cell_prev + gate_in * gate_cand
    hidden = (gate_out * jnp.tanh(cell)).astype(jnp.bfloat16)
    return (gate_in, gate_forget, gate_cand, gate_out), cell, hidden


def cell_grads(grad_cell, grad_hidden, gates, cell_prev, cell_now):
    gate_in, gate_forget, gate_cand, gate_out = gates
    tanh_cell = jnp.tanh(cell_now)
    summed = grad_hidden * gate_out * (1.0 - tanh_cell * tanh_cell)
    if grad_cell is not None:
        summed = grad_cell + summed
    pre_in = summed * gate_cand * gate_in * (1.0 - gate_in)
    pre_forget = summed * cell_prev * gate_forget * (1.0 - gate_forget)
    pre_cand = summed * gate_in * (1.0 - gate_cand * gate_cand)
    pre_out = grad_hidden * tanh_cell * gate_out * (1.0 - gate_out)
    grad_gates = jnp.concatenate([pre_in, pre_forget, pre_cand, pre_out], axis=-1).astype(
        jnp.bfloat16
    )
    return grad_gates, summed * gate_forget


def shards(frames, hidden_start, cell_start, kernel, gate_bias, cotangent):
    rows_dev = hidden_start.shape[0]
    cols_dev = hidden_start.shape[1]
    chans = CI + HC
    cells = rows_dev * cols_dev
    reach = 2 * STEPS
    pack = jnp.concatenate(
        [
            frames[0].reshape(rows_dev, cols_dev, CI),
            frames[1].reshape(rows_dev, cols_dev, CI),
            hidden_start,
            cotangent[0],
            cotangent[1],
            split_exact(cell_start),
        ],
        axis=-1,
    )
    pack = surround(pack, reach)
    cell_zero = inner(join_exact(pack[..., 2 * CI + 3 * HC :]), reach, reach - 1)
    pack = pack[..., : 2 * CI + 3 * HC]
    inputs_one = pack[..., :CI]
    inputs_two = pack[..., CI : 2 * CI]
    hidden_zero = pack[..., 2 * CI : 2 * CI + HC]
    cot_zero = pack[..., 2 * CI + HC : 2 * CI + 2 * HC]
    cot_one = pack[..., 2 * CI + 2 * HC :]

    weights = kernel.reshape(KS, KS, chans, GATES)
    flipped = jnp.transpose(weights[::-1, ::-1, CI:, :], (0, 1, 3, 2))
    stacked_one = jnp.concatenate([inputs_one, hidden_zero], axis=-1)
    gates_one, cell_one, hidden_one = cell_step(stacked_one, weights, gate_bias, cell_zero)
    hidden_one = jnp.where(inside(rows_dev, cols_dev, reach - 1), hidden_one, 0)

    stacked_two = jnp.concatenate([inner(inputs_two, reach, reach - 1), hidden_one], axis=-1)
    cell_one_two = inner(cell_one, reach - 1, reach - 2)
    gates_two, cell_two, hidden_two = cell_step(stacked_two, weights, gate_bias, cell_one_two)
    hidden_final = inner(hidden_two, reach - 2, 0)

    grad_gates_two, grad_cell = cell_grads(
        None, inner(cot_one, reach, reach - 2).astype(jnp.float32), gates_two, cell_one_two, cell_two
    )
    masked_two = jnp.where(inside(rows_dev, cols_dev, reach - 2), grad_gates_two, 0)
    grad_hidden = convolve(masked_two, flipped) + inner(cot_zero, reach, reach - 3).astype(jnp.float32)

    def near(values, width):
        return inner(values, width, reach - 3)

    gates_near = tuple(near(g, reach - 1) for g in gates_one)
    grad_gates_one, grad_cell = cell_grads(
        near(grad_cell, reach - 2),
        grad_hidden,
        gates_near,
        near(cell_zero, reach - 1),
        near(cell_one, reach - 1),
    )
    grad_cell_start = inner(grad_cell, reach - 3, 0)
    masked_one = jnp.where(inside(rows_dev, cols_dev, reach - 3), grad_gates_one, 0)
    grad_hidden_start = convolve(masked_one, flipped)

    spare = SUM_ROWS - KIN - 1
    near = [inner(stacked_two, reach - 1, 1), inner(stacked_one, reach, 1)]
    grads_seen = [
        inner(grad_gates_two, reach - 2, 0).reshape(cells, GATES),
        inner(grad_gates_one, reach - 3, 0).reshape(cells, GATES),
    ]
    first, rest = summing_levels()
    axis, bit = first[0]
    pairs = flip_pairs(axis, bit)
    upper = (lax.axis_index(axis) >> bit) & 1
    near = near + [lax.ppermute(s, axis, pairs) for s in near]
    grads_seen = grads_seen + [lax.ppermute(g, axis, pairs) for g in grads_seen]
    lifted = []
    for stacked in near:
        patches = tap_columns(stacked, rows_dev, cols_dev, False)
        lifted.append(
            jnp.concatenate(
                [
                    patches,
                    jnp.ones((cells, 1), patches.dtype),
                    jnp.zeros((cells, spare), patches.dtype),
                ],
                axis=1,
            )
        )
    half = SUM_ROWS // 2
    lifted = lax.dynamic_slice_in_dim(jnp.concatenate(lifted, axis=0), upper * half, half, 1)
    total_cells = STEPS * rows_dev * lax.axis_size("rows") * cols_dev * lax.axis_size("cols")
    norm_scale = 1.0 / math.sqrt(total_cells)
    grads_all = jnp.concatenate(grads_seen, axis=0)
    ways = min(SUM_WAYS, max(len(rest), 1))
    width = half // ways
    parts = [
        jnp.dot(
            lifted[:, way * width : (way + 1) * width].T,
            grads_all,
            preferred_element_type=jnp.float32,
        )
        * norm_scale
        for way in range(ways)
    ]
    kernel_grad, bias_grad = sum_everywhere(parts, first, rest)
    return (hidden_final, grad_hidden_start, grad_cell_start, kernel_grad, bias_grad)


def solution(mesh):
    placed = (
        P(None, "rows", "cols"),
        P("rows", "cols", None),
        P("rows", "cols", None),
        P(),
        P(),
        P(None, "rows", "cols", None),
    )
    return jax.shard_map(
        shards,
        mesh=mesh,
        in_specs=placed,
        out_specs=(
            P("rows", "cols", None),
            P("rows", "cols", None),
            P("rows", "cols", None),
            P(),
            P(),
        ),
        check_vma=False,
    )
```

```python
import math

import jax
import jax.numpy as jnp
from jax import lax
from jax.sharding import PartitionSpec as P

HC = 128
CI = 32
KS = 3
STEPS = 2
GATES = 512
KIN = 1440
SUM_ROWS = 1536
SUM_WAYS = 3
SUM_SHARED = 2


def flip_pairs(axis, bit):
    count = lax.axis_size(axis)
    return [(i, i ^ (1 << bit)) for i in range(count)]


def summing_levels():
    levels = []
    for axis in ("cols", "rows"):
        count = lax.axis_size(axis)
        depth = count.bit_length() - 1
        assert (1 << depth) == count
        levels.extend((axis, bit) for bit in range(depth))
    cols_levels = [lv for lv in levels if lv[0] == "cols"]
    rows_levels = [lv for lv in levels if lv[0] == "rows"]
    return cols_levels[:1], cols_levels[1:2] + rows_levels + cols_levels[2:]


def halve(part, levels, limit=None):
    halved = []
    for axis, bit in levels:
        rows = part.shape[0]
        if rows % 16 != 0 or len(halved) == limit:
            break
        half = rows // 2
        upper = (lax.axis_index(axis) >> bit) & 1
        keep = lax.dynamic_slice_in_dim(part, upper * half, half, 0)
        send = lax.dynamic_slice_in_dim(part, (1 - upper) * half, half, 0)
        part = keep + lax.ppermute(send, axis, flip_pairs(axis, bit))
        halved.append((axis, bit))
    for axis, bit in levels[len(halved):]:
        part = part + lax.ppermute(part, axis, flip_pairs(axis, bit))
    return part, halved


def double(piece, halved):
    for axis, bit in reversed(halved):
        upper = (lax.axis_index(axis) >> bit) & 1
        got = lax.ppermute(piece, axis, flip_pairs(axis, bit))
        low = jnp.where(upper == 0, piece, got)
        high = jnp.where(upper == 0, got, piece)
        piece = jnp.concatenate([low, high], axis=0)
    return piece


def sum_everywhere(part, first_halved, rest):
    ways = min(SUM_WAYS, max(len(rest), 1))
    width = part.shape[0] // ways
    pieces = []
    for way in range(ways):
        order = rest[way:] + rest[:way]
        chunk, halved = halve(
            part[way * width : (way + 1) * width], order, max(len(order) - SUM_SHARED, 0)
        )
        pieces.append(double(chunk.astype(jnp.bfloat16), halved))
    if len(first_halved) == 1:
        axis, bit = first_halved[0]
        upper = (lax.axis_index(axis) >> bit) & 1
        pairs = flip_pairs(axis, bit)
        swapped = [(p, lax.ppermute(p, axis, pairs)) for p in pieces]
        low = jnp.concatenate([jnp.where(upper == 0, p, g) for p, g in swapped], axis=0)
        high = jnp.concatenate([jnp.where(upper == 0, g, p) for p, g in swapped], axis=0)
        split = KIN - low.shape[0]
        kernel_part = jnp.concatenate([low, high[:split]], axis=0).astype(jnp.float32)
        return kernel_part, high[split].astype(jnp.float32)
    summed = double(jnp.concatenate(pieces, axis=0), first_halved).astype(jnp.float32)
    return summed[:KIN], summed[KIN]


def tap_columns(padded, rows_dev, cols_dev, reverse):
    pieces = []
    for tap_row in range(KS):
        for tap_col in range(KS):
            if reverse:
                first_row = KS - 1 - tap_row
                first_col = KS - 1 - tap_col
            else:
                first_row = tap_row
                first_col = tap_col
            pieces.append(
                padded[first_row : first_row + rows_dev, first_col : first_col + cols_dev]
            )
    joined = jnp.concatenate(pieces, axis=-1)
    return joined.reshape(rows_dev * cols_dev, joined.shape[-1])


def widen(cells, axis, dim, width):
    count = lax.axis_size(axis)
    size = cells.shape[dim]
    before, after = [], []
    need, dist = width, 1
    while need > 0:
        take = min(need, size)
        if dist < count:
            tail = lax.slice_in_dim(cells, size - take, size, axis=dim)
            head = lax.slice_in_dim(cells, 0, take, axis=dim)
            before.insert(0, lax.ppermute(tail, axis, [(i, i + dist) for i in range(count - dist)]))
            after.append(lax.ppermute(head, axis, [(i + dist, i) for i in range(count - dist)]))
        else:
            blank = list(cells.shape)
            blank[dim] = take
            before.insert(0, jnp.zeros(blank, cells.dtype))
            after.append(jnp.zeros(blank, cells.dtype))
        need -= take
        dist += 1
    return jnp.concatenate(before + [cells] + after, axis=dim)


def split_exact(values):
    high = lax.reduce_precision(values, exponent_bits=8, mantissa_bits=7)
    rest = values - high
    middle = lax.reduce_precision(rest, exponent_bits=8, mantissa_bits=7)
    low = rest - middle
    parts = [high, middle, low]
    return jnp.concatenate([p.astype(jnp.bfloat16) for p in parts], axis=-1)


def join_exact(parts):
    width = parts.shape[-1] // 3
    pieces = [parts[..., k * width : (k + 1) * width].astype(jnp.float32) for k in range(3)]
    return (pieces[0] + pieces[1]) + pieces[2]


def surround(cells, width):
    return widen(widen(cells, "rows", 0, width), "cols", 1, width)


def inner(cells, outer, inner_width):
    cut = outer - inner_width
    return cells[cut : cells.shape[0] - cut, cut : cells.shape[1] - cut]


def inside(rows_dev, cols_dev, width):
    rows_all = rows_dev * lax.axis_size("rows")
    cols_all = cols_dev * lax.axis_size("cols")
    row_at = lax.axis_index("rows") * rows_dev - width + jnp.arange(rows_dev + 2 * width)
    col_at = lax.axis_index("cols") * cols_dev - width + jnp.arange(cols_dev + 2 * width)
    row_ok = (row_at >= 0) & (row_at < rows_all)
    col_ok = (col_at >= 0) & (col_at < cols_all)
    return (row_ok[:, None] & col_ok[None, :])[..., None]


def convolve(field, weights):
    numbers = ("NHWC", "HWIO", "NHWC")
    result = lax.conv_general_dilated(
        field[None], weights, (1, 1), "VALID", dimension_numbers=numbers,
        preferred_element_type=jnp.float32,
    )
    return result[0]


def cell_step(stacked, weights, gate_bias, cell_prev):
    gates = convolve(stacked, weights) + gate_bias
    gate_in = jax.nn.sigmoid(gates[..., :HC])
    gate_forget = jax.nn.sigmoid(gates[..., HC : 2 * HC])
    gate_cand = jnp.tanh(gates[..., 2 * HC : 3 * HC])
    gate_out = jax.nn.sigmoid(gates[..., 3 * HC :])
    cell = gate_forget * cell_prev + gate_in * gate_cand
    hidden = (gate_out * jnp.tanh(cell)).astype(jnp.bfloat16)
    return (gate_in, gate_forget, gate_cand, gate_out), cell, hidden


def cell_grads(grad_cell, grad_hidden, gates, cell_prev, cell_now):
    gate_in, gate_forget, gate_cand, gate_out = gates
    tanh_cell = jnp.tanh(cell_now)
    summed = grad_hidden * gate_out * (1.0 - tanh_cell * tanh_cell)
    if grad_cell is not None:
        summed = grad_cell + summed
    pre_in = summed * gate_cand * gate_in * (1.0 - gate_in)
    pre_forget = summed * cell_prev * gate_forget * (1.0 - gate_forget)
    pre_cand = summed * gate_in * (1.0 - gate_cand * gate_cand)
    pre_out = grad_hidden * tanh_cell * gate_out * (1.0 - gate_out)
    grad_gates = jnp.concatenate([pre_in, pre_forget, pre_cand, pre_out], axis=-1).astype(
        jnp.bfloat16
    )
    return grad_gates, summed * gate_forget


def shards(frames, hidden_start, cell_start, kernel, gate_bias, cotangent):
    rows_dev = hidden_start.shape[0]
    cols_dev = hidden_start.shape[1]
    chans = CI + HC
    cells = rows_dev * cols_dev
    reach = 2 * STEPS
    pack = jnp.concatenate(
        [
            frames[0].reshape(rows_dev, cols_dev, CI),
            frames[1].reshape(rows_dev, cols_dev, CI),
            hidden_start,
            cotangent[0],
            cotangent[1],
            split_exact(cell_start),
        ],
        axis=-1,
    )
    pack = surround(pack, reach)
    cell_zero = inner(join_exact(pack[..., 2 * CI + 3 * HC :]), reach, reach - 1)
    pack = pack[..., : 2 * CI + 3 * HC]
    inputs_one = pack[..., :CI]
    inputs_two = pack[..., CI : 2 * CI]
    hidden_zero = pack[..., 2 * CI : 2 * CI + HC]
    cot_zero = pack[..., 2 * CI + HC : 2 * CI + 2 * HC]
    cot_one = pack[..., 2 * CI + 2 * HC :]

    weights = kernel.reshape(KS, KS, chans, GATES)
    flipped = jnp.transpose(weights[::-1, ::-1, CI:, :], (0, 1, 3, 2))
    stacked_one = jnp.concatenate([inputs_one, hidden_zero], axis=-1)
    gates_one, cell_one, hidden_one = cell_step(stacked_one, weights, gate_bias, cell_zero)
    hidden_one = jnp.where(inside(rows_dev, cols_dev, reach - 1), hidden_one, 0)

    stacked_two = jnp.concatenate([inner(inputs_two, reach, reach - 1), hidden_one], axis=-1)
    cell_one_two = inner(cell_one, reach - 1, reach - 2)
    gates_two, cell_two, hidden_two = cell_step(stacked_two, weights, gate_bias, cell_one_two)
    hidden_final = inner(hidden_two, reach - 2, 0)

    grad_gates_two, grad_cell = cell_grads(
        None, inner(cot_one, reach, reach - 2).astype(jnp.float32), gates_two, cell_one_two, cell_two
    )
    masked_two = jnp.where(inside(rows_dev, cols_dev, reach - 2), grad_gates_two, 0)
    grad_hidden = convolve(masked_two, flipped) + inner(cot_zero, reach, reach - 3).astype(jnp.float32)

    def near(values, width):
        return inner(values, width, reach - 3)

    gates_near = tuple(near(g, reach - 1) for g in gates_one)
    grad_gates_one, grad_cell = cell_grads(
        near(grad_cell, reach - 2),
        grad_hidden,
        gates_near,
        near(cell_zero, reach - 1),
        near(cell_one, reach - 1),
    )
    grad_cell_start = inner(grad_cell, reach - 3, 0)
    masked_one = jnp.where(inside(rows_dev, cols_dev, reach - 3), grad_gates_one, 0)
    grad_hidden_start = convolve(masked_one, flipped)

    spare = SUM_ROWS - KIN - 1
    near = [inner(stacked_two, reach - 1, 1), inner(stacked_one, reach, 1)]
    grads_seen = [
        inner(grad_gates_two, reach - 2, 0).reshape(cells, GATES),
        inner(grad_gates_one, reach - 3, 0).reshape(cells, GATES),
    ]
    first, rest = summing_levels()
    axis, bit = first[0]
    pairs = flip_pairs(axis, bit)
    upper = (lax.axis_index(axis) >> bit) & 1
    near = near + [lax.ppermute(s, axis, pairs) for s in near]
    grads_seen = grads_seen + [lax.ppermute(g, axis, pairs) for g in grads_seen]
    lifted = []
    for stacked in near:
        patches = tap_columns(stacked, rows_dev, cols_dev, False)
        lifted.append(
            jnp.concatenate(
                [
                    patches,
                    jnp.ones((cells, 1), patches.dtype),
                    jnp.zeros((cells, spare), patches.dtype),
                ],
                axis=1,
            )
        )
    half = SUM_ROWS // 2
    lifted = lax.dynamic_slice_in_dim(jnp.concatenate(lifted, axis=0), upper * half, half, 1)
    total_cells = STEPS * rows_dev * lax.axis_size("rows") * cols_dev * lax.axis_size("cols")
    norm_scale = 1.0 / math.sqrt(total_cells)
    joined = jnp.dot(
        lifted.T, jnp.concatenate(grads_seen, axis=0), preferred_element_type=jnp.float32
    )
    kernel_grad, bias_grad = sum_everywhere(joined * norm_scale, first, rest)
    return (hidden_final, grad_hidden_start, grad_cell_start, kernel_grad, bias_grad)


def solution(mesh):
    placed = (
        P(None, "rows", "cols"),
        P("rows", "cols", None),
        P("rows", "cols", None),
        P(),
        P(),
        P(None, "rows", "cols", None),
    )
    return jax.shard_map(
        shards,
        mesh=mesh,
        in_specs=placed,
        out_specs=(
            P("rows", "cols", None),
            P("rows", "cols", None),
            P("rows", "cols", None),
            P(),
            P(),
        ),
        check_vma=False,
    )
```

```python
import math

import jax
import jax.numpy as jnp
from jax import lax
from jax.sharding import PartitionSpec as P

HC = 128
CI = 32
KS = 3
STEPS = 2
GATES = 512
KIN = 1440
SUM_ROWS = 1536
SUM_WAYS = 3
SUM_SHARED = 2


def flip_pairs(axis, bit):
    count = lax.axis_size(axis)
    return [(i, i ^ (1 << bit)) for i in range(count)]


def summing_levels():
    levels = []
    for axis in ("cols", "rows"):
        count = lax.axis_size(axis)
        depth = count.bit_length() - 1
        assert (1 << depth) == count
        levels.extend((axis, bit) for bit in range(depth))
    cols_levels = [lv for lv in levels if lv[0] == "cols"]
    rows_levels = [lv for lv in levels if lv[0] == "rows"]
    return cols_levels[:1], cols_levels[1:2] + rows_levels + cols_levels[2:]


def halve(part, levels, limit=None):
    halved = []
    for axis, bit in levels:
        rows = part.shape[0]
        if rows % 16 != 0 or len(halved) == limit:
            break
        half = rows // 2
        upper = (lax.axis_index(axis) >> bit) & 1
        keep = lax.dynamic_slice_in_dim(part, upper * half, half, 0)
        send = lax.dynamic_slice_in_dim(part, (1 - upper) * half, half, 0)
        part = keep + lax.ppermute(send, axis, flip_pairs(axis, bit))
        halved.append((axis, bit))
    for axis, bit in levels[len(halved):]:
        part = part + lax.ppermute(part, axis, flip_pairs(axis, bit))
    return part, halved


def double(piece, halved):
    for axis, bit in reversed(halved):
        upper = (lax.axis_index(axis) >> bit) & 1
        got = lax.ppermute(piece, axis, flip_pairs(axis, bit))
        low = jnp.where(upper == 0, piece, got)
        high = jnp.where(upper == 0, got, piece)
        piece = jnp.concatenate([low, high], axis=0)
    return piece


def sum_everywhere(part, first_halved, rest):
    ways = min(SUM_WAYS, max(len(rest), 1))
    width = part.shape[0] // ways
    pieces = []
    for way in range(ways):
        order = rest[way:] + rest[:way]
        chunk, halved = halve(
            part[way * width : (way + 1) * width], order, max(len(order) - SUM_SHARED, 0)
        )
        pieces.append(double(chunk.astype(jnp.bfloat16), halved))
    if len(first_halved) == 1:
        axis, bit = first_halved[0]
        upper = (lax.axis_index(axis) >> bit) & 1
        pairs = flip_pairs(axis, bit)
        swapped = [(p, lax.ppermute(p, axis, pairs)) for p in pieces]
        half = sum(p.shape[0] for p in pieces)
        kernel_part = jnp.zeros((KIN, GATES), jnp.float32)
        bias_part = None
        for way in reversed(range(len(pieces))):
            mine, got = swapped[way]
            start = sum(p.shape[0] for p in pieces[:way])
            for base, rows in ((0, jnp.where(upper == 0, mine, got)),
                               (half, jnp.where(upper == 0, got, mine))):
                first_row = base + start
                if first_row <= KIN < first_row + rows.shape[0]:
                    bias_part = rows[KIN - first_row].astype(jnp.float32)
                keep = min(rows.shape[0], KIN - first_row)
                if keep > 0:
                    kernel_part = lax.dynamic_update_slice_in_dim(
                        kernel_part, rows[:keep].astype(jnp.float32), first_row, 0
                    )
        return kernel_part, bias_part
    summed = double(jnp.concatenate(pieces, axis=0), first_halved).astype(jnp.float32)
    return summed[:KIN], summed[KIN]


def tap_columns(padded, rows_dev, cols_dev, reverse):
    pieces = []
    for tap_row in range(KS):
        for tap_col in range(KS):
            if reverse:
                first_row = KS - 1 - tap_row
                first_col = KS - 1 - tap_col
            else:
                first_row = tap_row
                first_col = tap_col
            pieces.append(
                padded[first_row : first_row + rows_dev, first_col : first_col + cols_dev]
            )
    joined = jnp.concatenate(pieces, axis=-1)
    return joined.reshape(rows_dev * cols_dev, joined.shape[-1])


def widen(cells, axis, dim, width):
    count = lax.axis_size(axis)
    size = cells.shape[dim]
    before, after = [], []
    need, dist = width, 1
    while need > 0:
        take = min(need, size)
        if dist < count:
            tail = lax.slice_in_dim(cells, size - take, size, axis=dim)
            head = lax.slice_in_dim(cells, 0, take, axis=dim)
            before.insert(0, lax.ppermute(tail, axis, [(i, i + dist) for i in range(count - dist)]))
            after.append(lax.ppermute(head, axis, [(i + dist, i) for i in range(count - dist)]))
        else:
            blank = list(cells.shape)
            blank[dim] = take
            before.insert(0, jnp.zeros(blank, cells.dtype))
            after.append(jnp.zeros(blank, cells.dtype))
        need -= take
        dist += 1
    return jnp.concatenate(before + [cells] + after, axis=dim)


def split_exact(values):
    high = lax.reduce_precision(values, exponent_bits=8, mantissa_bits=7)
    rest = values - high
    middle = lax.reduce_precision(rest, exponent_bits=8, mantissa_bits=7)
    low = rest - middle
    parts = [high, middle, low]
    return jnp.concatenate([p.astype(jnp.bfloat16) for p in parts], axis=-1)


def join_exact(parts):
    width = parts.shape[-1] // 3
    pieces = [parts[..., k * width : (k + 1) * width].astype(jnp.float32) for k in range(3)]
    return (pieces[0] + pieces[1]) + pieces[2]


def surround(cells, width):
    return widen(widen(cells, "rows", 0, width), "cols", 1, width)


def inner(cells, outer, inner_width):
    cut = outer - inner_width
    return cells[cut : cells.shape[0] - cut, cut : cells.shape[1] - cut]


def inside(rows_dev, cols_dev, width):
    rows_all = rows_dev * lax.axis_size("rows")
    cols_all = cols_dev * lax.axis_size("cols")
    row_at = lax.axis_index("rows") * rows_dev - width + jnp.arange(rows_dev + 2 * width)
    col_at = lax.axis_index("cols") * cols_dev - width + jnp.arange(cols_dev + 2 * width)
    row_ok = (row_at >= 0) & (row_at < rows_all)
    col_ok = (col_at >= 0) & (col_at < cols_all)
    return (row_ok[:, None] & col_ok[None, :])[..., None]


def convolve(field, weights):
    numbers = ("NHWC", "HWIO", "NHWC")
    result = lax.conv_general_dilated(
        field[None], weights, (1, 1), "VALID", dimension_numbers=numbers,
        preferred_element_type=jnp.float32,
    )
    return result[0]


def cell_step(stacked, weights, gate_bias, cell_prev):
    gates = convolve(stacked, weights) + gate_bias
    gate_in = jax.nn.sigmoid(gates[..., :HC])
    gate_forget = jax.nn.sigmoid(gates[..., HC : 2 * HC])
    gate_cand = jnp.tanh(gates[..., 2 * HC : 3 * HC])
    gate_out = jax.nn.sigmoid(gates[..., 3 * HC :])
    cell = gate_forget * cell_prev + gate_in * gate_cand
    hidden = (gate_out * jnp.tanh(cell)).astype(jnp.bfloat16)
    return (gate_in, gate_forget, gate_cand, gate_out), cell, hidden


def cell_grads(grad_cell, grad_hidden, gates, cell_prev, cell_now):
    gate_in, gate_forget, gate_cand, gate_out = gates
    tanh_cell = jnp.tanh(cell_now)
    summed = grad_hidden * gate_out * (1.0 - tanh_cell * tanh_cell)
    if grad_cell is not None:
        summed = grad_cell + summed
    pre_in = summed * gate_cand * gate_in * (1.0 - gate_in)
    pre_forget = summed * cell_prev * gate_forget * (1.0 - gate_forget)
    pre_cand = summed * gate_in * (1.0 - gate_cand * gate_cand)
    pre_out = grad_hidden * tanh_cell * gate_out * (1.0 - gate_out)
    grad_gates = jnp.concatenate([pre_in, pre_forget, pre_cand, pre_out], axis=-1).astype(
        jnp.bfloat16
    )
    return grad_gates, summed * gate_forget


def shards(frames, hidden_start, cell_start, kernel, gate_bias, cotangent):
    rows_dev = hidden_start.shape[0]
    cols_dev = hidden_start.shape[1]
    chans = CI + HC
    cells = rows_dev * cols_dev
    reach = 2 * STEPS
    pack = jnp.concatenate(
        [
            frames[0].reshape(rows_dev, cols_dev, CI),
            frames[1].reshape(rows_dev, cols_dev, CI),
            hidden_start,
            cotangent[0],
            cotangent[1],
            split_exact(cell_start),
        ],
        axis=-1,
    )
    pack = surround(pack, reach)
    cell_zero = inner(join_exact(pack[..., 2 * CI + 3 * HC :]), reach, reach - 1)
    pack = pack[..., : 2 * CI + 3 * HC]
    inputs_one = pack[..., :CI]
    inputs_two = pack[..., CI : 2 * CI]
    hidden_zero = pack[..., 2 * CI : 2 * CI + HC]
    cot_zero = pack[..., 2 * CI + HC : 2 * CI + 2 * HC]
    cot_one = pack[..., 2 * CI + 2 * HC :]

    weights = kernel.reshape(KS, KS, chans, GATES)
    flipped = jnp.transpose(weights[::-1, ::-1, CI:, :], (0, 1, 3, 2))
    stacked_one = jnp.concatenate([inputs_one, hidden_zero], axis=-1)
    gates_one, cell_one, hidden_one = cell_step(stacked_one, weights, gate_bias, cell_zero)
    hidden_one = jnp.where(inside(rows_dev, cols_dev, reach - 1), hidden_one, 0)

    stacked_two = jnp.concatenate([inner(inputs_two, reach, reach - 1), hidden_one], axis=-1)
    cell_one_two = inner(cell_one, reach - 1, reach - 2)
    gates_two, cell_two, hidden_two = cell_step(stacked_two, weights, gate_bias, cell_one_two)
    hidden_final = inner(hidden_two, reach - 2, 0)

    grad_gates_two, grad_cell = cell_grads(
        None, inner(cot_one, reach, reach - 2).astype(jnp.float32), gates_two, cell_one_two, cell_two
    )
    masked_two = jnp.where(inside(rows_dev, cols_dev, reach - 2), grad_gates_two, 0)
    grad_hidden = convolve(masked_two, flipped) + inner(cot_zero, reach, reach - 3).astype(jnp.float32)

    def near(values, width):
        return inner(values, width, reach - 3)

    gates_near = tuple(near(g, reach - 1) for g in gates_one)
    grad_gates_one, grad_cell = cell_grads(
        near(grad_cell, reach - 2),
        grad_hidden,
        gates_near,
        near(cell_zero, reach - 1),
        near(cell_one, reach - 1),
    )
    grad_cell_start = inner(grad_cell, reach - 3, 0)
    masked_one = jnp.where(inside(rows_dev, cols_dev, reach - 3), grad_gates_one, 0)
    grad_hidden_start = convolve(masked_one, flipped)

    spare = SUM_ROWS - KIN - 1
    near = [inner(stacked_two, reach - 1, 1), inner(stacked_one, reach, 1)]
    grads_seen = [
        inner(grad_gates_two, reach - 2, 0).reshape(cells, GATES),
        inner(grad_gates_one, reach - 3, 0).reshape(cells, GATES),
    ]
    first, rest = summing_levels()
    axis, bit = first[0]
    pairs = flip_pairs(axis, bit)
    upper = (lax.axis_index(axis) >> bit) & 1
    near = near + [lax.ppermute(s, axis, pairs) for s in near]
    grads_seen = grads_seen + [lax.ppermute(g, axis, pairs) for g in grads_seen]
    lifted = []
    for stacked in near:
        patches = tap_columns(stacked, rows_dev, cols_dev, False)
        lifted.append(
            jnp.concatenate(
                [
                    patches,
                    jnp.ones((cells, 1), patches.dtype),
                    jnp.zeros((cells, spare), patches.dtype),
                ],
                axis=1,
            )
        )
    half = SUM_ROWS // 2
    lifted = lax.dynamic_slice_in_dim(jnp.concatenate(lifted, axis=0), upper * half, half, 1)
    total_cells = STEPS * rows_dev * lax.axis_size("rows") * cols_dev * lax.axis_size("cols")
    norm_scale = 1.0 / math.sqrt(total_cells)
    joined = jnp.dot(
        lifted.T, jnp.concatenate(grads_seen, axis=0), preferred_element_type=jnp.float32
    )
    kernel_grad, bias_grad = sum_everywhere(joined * norm_scale, first, rest)
    return (hidden_final, grad_hidden_start, grad_cell_start, kernel_grad, bias_grad)


def solution(mesh):
    placed = (
        P(None, "rows", "cols"),
        P("rows", "cols", None),
        P("rows", "cols", None),
        P(),
        P(),
        P(None, "rows", "cols", None),
    )
    return jax.shard_map(
        shards,
        mesh=mesh,
        in_specs=placed,
        out_specs=(
            P("rows", "cols", None),
            P("rows", "cols", None),
            P("rows", "cols", None),
            P(),
            P(),
        ),
        check_vma=False,
    )
```

```python
import math

import jax
import jax.numpy as jnp
from jax import lax
from jax.sharding import PartitionSpec as P

HC = 128
CI = 32
KS = 3
STEPS = 2
GATES = 512
KIN = 1440
SUM_ROWS = 1536
SUM_WAYS = 3
SUM_SHARED = 2


def flip_pairs(axis, bit):
    count = lax.axis_size(axis)
    return [(i, i ^ (1 << bit)) for i in range(count)]


def summing_levels():
    levels = []
    for axis in ("cols", "rows"):
        count = lax.axis_size(axis)
        depth = count.bit_length() - 1
        assert (1 << depth) == count
        levels.extend((axis, bit) for bit in range(depth))
    cols_levels = [lv for lv in levels if lv[0] == "cols"]
    rows_levels = [lv for lv in levels if lv[0] == "rows"]
    return cols_levels[:1], cols_levels[1:2] + rows_levels + cols_levels[2:]


def halve(part, levels, limit=None):
    halved = []
    for axis, bit in levels:
        rows = part.shape[0]
        if rows % 16 != 0 or len(halved) == limit:
            break
        half = rows // 2
        upper = (lax.axis_index(axis) >> bit) & 1
        keep = lax.dynamic_slice_in_dim(part, upper * half, half, 0)
        send = lax.dynamic_slice_in_dim(part, (1 - upper) * half, half, 0)
        part = keep + lax.ppermute(send, axis, flip_pairs(axis, bit))
        halved.append((axis, bit))
    for axis, bit in levels[len(halved):]:
        part = part + lax.ppermute(part, axis, flip_pairs(axis, bit))
    return part, halved


def double(piece, halved):
    for axis, bit in reversed(halved):
        upper = (lax.axis_index(axis) >> bit) & 1
        got = lax.ppermute(piece, axis, flip_pairs(axis, bit))
        low = jnp.where(upper == 0, piece, got)
        high = jnp.where(upper == 0, got, piece)
        piece = jnp.concatenate([low, high], axis=0)
    return piece


def sum_everywhere(part, first_halved, rest):
    ways = min(SUM_WAYS, max(len(rest), 1))
    width = part.shape[0] // ways
    pieces = []
    for way in range(ways):
        order = rest[way:] + rest[:way]
        chunk, halved = halve(
            part[way * width : (way + 1) * width], order, max(len(order) - SUM_SHARED, 0)
        )
        pieces.append(double(chunk.astype(jnp.bfloat16), halved))
    if len(first_halved) == 1:
        axis, bit = first_halved[0]
        upper = (lax.axis_index(axis) >> bit) & 1
        pairs = flip_pairs(axis, bit)
        swapped = [(p, lax.ppermute(p, axis, pairs)) for p in pieces]
        half = sum(p.shape[0] for p in pieces)
        kernel_part = jnp.zeros((KIN, GATES), jnp.float32)
        bias_part = None
        for way in range(len(pieces)):
            mine, got = swapped[way]
            start = sum(p.shape[0] for p in pieces[:way])
            for base, rows in ((0, jnp.where(upper == 0, mine, got)),
                               (half, jnp.where(upper == 0, got, mine))):
                first_row = base + start
                if first_row <= KIN < first_row + rows.shape[0]:
                    bias_part = rows[KIN - first_row].astype(jnp.float32)
                keep = min(rows.shape[0], KIN - first_row)
                if keep > 0:
                    kernel_part = lax.dynamic_update_slice_in_dim(
                        kernel_part, rows[:keep].astype(jnp.float32), first_row, 0
                    )
        return kernel_part, bias_part
    summed = double(jnp.concatenate(pieces, axis=0), first_halved).astype(jnp.float32)
    return summed[:KIN], summed[KIN]


def tap_columns(padded, rows_dev, cols_dev, reverse):
    pieces = []
    for tap_row in range(KS):
        for tap_col in range(KS):
            if reverse:
                first_row = KS - 1 - tap_row
                first_col = KS - 1 - tap_col
            else:
                first_row = tap_row
                first_col = tap_col
            pieces.append(
                padded[first_row : first_row + rows_dev, first_col : first_col + cols_dev]
            )
    joined = jnp.concatenate(pieces, axis=-1)
    return joined.reshape(rows_dev * cols_dev, joined.shape[-1])


def widen(cells, axis, dim, width):
    count = lax.axis_size(axis)
    size = cells.shape[dim]
    before, after = [], []
    need, dist = width, 1
    while need > 0:
        take = min(need, size)
        if dist < count:
            tail = lax.slice_in_dim(cells, size - take, size, axis=dim)
            head = lax.slice_in_dim(cells, 0, take, axis=dim)
            before.insert(0, lax.ppermute(tail, axis, [(i, i + dist) for i in range(count - dist)]))
            after.append(lax.ppermute(head, axis, [(i + dist, i) for i in range(count - dist)]))
        else:
            blank = list(cells.shape)
            blank[dim] = take
            before.insert(0, jnp.zeros(blank, cells.dtype))
            after.append(jnp.zeros(blank, cells.dtype))
        need -= take
        dist += 1
    return jnp.concatenate(before + [cells] + after, axis=dim)


def split_exact(values):
    high = lax.reduce_precision(values, exponent_bits=8, mantissa_bits=7)
    rest = values - high
    middle = lax.reduce_precision(rest, exponent_bits=8, mantissa_bits=7)
    low = rest - middle
    parts = [high, middle, low]
    return jnp.concatenate([p.astype(jnp.bfloat16) for p in parts], axis=-1)


def join_exact(parts):
    width = parts.shape[-1] // 3
    pieces = [parts[..., k * width : (k + 1) * width].astype(jnp.float32) for k in range(3)]
    return (pieces[0] + pieces[1]) + pieces[2]


def surround(cells, width):
    return widen(widen(cells, "rows", 0, width), "cols", 1, width)


def inner(cells, outer, inner_width):
    cut = outer - inner_width
    return cells[cut : cells.shape[0] - cut, cut : cells.shape[1] - cut]


def inside(rows_dev, cols_dev, width):
    rows_all = rows_dev * lax.axis_size("rows")
    cols_all = cols_dev * lax.axis_size("cols")
    row_at = lax.axis_index("rows") * rows_dev - width + jnp.arange(rows_dev + 2 * width)
    col_at = lax.axis_index("cols") * cols_dev - width + jnp.arange(cols_dev + 2 * width)
    row_ok = (row_at >= 0) & (row_at < rows_all)
    col_ok = (col_at >= 0) & (col_at < cols_all)
    return (row_ok[:, None] & col_ok[None, :])[..., None]


def convolve(field, weights):
    numbers = ("NHWC", "HWIO", "NHWC")
    result = lax.conv_general_dilated(
        field[None], weights, (1, 1), "VALID", dimension_numbers=numbers,
        preferred_element_type=jnp.float32,
    )
    return result[0]


def cell_step(stacked, weights, gate_bias, cell_prev):
    gates = convolve(stacked, weights) + gate_bias
    gate_in = jax.nn.sigmoid(gates[..., :HC])
    gate_forget = jax.nn.sigmoid(gates[..., HC : 2 * HC])
    gate_cand = jnp.tanh(gates[..., 2 * HC : 3 * HC])
    gate_out = jax.nn.sigmoid(gates[..., 3 * HC :])
    cell = gate_forget * cell_prev + gate_in * gate_cand
    hidden = (gate_out * jnp.tanh(cell)).astype(jnp.bfloat16)
    return (gate_in, gate_forget, gate_cand, gate_out), cell, hidden


def cell_grads(grad_cell, grad_hidden, gates, cell_prev, cell_now):
    gate_in, gate_forget, gate_cand, gate_out = gates
    tanh_cell = jnp.tanh(cell_now)
    summed = grad_hidden * gate_out * (1.0 - tanh_cell * tanh_cell)
    if grad_cell is not None:
        summed = grad_cell + summed
    pre_in = summed * gate_cand * gate_in * (1.0 - gate_in)
    pre_forget = summed * cell_prev * gate_forget * (1.0 - gate_forget)
    pre_cand = summed * gate_in * (1.0 - gate_cand * gate_cand)
    pre_out = grad_hidden * tanh_cell * gate_out * (1.0 - gate_out)
    grad_gates = jnp.concatenate([pre_in, pre_forget, pre_cand, pre_out], axis=-1).astype(
        jnp.bfloat16
    )
    return grad_gates, summed * gate_forget


def shards(frames, hidden_start, cell_start, kernel, gate_bias, cotangent):
    rows_dev = hidden_start.shape[0]
    cols_dev = hidden_start.shape[1]
    chans = CI + HC
    cells = rows_dev * cols_dev
    reach = 2 * STEPS
    pack = jnp.concatenate(
        [
            frames[0].reshape(rows_dev, cols_dev, CI),
            frames[1].reshape(rows_dev, cols_dev, CI),
            hidden_start,
            cotangent[0],
            cotangent[1],
            split_exact(cell_start),
        ],
        axis=-1,
    )
    pack = surround(pack, reach)
    cell_zero = inner(join_exact(pack[..., 2 * CI + 3 * HC :]), reach, reach - 1)
    pack = pack[..., : 2 * CI + 3 * HC]
    inputs_one = pack[..., :CI]
    inputs_two = pack[..., CI : 2 * CI]
    hidden_zero = pack[..., 2 * CI : 2 * CI + HC]
    cot_zero = pack[..., 2 * CI + HC : 2 * CI + 2 * HC]
    cot_one = pack[..., 2 * CI + 2 * HC :]

    weights = kernel.reshape(KS, KS, chans, GATES)
    flipped = jnp.transpose(weights[::-1, ::-1, CI:, :], (0, 1, 3, 2))
    stacked_one = jnp.concatenate([inputs_one, hidden_zero], axis=-1)
    gates_one, cell_one, hidden_one = cell_step(stacked_one, weights, gate_bias, cell_zero)
    hidden_one = jnp.where(inside(rows_dev, cols_dev, reach - 1), hidden_one, 0)

    stacked_two = jnp.concatenate([inner(inputs_two, reach, reach - 1), hidden_one], axis=-1)
    cell_one_two = inner(cell_one, reach - 1, reach - 2)
    gates_two, cell_two, hidden_two = cell_step(stacked_two, weights, gate_bias, cell_one_two)
    hidden_final = inner(hidden_two, reach - 2, 0)

    grad_gates_two, grad_cell = cell_grads(
        None, inner(cot_one, reach, reach - 2).astype(jnp.float32), gates_two, cell_one_two, cell_two
    )
    masked_two = jnp.where(inside(rows_dev, cols_dev, reach - 2), grad_gates_two, 0)
    grad_hidden = convolve(masked_two, flipped) + inner(cot_zero, reach, reach - 3).astype(jnp.float32)

    def near(values, width):
        return inner(values, width, reach - 3)

    gates_near = tuple(near(g, reach - 1) for g in gates_one)
    grad_gates_one, grad_cell = cell_grads(
        near(grad_cell, reach - 2),
        grad_hidden,
        gates_near,
        near(cell_zero, reach - 1),
        near(cell_one, reach - 1),
    )
    grad_cell_start = inner(grad_cell, reach - 3, 0)
    masked_one = jnp.where(inside(rows_dev, cols_dev, reach - 3), grad_gates_one, 0)
    grad_hidden_start = convolve(masked_one, flipped)

    spare = SUM_ROWS - KIN - 1
    near = [inner(stacked_two, reach - 1, 1), inner(stacked_one, reach, 1)]
    grads_seen = [
        inner(grad_gates_two, reach - 2, 0).reshape(cells, GATES),
        inner(grad_gates_one, reach - 3, 0).reshape(cells, GATES),
    ]
    first, rest = summing_levels()
    axis, bit = first[0]
    pairs = flip_pairs(axis, bit)
    upper = (lax.axis_index(axis) >> bit) & 1
    near = near + [lax.ppermute(s, axis, pairs) for s in near]
    grads_seen = grads_seen + [lax.ppermute(g, axis, pairs) for g in grads_seen]
    lifted = []
    for stacked in near:
        patches = tap_columns(stacked, rows_dev, cols_dev, False)
        lifted.append(
            jnp.concatenate(
                [
                    patches,
                    jnp.ones((cells, 1), patches.dtype),
                    jnp.zeros((cells, spare), patches.dtype),
                ],
                axis=1,
            )
        )
    half = SUM_ROWS // 2
    lifted = lax.dynamic_slice_in_dim(jnp.concatenate(lifted, axis=0), upper * half, half, 1)
    total_cells = STEPS * rows_dev * lax.axis_size("rows") * cols_dev * lax.axis_size("cols")
    norm_scale = 1.0 / math.sqrt(total_cells)
    joined = jnp.dot(
        lifted.T, jnp.concatenate(grads_seen, axis=0), preferred_element_type=jnp.float32
    )
    kernel_grad, bias_grad = sum_everywhere(joined * norm_scale, first, rest)
    return (hidden_final, grad_hidden_start, grad_cell_start, kernel_grad, bias_grad)


def solution(mesh):
    placed = (
        P(None, "rows", "cols"),
        P("rows", "cols", None),
        P("rows", "cols", None),
        P(),
        P(),
        P(None, "rows", "cols", None),
    )
    return jax.shard_map(
        shards,
        mesh=mesh,
        in_specs=placed,
        out_specs=(
            P("rows", "cols", None),
            P("rows", "cols", None),
            P("rows", "cols", None),
            P(),
            P(),
        ),
        check_vma=False,
    )
```

```python
import math

import jax
import jax.numpy as jnp
from jax import lax
from jax.sharding import PartitionSpec as P

HC = 128
CI = 32
KS = 3
STEPS = 2
GATES = 512
KIN = 1440
SUM_ROWS = 1536
SUM_WAYS = 3
SUM_SHARED = 2


def flip_pairs(axis, bit):
    count = lax.axis_size(axis)
    return [(i, i ^ (1 << bit)) for i in range(count)]


def summing_levels():
    levels = []
    for axis in ("cols", "rows"):
        count = lax.axis_size(axis)
        depth = count.bit_length() - 1
        assert (1 << depth) == count
        levels.extend((axis, bit) for bit in range(depth))
    cols_levels = [lv for lv in levels if lv[0] == "cols"]
    rows_levels = [lv for lv in levels if lv[0] == "rows"]
    return cols_levels[:1], cols_levels[1:2] + rows_levels + cols_levels[2:]


def halve(part, levels, limit=None):
    halved = []
    for axis, bit in levels:
        rows = part.shape[0]
        if rows % 16 != 0 or len(halved) == limit:
            break
        half = rows // 2
        upper = (lax.axis_index(axis) >> bit) & 1
        keep = lax.dynamic_slice_in_dim(part, upper * half, half, 0)
        send = lax.dynamic_slice_in_dim(part, (1 - upper) * half, half, 0)
        part = keep + lax.ppermute(send, axis, flip_pairs(axis, bit))
        halved.append((axis, bit))
    for axis, bit in levels[len(halved):]:
        part = part + lax.ppermute(part, axis, flip_pairs(axis, bit))
    return part, halved


def double(piece, halved):
    for axis, bit in reversed(halved):
        upper = (lax.axis_index(axis) >> bit) & 1
        got = lax.ppermute(piece, axis, flip_pairs(axis, bit))
        low = jnp.where(upper == 0, piece, got)
        high = jnp.where(upper == 0, got, piece)
        piece = jnp.concatenate([low, high], axis=0)
    return piece


def sum_everywhere(part, first_halved, rest):
    ways = min(SUM_WAYS, max(len(rest), 1))
    width = part.shape[0] // ways
    pieces = []
    for way in range(ways):
        order = rest[way:] + rest[:way]
        chunk, halved = halve(
            part[way * width : (way + 1) * width], order, max(len(order) - SUM_SHARED, 0)
        )
        pieces.append(double(chunk.astype(jnp.bfloat16), halved))
    if len(first_halved) == 1:
        axis, bit = first_halved[0]
        upper = (lax.axis_index(axis) >> bit) & 1
        pairs = flip_pairs(axis, bit)
        swapped = [(p, lax.ppermute(p, axis, pairs)) for p in pieces]
        half = sum(p.shape[0] for p in pieces)
        kernel_part = jnp.zeros((KIN, GATES), jnp.float32)
        bias_part = None
        for way in reversed(range(len(pieces))):
            mine, got = swapped[way]
            start = sum(p.shape[0] for p in pieces[:way])
            for base, rows in ((0, jnp.where(upper == 0, mine, got)),
                               (half, jnp.where(upper == 0, got, mine))):
                first_row = base + start
                if first_row <= KIN < first_row + rows.shape[0]:
                    bias_part = rows[KIN - first_row].astype(jnp.float32)
                keep = min(rows.shape[0], KIN - first_row)
                if keep > 0:
                    kernel_part = lax.dynamic_update_slice_in_dim(
                        kernel_part, rows[:keep].astype(jnp.float32), first_row, 0
                    )
        return kernel_part, bias_part
    summed = double(jnp.concatenate(pieces, axis=0), first_halved).astype(jnp.float32)
    return summed[:KIN], summed[KIN]


def tap_columns(padded, rows_dev, cols_dev, reverse):
    pieces = []
    for tap_row in range(KS):
        for tap_col in range(KS):
            if reverse:
                first_row = KS - 1 - tap_row
                first_col = KS - 1 - tap_col
            else:
                first_row = tap_row
                first_col = tap_col
            pieces.append(
                padded[first_row : first_row + rows_dev, first_col : first_col + cols_dev]
            )
    joined = jnp.concatenate(pieces, axis=-1)
    return joined.reshape(rows_dev * cols_dev, joined.shape[-1])


def widen(cells, axis, dim, width):
    count = lax.axis_size(axis)
    size = cells.shape[dim]
    before, after = [], []
    need, dist = width, 1
    while need > 0:
        take = min(need, size)
        if dist < count:
            tail = lax.slice_in_dim(cells, size - take, size, axis=dim)
            head = lax.slice_in_dim(cells, 0, take, axis=dim)
            before.insert(0, lax.ppermute(tail, axis, [(i, i + dist) for i in range(count - dist)]))
            after.append(lax.ppermute(head, axis, [(i + dist, i) for i in range(count - dist)]))
        else:
            blank = list(cells.shape)
            blank[dim] = take
            before.insert(0, jnp.zeros(blank, cells.dtype))
            after.append(jnp.zeros(blank, cells.dtype))
        need -= take
        dist += 1
    return jnp.concatenate(before + [cells] + after, axis=dim)


def split_exact(values):
    high = lax.reduce_precision(values, exponent_bits=8, mantissa_bits=7)
    rest = values - high
    middle = lax.reduce_precision(rest, exponent_bits=8, mantissa_bits=7)
    low = rest - middle
    parts = [high, middle, low]
    return jnp.concatenate([p.astype(jnp.bfloat16) for p in parts], axis=-1)


def join_exact(parts):
    width = parts.shape[-1] // 3
    pieces = [parts[..., k * width : (k + 1) * width].astype(jnp.float32) for k in range(3)]
    return (pieces[0] + pieces[1]) + pieces[2]


def surround(cells, width):
    return widen(widen(cells, "rows", 0, width), "cols", 1, width)


def inner(cells, outer, inner_width):
    cut = outer - inner_width
    return cells[cut : cells.shape[0] - cut, cut : cells.shape[1] - cut]


def inside(rows_dev, cols_dev, width):
    rows_all = rows_dev * lax.axis_size("rows")
    cols_all = cols_dev * lax.axis_size("cols")
    row_at = lax.axis_index("rows") * rows_dev - width + jnp.arange(rows_dev + 2 * width)
    col_at = lax.axis_index("cols") * cols_dev - width + jnp.arange(cols_dev + 2 * width)
    row_ok = (row_at >= 0) & (row_at < rows_all)
    col_ok = (col_at >= 0) & (col_at < cols_all)
    return (row_ok[:, None] & col_ok[None, :])[..., None]


def convolve(field, weights):
    numbers = ("NHWC", "HWIO", "NHWC")
    result = lax.conv_general_dilated(
        field[None], weights, (1, 1), "VALID", dimension_numbers=numbers,
        preferred_element_type=jnp.float32,
    )
    return result[0]


def cell_step(stacked, weights, gate_bias, cell_prev):
    gates = convolve(stacked, weights) + gate_bias
    gate_in = jax.nn.sigmoid(gates[..., :HC])
    gate_forget = jax.nn.sigmoid(gates[..., HC : 2 * HC])
    gate_cand = jnp.tanh(gates[..., 2 * HC : 3 * HC])
    gate_out = jax.nn.sigmoid(gates[..., 3 * HC :])
    cell = gate_forget * cell_prev + gate_in * gate_cand
    hidden = (gate_out * jnp.tanh(cell)).astype(jnp.bfloat16)
    return (gate_in, gate_forget, gate_cand, gate_out), cell, hidden


def cell_grads(grad_cell, grad_hidden, gates, cell_prev, cell_now):
    gate_in, gate_forget, gate_cand, gate_out = gates
    tanh_cell = jnp.tanh(cell_now)
    summed = grad_hidden * gate_out * (1.0 - tanh_cell * tanh_cell)
    if grad_cell is not None:
        summed = grad_cell + summed
    pre_in = summed * gate_cand * gate_in * (1.0 - gate_in)
    pre_forget = summed * cell_prev * gate_forget * (1.0 - gate_forget)
    pre_cand = summed * gate_in * (1.0 - gate_cand * gate_cand)
    pre_out = grad_hidden * tanh_cell * gate_out * (1.0 - gate_out)
    grad_gates = jnp.concatenate([pre_in, pre_forget, pre_cand, pre_out], axis=-1).astype(
        jnp.bfloat16
    )
    return grad_gates, summed * gate_forget


def shards(frames, hidden_start, cell_start, kernel, gate_bias, cotangent):
    rows_dev = hidden_start.shape[0]
    cols_dev = hidden_start.shape[1]
    chans = CI + HC
    cells = rows_dev * cols_dev
    reach = 2 * STEPS
    pack = jnp.concatenate(
        [
            frames[0].reshape(rows_dev, cols_dev, CI),
            frames[1].reshape(rows_dev, cols_dev, CI),
            hidden_start,
            cotangent[0],
            cotangent[1],
            split_exact(cell_start),
        ],
        axis=-1,
    )
    pack = surround(pack, reach)
    cell_zero = inner(join_exact(pack[..., 2 * CI + 3 * HC :]), reach, reach - 1)
    pack = pack[..., : 2 * CI + 3 * HC]
    inputs_one = pack[..., :CI]
    inputs_two = pack[..., CI : 2 * CI]
    hidden_zero = pack[..., 2 * CI : 2 * CI + HC]
    cot_zero = pack[..., 2 * CI + HC : 2 * CI + 2 * HC]
    cot_one = pack[..., 2 * CI + 2 * HC :]

    weights = kernel.reshape(KS, KS, chans, GATES)
    flipped = jnp.transpose(weights[::-1, ::-1, CI:, :], (0, 1, 3, 2))
    stacked_one = jnp.concatenate([inputs_one, hidden_zero], axis=-1)
    gates_one, cell_one, hidden_one = cell_step(stacked_one, weights, gate_bias, cell_zero)
    hidden_one = jnp.where(inside(rows_dev, cols_dev, reach - 1), hidden_one, 0)

    stacked_two = jnp.concatenate([inner(inputs_two, reach, reach - 1), hidden_one], axis=-1)
    cell_one_two = inner(cell_one, reach - 1, reach - 2)
    gates_two, cell_two, hidden_two = cell_step(stacked_two, weights, gate_bias, cell_one_two)
    hidden_final = inner(hidden_two, reach - 2, 0)

    grad_gates_two, grad_cell = cell_grads(
        None, inner(cot_one, reach, reach - 2).astype(jnp.float32), gates_two, cell_one_two, cell_two
    )
    masked_two = jnp.where(inside(rows_dev, cols_dev, reach - 2), grad_gates_two, 0)
    grad_hidden = convolve(masked_two, flipped) + inner(cot_zero, reach, reach - 3).astype(jnp.float32)

    def near(values, width):
        return inner(values, width, reach - 3)

    gates_near = tuple(near(g, reach - 1) for g in gates_one)
    grad_gates_one, grad_cell = cell_grads(
        near(grad_cell, reach - 2),
        grad_hidden,
        gates_near,
        near(cell_zero, reach - 1),
        near(cell_one, reach - 1),
    )
    grad_cell_start = inner(grad_cell, reach - 3, 0)
    masked_one = jnp.where(inside(rows_dev, cols_dev, reach - 3), grad_gates_one, 0)
    grad_hidden_start = convolve(masked_one, flipped)

    spare = SUM_ROWS - KIN - 1
    near = [inner(stacked_two, reach - 1, 1), inner(stacked_one, reach, 1)]
    grads_seen = [
        inner(grad_gates_two, reach - 2, 0).reshape(cells, GATES),
        inner(grad_gates_one, reach - 3, 0).reshape(cells, GATES),
    ]
    first, rest = summing_levels()
    axis, bit = first[0]
    pairs = flip_pairs(axis, bit)
    upper = (lax.axis_index(axis) >> bit) & 1
    near = near + [lax.ppermute(s, axis, pairs) for s in near]
    grads_seen = grads_seen + [lax.ppermute(g, axis, pairs) for g in grads_seen]
    lifted = []
    for stacked in near:
        patches = tap_columns(stacked, rows_dev, cols_dev, False)
        lifted.append(
            jnp.concatenate(
                [
                    patches,
                    jnp.ones((cells, 1), patches.dtype),
                    jnp.zeros((cells, spare), patches.dtype),
                ],
                axis=1,
            )
        )
    half = SUM_ROWS // 2
    lifted = lax.dynamic_slice_in_dim(jnp.concatenate(lifted, axis=0), upper * half, half, 1)
    total_cells = STEPS * rows_dev * lax.axis_size("rows") * cols_dev * lax.axis_size("cols")
    norm_scale = 1.0 / math.sqrt(total_cells)
    early = (len(grads_seen) - 1) * cells
    grads_all = jnp.concatenate(grads_seen, axis=0)
    joined = jnp.dot(
        lifted[:early].T, grads_all[:early], preferred_element_type=jnp.float32
    ) + jnp.dot(lifted[early:].T, grads_all[early:], preferred_element_type=jnp.float32)
    kernel_grad, bias_grad = sum_everywhere(joined * norm_scale, first, rest)
    return (hidden_final, grad_hidden_start, grad_cell_start, kernel_grad, bias_grad)


def solution(mesh):
    placed = (
        P(None, "rows", "cols"),
        P("rows", "cols", None),
        P("rows", "cols", None),
        P(),
        P(),
        P(None, "rows", "cols", None),
    )
    return jax.shard_map(
        shards,
        mesh=mesh,
        in_specs=placed,
        out_specs=(
            P("rows", "cols", None),
            P("rows", "cols", None),
            P("rows", "cols", None),
            P(),
            P(),
        ),
        check_vma=False,
    )
```

```python
import math

import jax
import jax.numpy as jnp
from jax import lax
from jax.sharding import PartitionSpec as P

HC = 128
CI = 32
KS = 3
STEPS = 2
GATES = 512
KIN = 1440
SUM_ROWS = 1536
SUM_WAYS = 3
SUM_SHARED = 1


def flip_pairs(axis, bit):
    count = lax.axis_size(axis)
    return [(i, i ^ (1 << bit)) for i in range(count)]


def summing_levels():
    levels = []
    for axis in ("cols", "rows"):
        count = lax.axis_size(axis)
        depth = count.bit_length() - 1
        assert (1 << depth) == count
        levels.extend((axis, bit) for bit in range(depth))
    cols_levels = [lv for lv in levels if lv[0] == "cols"]
    rows_levels = [lv for lv in levels if lv[0] == "rows"]
    return cols_levels[:1], cols_levels[1:2] + rows_levels + cols_levels[2:]


def halve(part, levels, limit=None):
    halved = []
    for axis, bit in levels:
        rows = part.shape[0]
        if rows % 16 != 0 or len(halved) == limit:
            break
        half = rows // 2
        upper = (lax.axis_index(axis) >> bit) & 1
        keep = lax.dynamic_slice_in_dim(part, upper * half, half, 0)
        send = lax.dynamic_slice_in_dim(part, (1 - upper) * half, half, 0)
        part = keep + lax.ppermute(send, axis, flip_pairs(axis, bit))
        halved.append((axis, bit))
    for axis, bit in levels[len(halved):]:
        part = part + lax.ppermute(part, axis, flip_pairs(axis, bit))
    return part, halved


def double(piece, halved):
    for axis, bit in reversed(halved):
        upper = (lax.axis_index(axis) >> bit) & 1
        got = lax.ppermute(piece, axis, flip_pairs(axis, bit))
        low = jnp.where(upper == 0, piece, got)
        high = jnp.where(upper == 0, got, piece)
        piece = jnp.concatenate([low, high], axis=0)
    return piece


def sum_everywhere(part, first_halved, rest):
    ways = min(SUM_WAYS, max(len(rest), 1))
    width = part.shape[0] // ways
    pieces = []
    for way in range(ways):
        order = rest[way:] + rest[:way]
        chunk, halved = halve(
            part[way * width : (way + 1) * width], order, max(len(order) - SUM_SHARED, 0)
        )
        pieces.append(double(chunk.astype(jnp.bfloat16), halved))
    if len(first_halved) == 1:
        axis, bit = first_halved[0]
        upper = (lax.axis_index(axis) >> bit) & 1
        pairs = flip_pairs(axis, bit)
        swapped = [(p, lax.ppermute(p, axis, pairs)) for p in pieces]
        half = sum(p.shape[0] for p in pieces)
        kernel_part = jnp.zeros((KIN, GATES), jnp.float32)
        bias_part = None
        for way in reversed(range(len(pieces))):
            mine, got = swapped[way]
            start = sum(p.shape[0] for p in pieces[:way])
            for base, rows in ((0, jnp.where(upper == 0, mine, got)),
                               (half, jnp.where(upper == 0, got, mine))):
                first_row = base + start
                if first_row <= KIN < first_row + rows.shape[0]:
                    bias_part = rows[KIN - first_row].astype(jnp.float32)
                keep = min(rows.shape[0], KIN - first_row)
                if keep > 0:
                    kernel_part = lax.dynamic_update_slice_in_dim(
                        kernel_part, rows[:keep].astype(jnp.float32), first_row, 0
                    )
        return kernel_part, bias_part
    summed = double(jnp.concatenate(pieces, axis=0), first_halved).astype(jnp.float32)
    return summed[:KIN], summed[KIN]


def tap_columns(padded, rows_dev, cols_dev, reverse):
    pieces = []
    for tap_row in range(KS):
        for tap_col in range(KS):
            if reverse:
                first_row = KS - 1 - tap_row
                first_col = KS - 1 - tap_col
            else:
                first_row = tap_row
                first_col = tap_col
            pieces.append(
                padded[first_row : first_row + rows_dev, first_col : first_col + cols_dev]
            )
    joined = jnp.concatenate(pieces, axis=-1)
    return joined.reshape(rows_dev * cols_dev, joined.shape[-1])


def widen(cells, axis, dim, width):
    count = lax.axis_size(axis)
    size = cells.shape[dim]
    before, after = [], []
    need, dist = width, 1
    while need > 0:
        take = min(need, size)
        if dist < count:
            tail = lax.slice_in_dim(cells, size - take, size, axis=dim)
            head = lax.slice_in_dim(cells, 0, take, axis=dim)
            before.insert(0, lax.ppermute(tail, axis, [(i, i + dist) for i in range(count - dist)]))
            after.append(lax.ppermute(head, axis, [(i + dist, i) for i in range(count - dist)]))
        else:
            blank = list(cells.shape)
            blank[dim] = take
            before.insert(0, jnp.zeros(blank, cells.dtype))
            after.append(jnp.zeros(blank, cells.dtype))
        need -= take
        dist += 1
    return jnp.concatenate(before + [cells] + after, axis=dim)


def split_exact(values):
    high = lax.reduce_precision(values, exponent_bits=8, mantissa_bits=7)
    rest = values - high
    middle = lax.reduce_precision(rest, exponent_bits=8, mantissa_bits=7)
    low = rest - middle
    parts = [high, middle, low]
    return jnp.concatenate([p.astype(jnp.bfloat16) for p in parts], axis=-1)


def join_exact(parts):
    width = parts.shape[-1] // 3
    pieces = [parts[..., k * width : (k + 1) * width].astype(jnp.float32) for k in range(3)]
    return (pieces[0] + pieces[1]) + pieces[2]


def surround(cells, width):
    return widen(widen(cells, "rows", 0, width), "cols", 1, width)


def inner(cells, outer, inner_width):
    cut = outer - inner_width
    return cells[cut : cells.shape[0] - cut, cut : cells.shape[1] - cut]


def inside(rows_dev, cols_dev, width):
    rows_all = rows_dev * lax.axis_size("rows")
    cols_all = cols_dev * lax.axis_size("cols")
    row_at = lax.axis_index("rows") * rows_dev - width + jnp.arange(rows_dev + 2 * width)
    col_at = lax.axis_index("cols") * cols_dev - width + jnp.arange(cols_dev + 2 * width)
    row_ok = (row_at >= 0) & (row_at < rows_all)
    col_ok = (col_at >= 0) & (col_at < cols_all)
    return (row_ok[:, None] & col_ok[None, :])[..., None]


def convolve(field, weights):
    numbers = ("NHWC", "HWIO", "NHWC")
    result = lax.conv_general_dilated(
        field[None], weights, (1, 1), "VALID", dimension_numbers=numbers,
        preferred_element_type=jnp.float32,
    )
    return result[0]


def cell_step(stacked, weights, gate_bias, cell_prev):
    gates = convolve(stacked, weights) + gate_bias
    gate_in = jax.nn.sigmoid(gates[..., :HC])
    gate_forget = jax.nn.sigmoid(gates[..., HC : 2 * HC])
    gate_cand = jnp.tanh(gates[..., 2 * HC : 3 * HC])
    gate_out = jax.nn.sigmoid(gates[..., 3 * HC :])
    cell = gate_forget * cell_prev + gate_in * gate_cand
    hidden = (gate_out * jnp.tanh(cell)).astype(jnp.bfloat16)
    return (gate_in, gate_forget, gate_cand, gate_out), cell, hidden


def cell_grads(grad_cell, grad_hidden, gates, cell_prev, cell_now):
    gate_in, gate_forget, gate_cand, gate_out = gates
    tanh_cell = jnp.tanh(cell_now)
    summed = grad_hidden * gate_out * (1.0 - tanh_cell * tanh_cell)
    if grad_cell is not None:
        summed = grad_cell + summed
    pre_in = summed * gate_cand * gate_in * (1.0 - gate_in)
    pre_forget = summed * cell_prev * gate_forget * (1.0 - gate_forget)
    pre_cand = summed * gate_in * (1.0 - gate_cand * gate_cand)
    pre_out = grad_hidden * tanh_cell * gate_out * (1.0 - gate_out)
    grad_gates = jnp.concatenate([pre_in, pre_forget, pre_cand, pre_out], axis=-1).astype(
        jnp.bfloat16
    )
    return grad_gates, summed * gate_forget


def shards(frames, hidden_start, cell_start, kernel, gate_bias, cotangent):
    rows_dev = hidden_start.shape[0]
    cols_dev = hidden_start.shape[1]
    chans = CI + HC
    cells = rows_dev * cols_dev
    reach = 2 * STEPS
    pack = jnp.concatenate(
        [
            frames[0].reshape(rows_dev, cols_dev, CI),
            frames[1].reshape(rows_dev, cols_dev, CI),
            hidden_start,
            cotangent[0],
            cotangent[1],
            split_exact(cell_start),
        ],
        axis=-1,
    )
    pack = surround(pack, reach)
    cell_zero = inner(join_exact(pack[..., 2 * CI + 3 * HC :]), reach, reach - 1)
    pack = pack[..., : 2 * CI + 3 * HC]
    inputs_one = pack[..., :CI]
    inputs_two = pack[..., CI : 2 * CI]
    hidden_zero = pack[..., 2 * CI : 2 * CI + HC]
    cot_zero = pack[..., 2 * CI + HC : 2 * CI + 2 * HC]
    cot_one = pack[..., 2 * CI + 2 * HC :]

    weights = kernel.reshape(KS, KS, chans, GATES)
    flipped = jnp.transpose(weights[::-1, ::-1, CI:, :], (0, 1, 3, 2))
    stacked_one = jnp.concatenate([inputs_one, hidden_zero], axis=-1)
    gates_one, cell_one, hidden_one = cell_step(stacked_one, weights, gate_bias, cell_zero)
    hidden_one = jnp.where(inside(rows_dev, cols_dev, reach - 1), hidden_one, 0)

    stacked_two = jnp.concatenate([inner(inputs_two, reach, reach - 1), hidden_one], axis=-1)
    cell_one_two = inner(cell_one, reach - 1, reach - 2)
    gates_two, cell_two, hidden_two = cell_step(stacked_two, weights, gate_bias, cell_one_two)
    hidden_final = inner(hidden_two, reach - 2, 0)

    grad_gates_two, grad_cell = cell_grads(
        None, inner(cot_one, reach, reach - 2).astype(jnp.float32), gates_two, cell_one_two, cell_two
    )
    masked_two = jnp.where(inside(rows_dev, cols_dev, reach - 2), grad_gates_two, 0)
    grad_hidden = convolve(masked_two, flipped) + inner(cot_zero, reach, reach - 3).astype(jnp.float32)

    def near(values, width):
        return inner(values, width, reach - 3)

    gates_near = tuple(near(g, reach - 1) for g in gates_one)
    grad_gates_one, grad_cell = cell_grads(
        near(grad_cell, reach - 2),
        grad_hidden,
        gates_near,
        near(cell_zero, reach - 1),
        near(cell_one, reach - 1),
    )
    grad_cell_start = inner(grad_cell, reach - 3, 0)
    masked_one = jnp.where(inside(rows_dev, cols_dev, reach - 3), grad_gates_one, 0)
    grad_hidden_start = convolve(masked_one, flipped)

    spare = SUM_ROWS - KIN - 1
    near = [inner(stacked_two, reach - 1, 1), inner(stacked_one, reach, 1)]
    grads_seen = [
        inner(grad_gates_two, reach - 2, 0).reshape(cells, GATES),
        inner(grad_gates_one, reach - 3, 0).reshape(cells, GATES),
    ]
    first, rest = summing_levels()
    axis, bit = first[0]
    pairs = flip_pairs(axis, bit)
    upper = (lax.axis_index(axis) >> bit) & 1
    near = near + [lax.ppermute(s, axis, pairs) for s in near]
    grads_seen = grads_seen + [lax.ppermute(g, axis, pairs) for g in grads_seen]
    lifted = []
    for stacked in near:
        patches = tap_columns(stacked, rows_dev, cols_dev, False)
        lifted.append(
            jnp.concatenate(
                [
                    patches,
                    jnp.ones((cells, 1), patches.dtype),
                    jnp.zeros((cells, spare), patches.dtype),
                ],
                axis=1,
            )
        )
    half = SUM_ROWS // 2
    lifted = lax.dynamic_slice_in_dim(jnp.concatenate(lifted, axis=0), upper * half, half, 1)
    total_cells = STEPS * rows_dev * lax.axis_size("rows") * cols_dev * lax.axis_size("cols")
    norm_scale = 1.0 / math.sqrt(total_cells)
    joined = jnp.dot(
        lifted.T, jnp.concatenate(grads_seen, axis=0), preferred_element_type=jnp.float32
    )
    kernel_grad, bias_grad = sum_everywhere(joined * norm_scale, first, rest)
    return (hidden_final, grad_hidden_start, grad_cell_start, kernel_grad, bias_grad)


def solution(mesh):
    placed = (
        P(None, "rows", "cols"),
        P("rows", "cols", None),
        P("rows", "cols", None),
        P(),
        P(),
        P(None, "rows", "cols", None),
    )
    return jax.shard_map(
        shards,
        mesh=mesh,
        in_specs=placed,
        out_specs=(
            P("rows", "cols", None),
            P("rows", "cols", None),
            P("rows", "cols", None),
            P(),
            P(),
        ),
        check_vma=False,
    )
```

```python
import math

import jax
import jax.numpy as jnp
from jax import lax
from jax.sharding import PartitionSpec as P

HC = 128
CI = 32
KS = 3
STEPS = 2
GATES = 512
KIN = 1440
SUM_ROWS = 1536
SUM_WAYS = 3
SUM_SHARED = 0


def flip_pairs(axis, bit):
    count = lax.axis_size(axis)
    return [(i, i ^ (1 << bit)) for i in range(count)]


def summing_levels():
    levels = []
    for axis in ("cols", "rows"):
        count = lax.axis_size(axis)
        depth = count.bit_length() - 1
        assert (1 << depth) == count
        levels.extend((axis, bit) for bit in range(depth))
    cols_levels = [lv for lv in levels if lv[0] == "cols"]
    rows_levels = [lv for lv in levels if lv[0] == "rows"]
    return cols_levels[:1], cols_levels[1:2] + rows_levels + cols_levels[2:]


def halve(part, levels, limit=None):
    halved = []
    for axis, bit in levels:
        rows = part.shape[0]
        if rows % 16 != 0 or len(halved) == limit:
            break
        half = rows // 2
        upper = (lax.axis_index(axis) >> bit) & 1
        keep = lax.dynamic_slice_in_dim(part, upper * half, half, 0)
        send = lax.dynamic_slice_in_dim(part, (1 - upper) * half, half, 0)
        part = keep + lax.ppermute(send, axis, flip_pairs(axis, bit))
        halved.append((axis, bit))
    for axis, bit in levels[len(halved):]:
        part = part + lax.ppermute(part, axis, flip_pairs(axis, bit))
    return part, halved


def double(piece, halved):
    for axis, bit in reversed(halved):
        upper = (lax.axis_index(axis) >> bit) & 1
        got = lax.ppermute(piece, axis, flip_pairs(axis, bit))
        low = jnp.where(upper == 0, piece, got)
        high = jnp.where(upper == 0, got, piece)
        piece = jnp.concatenate([low, high], axis=0)
    return piece


def sum_everywhere(part, first_halved, rest):
    ways = min(SUM_WAYS, max(len(rest), 1))
    width = part.shape[0] // ways
    pieces = []
    for way in range(ways):
        order = rest[way:] + rest[:way]
        chunk, halved = halve(
            part[way * width : (way + 1) * width], order, max(len(order) - SUM_SHARED, 0)
        )
        pieces.append(double(chunk.astype(jnp.bfloat16), halved))
    if len(first_halved) == 1:
        axis, bit = first_halved[0]
        upper = (lax.axis_index(axis) >> bit) & 1
        pairs = flip_pairs(axis, bit)
        swapped = [(p, lax.ppermute(p, axis, pairs)) for p in pieces]
        half = sum(p.shape[0] for p in pieces)
        kernel_part = jnp.zeros((KIN, GATES), jnp.float32)
        bias_part = None
        for way in reversed(range(len(pieces))):
            mine, got = swapped[way]
            start = sum(p.shape[0] for p in pieces[:way])
            for base, rows in ((0, jnp.where(upper == 0, mine, got)),
                               (half, jnp.where(upper == 0, got, mine))):
                first_row = base + start
                if first_row <= KIN < first_row + rows.shape[0]:
                    bias_part = rows[KIN - first_row].astype(jnp.float32)
                keep = min(rows.shape[0], KIN - first_row)
                if keep > 0:
                    kernel_part = lax.dynamic_update_slice_in_dim(
                        kernel_part, rows[:keep].astype(jnp.float32), first_row, 0
                    )
        return kernel_part, bias_part
    summed = double(jnp.concatenate(pieces, axis=0), first_halved).astype(jnp.float32)
    return summed[:KIN], summed[KIN]


def tap_columns(padded, rows_dev, cols_dev, reverse):
    pieces = []
    for tap_row in range(KS):
        for tap_col in range(KS):
            if reverse:
                first_row = KS - 1 - tap_row
                first_col = KS - 1 - tap_col
            else:
                first_row = tap_row
                first_col = tap_col
            pieces.append(
                padded[first_row : first_row + rows_dev, first_col : first_col + cols_dev]
            )
    joined = jnp.concatenate(pieces, axis=-1)
    return joined.reshape(rows_dev * cols_dev, joined.shape[-1])


def widen(cells, axis, dim, width):
    count = lax.axis_size(axis)
    size = cells.shape[dim]
    before, after = [], []
    need, dist = width, 1
    while need > 0:
        take = min(need, size)
        if dist < count:
            tail = lax.slice_in_dim(cells, size - take, size, axis=dim)
            head = lax.slice_in_dim(cells, 0, take, axis=dim)
            before.insert(0, lax.ppermute(tail, axis, [(i, i + dist) for i in range(count - dist)]))
            after.append(lax.ppermute(head, axis, [(i + dist, i) for i in range(count - dist)]))
        else:
            blank = list(cells.shape)
            blank[dim] = take
            before.insert(0, jnp.zeros(blank, cells.dtype))
            after.append(jnp.zeros(blank, cells.dtype))
        need -= take
        dist += 1
    return jnp.concatenate(before + [cells] + after, axis=dim)


def split_exact(values):
    high = lax.reduce_precision(values, exponent_bits=8, mantissa_bits=7)
    rest = values - high
    middle = lax.reduce_precision(rest, exponent_bits=8, mantissa_bits=7)
    low = rest - middle
    parts = [high, middle, low]
    return jnp.concatenate([p.astype(jnp.bfloat16) for p in parts], axis=-1)


def join_exact(parts):
    width = parts.shape[-1] // 3
    pieces = [parts[..., k * width : (k + 1) * width].astype(jnp.float32) for k in range(3)]
    return (pieces[0] + pieces[1]) + pieces[2]


def surround(cells, width):
    return widen(widen(cells, "rows", 0, width), "cols", 1, width)


def inner(cells, outer, inner_width):
    cut = outer - inner_width
    return cells[cut : cells.shape[0] - cut, cut : cells.shape[1] - cut]


def inside(rows_dev, cols_dev, width):
    rows_all = rows_dev * lax.axis_size("rows")
    cols_all = cols_dev * lax.axis_size("cols")
    row_at = lax.axis_index("rows") * rows_dev - width + jnp.arange(rows_dev + 2 * width)
    col_at = lax.axis_index("cols") * cols_dev - width + jnp.arange(cols_dev + 2 * width)
    row_ok = (row_at >= 0) & (row_at < rows_all)
    col_ok = (col_at >= 0) & (col_at < cols_all)
    return (row_ok[:, None] & col_ok[None, :])[..., None]


def convolve(field, weights):
    numbers = ("NHWC", "HWIO", "NHWC")
    result = lax.conv_general_dilated(
        field[None], weights, (1, 1), "VALID", dimension_numbers=numbers,
        preferred_element_type=jnp.float32,
    )
    return result[0]


def cell_step(stacked, weights, gate_bias, cell_prev):
    gates = convolve(stacked, weights) + gate_bias
    gate_in = jax.nn.sigmoid(gates[..., :HC])
    gate_forget = jax.nn.sigmoid(gates[..., HC : 2 * HC])
    gate_cand = jnp.tanh(gates[..., 2 * HC : 3 * HC])
    gate_out = jax.nn.sigmoid(gates[..., 3 * HC :])
    cell = gate_forget * cell_prev + gate_in * gate_cand
    hidden = (gate_out * jnp.tanh(cell)).astype(jnp.bfloat16)
    return (gate_in, gate_forget, gate_cand, gate_out), cell, hidden


def cell_grads(grad_cell, grad_hidden, gates, cell_prev, cell_now):
    gate_in, gate_forget, gate_cand, gate_out = gates
    tanh_cell = jnp.tanh(cell_now)
    summed = grad_hidden * gate_out * (1.0 - tanh_cell * tanh_cell)
    if grad_cell is not None:
        summed = grad_cell + summed
    pre_in = summed * gate_cand * gate_in * (1.0 - gate_in)
    pre_forget = summed * cell_prev * gate_forget * (1.0 - gate_forget)
    pre_cand = summed * gate_in * (1.0 - gate_cand * gate_cand)
    pre_out = grad_hidden * tanh_cell * gate_out * (1.0 - gate_out)
    grad_gates = jnp.concatenate([pre_in, pre_forget, pre_cand, pre_out], axis=-1).astype(
        jnp.bfloat16
    )
    return grad_gates, summed * gate_forget


def shards(frames, hidden_start, cell_start, kernel, gate_bias, cotangent):
    rows_dev = hidden_start.shape[0]
    cols_dev = hidden_start.shape[1]
    chans = CI + HC
    cells = rows_dev * cols_dev
    reach = 2 * STEPS
    pack = jnp.concatenate(
        [
            frames[0].reshape(rows_dev, cols_dev, CI),
            frames[1].reshape(rows_dev, cols_dev, CI),
            hidden_start,
            cotangent[0],
            cotangent[1],
            split_exact(cell_start),
        ],
        axis=-1,
    )
    pack = surround(pack, reach)
    cell_zero = inner(join_exact(pack[..., 2 * CI + 3 * HC :]), reach, reach - 1)
    pack = pack[..., : 2 * CI + 3 * HC]
    inputs_one = pack[..., :CI]
    inputs_two = pack[..., CI : 2 * CI]
    hidden_zero = pack[..., 2 * CI : 2 * CI + HC]
    cot_zero = pack[..., 2 * CI + HC : 2 * CI + 2 * HC]
    cot_one = pack[..., 2 * CI + 2 * HC :]

    weights = kernel.reshape(KS, KS, chans, GATES)
    flipped = jnp.transpose(weights[::-1, ::-1, CI:, :], (0, 1, 3, 2))
    stacked_one = jnp.concatenate([inputs_one, hidden_zero], axis=-1)
    gates_one, cell_one, hidden_one = cell_step(stacked_one, weights, gate_bias, cell_zero)
    hidden_one = jnp.where(inside(rows_dev, cols_dev, reach - 1), hidden_one, 0)

    stacked_two = jnp.concatenate([inner(inputs_two, reach, reach - 1), hidden_one], axis=-1)
    cell_one_two = inner(cell_one, reach - 1, reach - 2)
    gates_two, cell_two, hidden_two = cell_step(stacked_two, weights, gate_bias, cell_one_two)
    hidden_final = inner(hidden_two, reach - 2, 0)

    grad_gates_two, grad_cell = cell_grads(
        None, inner(cot_one, reach, reach - 2).astype(jnp.float32), gates_two, cell_one_two, cell_two
    )
    masked_two = jnp.where(inside(rows_dev, cols_dev, reach - 2), grad_gates_two, 0)
    grad_hidden = convolve(masked_two, flipped) + inner(cot_zero, reach, reach - 3).astype(jnp.float32)

    def near(values, width):
        return inner(values, width, reach - 3)

    gates_near = tuple(near(g, reach - 1) for g in gates_one)
    grad_gates_one, grad_cell = cell_grads(
        near(grad_cell, reach - 2),
        grad_hidden,
        gates_near,
        near(cell_zero, reach - 1),
        near(cell_one, reach - 1),
    )
    grad_cell_start = inner(grad_cell, reach - 3, 0)
    masked_one = jnp.where(inside(rows_dev, cols_dev, reach - 3), grad_gates_one, 0)
    grad_hidden_start = convolve(masked_one, flipped)

    spare = SUM_ROWS - KIN - 1
    near = [inner(stacked_two, reach - 1, 1), inner(stacked_one, reach, 1)]
    grads_seen = [
        inner(grad_gates_two, reach - 2, 0).reshape(cells, GATES),
        inner(grad_gates_one, reach - 3, 0).reshape(cells, GATES),
    ]
    first, rest = summing_levels()
    axis, bit = first[0]
    pairs = flip_pairs(axis, bit)
    upper = (lax.axis_index(axis) >> bit) & 1
    near = near + [lax.ppermute(s, axis, pairs) for s in near]
    grads_seen = grads_seen + [lax.ppermute(g, axis, pairs) for g in grads_seen]
    lifted = []
    for stacked in near:
        patches = tap_columns(stacked, rows_dev, cols_dev, False)
        lifted.append(
            jnp.concatenate(
                [
                    patches,
                    jnp.ones((cells, 1), patches.dtype),
                    jnp.zeros((cells, spare), patches.dtype),
                ],
                axis=1,
            )
        )
    half = SUM_ROWS // 2
    lifted = lax.dynamic_slice_in_dim(jnp.concatenate(lifted, axis=0), upper * half, half, 1)
    total_cells = STEPS * rows_dev * lax.axis_size("rows") * cols_dev * lax.axis_size("cols")
    norm_scale = 1.0 / math.sqrt(total_cells)
    joined = jnp.dot(
        lifted.T, jnp.concatenate(grads_seen, axis=0), preferred_element_type=jnp.float32
    )
    kernel_grad, bias_grad = sum_everywhere(joined * norm_scale, first, rest)
    return (hidden_final, grad_hidden_start, grad_cell_start, kernel_grad, bias_grad)


def solution(mesh):
    placed = (
        P(None, "rows", "cols"),
        P("rows", "cols", None),
        P("rows", "cols", None),
        P(),
        P(),
        P(None, "rows", "cols", None),
    )
    return jax.shard_map(
        shards,
        mesh=mesh,
        in_specs=placed,
        out_specs=(
            P("rows", "cols", None),
            P("rows", "cols", None),
            P("rows", "cols", None),
            P(),
            P(),
        ),
        check_vma=False,
    )
```

```python
import math

import jax
import jax.numpy as jnp
from jax import lax
from jax.sharding import PartitionSpec as P

HC = 128
CI = 32
KS = 3
STEPS = 2
GATES = 512
KIN = 1440
SUM_ROWS = 1536
SUM_WAYS = 2
SUM_SHARED = 1


def flip_pairs(axis, bit):
    count = lax.axis_size(axis)
    return [(i, i ^ (1 << bit)) for i in range(count)]


def summing_levels():
    levels = []
    for axis in ("cols", "rows"):
        count = lax.axis_size(axis)
        depth = count.bit_length() - 1
        assert (1 << depth) == count
        levels.extend((axis, bit) for bit in range(depth))
    cols_levels = [lv for lv in levels if lv[0] == "cols"]
    rows_levels = [lv for lv in levels if lv[0] == "rows"]
    return cols_levels[:1], cols_levels[1:2] + rows_levels + cols_levels[2:]


def halve(part, levels, limit=None):
    halved = []
    for axis, bit in levels:
        rows = part.shape[0]
        if rows % 16 != 0 or len(halved) == limit:
            break
        half = rows // 2
        upper = (lax.axis_index(axis) >> bit) & 1
        keep = lax.dynamic_slice_in_dim(part, upper * half, half, 0)
        send = lax.dynamic_slice_in_dim(part, (1 - upper) * half, half, 0)
        part = keep + lax.ppermute(send, axis, flip_pairs(axis, bit))
        halved.append((axis, bit))
    for axis, bit in levels[len(halved):]:
        part = part + lax.ppermute(part, axis, flip_pairs(axis, bit))
    return part, halved


def double(piece, halved):
    for axis, bit in reversed(halved):
        upper = (lax.axis_index(axis) >> bit) & 1
        got = lax.ppermute(piece, axis, flip_pairs(axis, bit))
        low = jnp.where(upper == 0, piece, got)
        high = jnp.where(upper == 0, got, piece)
        piece = jnp.concatenate([low, high], axis=0)
    return piece


def sum_everywhere(part, first_halved, rest):
    ways = min(SUM_WAYS, max(len(rest), 1))
    width = part.shape[0] // ways
    pieces = []
    for way in range(ways):
        order = rest[way:] + rest[:way]
        chunk, halved = halve(
            part[way * width : (way + 1) * width], order, max(len(order) - SUM_SHARED, 0)
        )
        pieces.append(double(chunk.astype(jnp.bfloat16), halved))
    if len(first_halved) == 1:
        axis, bit = first_halved[0]
        upper = (lax.axis_index(axis) >> bit) & 1
        pairs = flip_pairs(axis, bit)
        swapped = [(p, lax.ppermute(p, axis, pairs)) for p in pieces]
        half = sum(p.shape[0] for p in pieces)
        kernel_part = jnp.zeros((KIN, GATES), jnp.float32)
        bias_part = None
        for way in reversed(range(len(pieces))):
            mine, got = swapped[way]
            start = sum(p.shape[0] for p in pieces[:way])
            for base, rows in ((0, jnp.where(upper == 0, mine, got)),
                               (half, jnp.where(upper == 0, got, mine))):
                first_row = base + start
                if first_row <= KIN < first_row + rows.shape[0]:
                    bias_part = rows[KIN - first_row].astype(jnp.float32)
                keep = min(rows.shape[0], KIN - first_row)
                if keep > 0:
                    kernel_part = lax.dynamic_update_slice_in_dim(
                        kernel_part, rows[:keep].astype(jnp.float32), first_row, 0
                    )
        return kernel_part, bias_part
    summed = double(jnp.concatenate(pieces, axis=0), first_halved).astype(jnp.float32)
    return summed[:KIN], summed[KIN]


def tap_columns(padded, rows_dev, cols_dev, reverse):
    pieces = []
    for tap_row in range(KS):
        for tap_col in range(KS):
            if reverse:
                first_row = KS - 1 - tap_row
                first_col = KS - 1 - tap_col
            else:
                first_row = tap_row
                first_col = tap_col
            pieces.append(
                padded[first_row : first_row + rows_dev, first_col : first_col + cols_dev]
            )
    joined = jnp.concatenate(pieces, axis=-1)
    return joined.reshape(rows_dev * cols_dev, joined.shape[-1])


def widen(cells, axis, dim, width):
    count = lax.axis_size(axis)
    size = cells.shape[dim]
    before, after = [], []
    need, dist = width, 1
    while need > 0:
        take = min(need, size)
        if dist < count:
            tail = lax.slice_in_dim(cells, size - take, size, axis=dim)
            head = lax.slice_in_dim(cells, 0, take, axis=dim)
            before.insert(0, lax.ppermute(tail, axis, [(i, i + dist) for i in range(count - dist)]))
            after.append(lax.ppermute(head, axis, [(i + dist, i) for i in range(count - dist)]))
        else:
            blank = list(cells.shape)
            blank[dim] = take
            before.insert(0, jnp.zeros(blank, cells.dtype))
            after.append(jnp.zeros(blank, cells.dtype))
        need -= take
        dist += 1
    return jnp.concatenate(before + [cells] + after, axis=dim)


def split_exact(values):
    high = lax.reduce_precision(values, exponent_bits=8, mantissa_bits=7)
    rest = values - high
    middle = lax.reduce_precision(rest, exponent_bits=8, mantissa_bits=7)
    low = rest - middle
    parts = [high, middle, low]
    return jnp.concatenate([p.astype(jnp.bfloat16) for p in parts], axis=-1)


def join_exact(parts):
    width = parts.shape[-1] // 3
    pieces = [parts[..., k * width : (k + 1) * width].astype(jnp.float32) for k in range(3)]
    return (pieces[0] + pieces[1]) + pieces[2]


def surround(cells, width):
    return widen(widen(cells, "rows", 0, width), "cols", 1, width)


def inner(cells, outer, inner_width):
    cut = outer - inner_width
    return cells[cut : cells.shape[0] - cut, cut : cells.shape[1] - cut]


def inside(rows_dev, cols_dev, width):
    rows_all = rows_dev * lax.axis_size("rows")
    cols_all = cols_dev * lax.axis_size("cols")
    row_at = lax.axis_index("rows") * rows_dev - width + jnp.arange(rows_dev + 2 * width)
    col_at = lax.axis_index("cols") * cols_dev - width + jnp.arange(cols_dev + 2 * width)
    row_ok = (row_at >= 0) & (row_at < rows_all)
    col_ok = (col_at >= 0) & (col_at < cols_all)
    return (row_ok[:, None] & col_ok[None, :])[..., None]


def convolve(field, weights):
    numbers = ("NHWC", "HWIO", "NHWC")
    result = lax.conv_general_dilated(
        field[None], weights, (1, 1), "VALID", dimension_numbers=numbers,
        preferred_element_type=jnp.float32,
    )
    return result[0]


def cell_step(stacked, weights, gate_bias, cell_prev):
    gates = convolve(stacked, weights) + gate_bias
    gate_in = jax.nn.sigmoid(gates[..., :HC])
    gate_forget = jax.nn.sigmoid(gates[..., HC : 2 * HC])
    gate_cand = jnp.tanh(gates[..., 2 * HC : 3 * HC])
    gate_out = jax.nn.sigmoid(gates[..., 3 * HC :])
    cell = gate_forget * cell_prev + gate_in * gate_cand
    hidden = (gate_out * jnp.tanh(cell)).astype(jnp.bfloat16)
    return (gate_in, gate_forget, gate_cand, gate_out), cell, hidden


def cell_grads(grad_cell, grad_hidden, gates, cell_prev, cell_now):
    gate_in, gate_forget, gate_cand, gate_out = gates
    tanh_cell = jnp.tanh(cell_now)
    summed = grad_hidden * gate_out * (1.0 - tanh_cell * tanh_cell)
    if grad_cell is not None:
        summed = grad_cell + summed
    pre_in = summed * gate_cand * gate_in * (1.0 - gate_in)
    pre_forget = summed * cell_prev * gate_forget * (1.0 - gate_forget)
    pre_cand = summed * gate_in * (1.0 - gate_cand * gate_cand)
    pre_out = grad_hidden * tanh_cell * gate_out * (1.0 - gate_out)
    grad_gates = jnp.concatenate([pre_in, pre_forget, pre_cand, pre_out], axis=-1).astype(
        jnp.bfloat16
    )
    return grad_gates, summed * gate_forget


def shards(frames, hidden_start, cell_start, kernel, gate_bias, cotangent):
    rows_dev = hidden_start.shape[0]
    cols_dev = hidden_start.shape[1]
    chans = CI + HC
    cells = rows_dev * cols_dev
    reach = 2 * STEPS
    pack = jnp.concatenate(
        [
            frames[0].reshape(rows_dev, cols_dev, CI),
            frames[1].reshape(rows_dev, cols_dev, CI),
            hidden_start,
            cotangent[0],
            cotangent[1],
            split_exact(cell_start),
        ],
        axis=-1,
    )
    pack = surround(pack, reach)
    cell_zero = inner(join_exact(pack[..., 2 * CI + 3 * HC :]), reach, reach - 1)
    pack = pack[..., : 2 * CI + 3 * HC]
    inputs_one = pack[..., :CI]
    inputs_two = pack[..., CI : 2 * CI]
    hidden_zero = pack[..., 2 * CI : 2 * CI + HC]
    cot_zero = pack[..., 2 * CI + HC : 2 * CI + 2 * HC]
    cot_one = pack[..., 2 * CI + 2 * HC :]

    weights = kernel.reshape(KS, KS, chans, GATES)
    flipped = jnp.transpose(weights[::-1, ::-1, CI:, :], (0, 1, 3, 2))
    stacked_one = jnp.concatenate([inputs_one, hidden_zero], axis=-1)
    gates_one, cell_one, hidden_one = cell_step(stacked_one, weights, gate_bias, cell_zero)
    hidden_one = jnp.where(inside(rows_dev, cols_dev, reach - 1), hidden_one, 0)

    stacked_two = jnp.concatenate([inner(inputs_two, reach, reach - 1), hidden_one], axis=-1)
    cell_one_two = inner(cell_one, reach - 1, reach - 2)
    gates_two, cell_two, hidden_two = cell_step(stacked_two, weights, gate_bias, cell_one_two)
    hidden_final = inner(hidden_two, reach - 2, 0)

    grad_gates_two, grad_cell = cell_grads(
        None, inner(cot_one, reach, reach - 2).astype(jnp.float32), gates_two, cell_one_two, cell_two
    )
    masked_two = jnp.where(inside(rows_dev, cols_dev, reach - 2), grad_gates_two, 0)
    grad_hidden = convolve(masked_two, flipped) + inner(cot_zero, reach, reach - 3).astype(jnp.float32)

    def near(values, width):
        return inner(values, width, reach - 3)

    gates_near = tuple(near(g, reach - 1) for g in gates_one)
    grad_gates_one, grad_cell = cell_grads(
        near(grad_cell, reach - 2),
        grad_hidden,
        gates_near,
        near(cell_zero, reach - 1),
        near(cell_one, reach - 1),
    )
    grad_cell_start = inner(grad_cell, reach - 3, 0)
    masked_one = jnp.where(inside(rows_dev, cols_dev, reach - 3), grad_gates_one, 0)
    grad_hidden_start = convolve(masked_one, flipped)

    spare = SUM_ROWS - KIN - 1
    near = [inner(stacked_two, reach - 1, 1), inner(stacked_one, reach, 1)]
    grads_seen = [
        inner(grad_gates_two, reach - 2, 0).reshape(cells, GATES),
        inner(grad_gates_one, reach - 3, 0).reshape(cells, GATES),
    ]
    first, rest = summing_levels()
    axis, bit = first[0]
    pairs = flip_pairs(axis, bit)
    upper = (lax.axis_index(axis) >> bit) & 1
    near = near + [lax.ppermute(s, axis, pairs) for s in near]
    grads_seen = grads_seen + [lax.ppermute(g, axis, pairs) for g in grads_seen]
    lifted = []
    for stacked in near:
        patches = tap_columns(stacked, rows_dev, cols_dev, False)
        lifted.append(
            jnp.concatenate(
                [
                    patches,
                    jnp.ones((cells, 1), patches.dtype),
                    jnp.zeros((cells, spare), patches.dtype),
                ],
                axis=1,
            )
        )
    half = SUM_ROWS // 2
    lifted = lax.dynamic_slice_in_dim(jnp.concatenate(lifted, axis=0), upper * half, half, 1)
    total_cells = STEPS * rows_dev * lax.axis_size("rows") * cols_dev * lax.axis_size("cols")
    norm_scale = 1.0 / math.sqrt(total_cells)
    joined = jnp.dot(
        lifted.T, jnp.concatenate(grads_seen, axis=0), preferred_element_type=jnp.float32
    )
    kernel_grad, bias_grad = sum_everywhere(joined * norm_scale, first, rest)
    return (hidden_final, grad_hidden_start, grad_cell_start, kernel_grad, bias_grad)


def solution(mesh):
    placed = (
        P(None, "rows", "cols"),
        P("rows", "cols", None),
        P("rows", "cols", None),
        P(),
        P(),
        P(None, "rows", "cols", None),
    )
    return jax.shard_map(
        shards,
        mesh=mesh,
        in_specs=placed,
        out_specs=(
            P("rows", "cols", None),
            P("rows", "cols", None),
            P("rows", "cols", None),
            P(),
            P(),
        ),
        check_vma=False,
    )
```
